128 devices in a mesh: trace: 8 (over x, core), seq: 16 (over y, z).
Axes of the slice: x: 4, y: 4, z: 4, core: 2. Of those that a mesh axis runs over, the one named last changes fastest.
Arguments:
- tokens: bfloat16 [131072, 1024], P(('trace', 'seq')), parts along dimension 0, may hold values from -6 to 6
- norm_gain: float32 [1024], replicated, may hold values from 0.1 to 1.9
- w_qkv: bfloat16 [1024, 3072], replicated, may hold values from -0.02734375 to 0.02734375
- conv_weight: float32 [4, 3072], replicated, may hold values from -3 to 3
- head_gain: float32 [1024], replicated, may hold values from 0.1 to 1.9
- w_out: bfloat16 [1024, 1024], replicated, may hold values from -0.1875 to 0.1875
Outputs:
- layer_out: bfloat16 [131072, 1024], P(('trace', 'seq')), parts along dimension 0
The draws below stay inside these ranges and needn't reach their ends.
There are 8 independent parts, one for each index of `trace`. The reference program is written for one: setup_inputs(seed, part) draws one part's arguments, and reference() takes and returns one part's arrays. A program takes and returns all parts, laid end to end along the dimension named above; an argument that names none is the same for every part. Nothing has to cross between parts.
All inputs are finite; a program needn't handle non-finite values.
Results may differ from the reference program's by a relative error of at most 0.012.
Values may be sent and summed in bfloat16 or wider, within the bound.
No kernel may reach another device: no remote copies, remote signals or barrier semaphores. Data moves between devices by JAX's collectives and lax.ppermute only.
A program may use at most 128 MiB of HBM per device.

```python
import jax
import jax.numpy as jnp
from jax import lax

H = 8
DH = 128
D = 1024
KW = 4
TOK_DEV = 1024
TOKENS = 16384


def level_of(own_key, dims, pieces, least, high):
    gain, own = 1.0, jax.random.fold_in(own_key, 6)
    for position, shards_of in pieces:
        draws = jnp.exp(jax.random.uniform(jax.random.fold_in(own, position), (shards_of,), jnp.float32, least / len(pieces), high / len(pieces)))
        gain = gain * jnp.repeat(draws, dims[position] // shards_of).reshape([-1 if axis == position else 1 for axis in range(len(dims))])
    return gain


def normal_values(rng, shape, deviation, limit, shards=(), held_as=jnp.bfloat16):
    result = jax.random.normal(rng, shape, jnp.float32) * deviation
    if len(shards) > 0:
        result = level_of(rng, shape, shards, -0.22, 0.18) * result
    return jnp.clip(result, min=-limit, max=limit).astype(held_as)


def setup_inputs(seed: int = 0, part: int = 0) -> dict:
    keys = jax.random.split(jax.random.key(seed), 7)
    part_splits = jax.random.split(jax.random.fold_in(keys[6], part), 7)
    tokens = normal_values(part_splits[0], (TOKENS, D), 1.0, 6.0, ((0, 16),))
    norm_gain = jnp.clip(1.0 + 0.18 * jax.random.normal(keys[1], (D,), jnp.float32), 0.1, 1.9)
    w_qkv = normal_values(keys[2], (D, 3 * D), (44 * D) ** -0.5, 0.02734375)
    conv_weight = normal_values(keys[3], (KW, 3 * D), 0.6, 3.0, (), jnp.float32)
    head_gain = jnp.clip(1.0 + 0.18 * jax.random.normal(keys[4], (D,), jnp.float32), 0.1, 1.9)
    w_out = normal_values(keys[5], (D, D), D ** -0.5, 0.1875)
    return dict(tokens=tokens, norm_gain=norm_gain, w_qkv=w_qkv, conv_weight=conv_weight, head_gain=head_gain, w_out=w_out)


def conv_silu(projected, conv_weight):
    length = projected.shape[0]
    padded = jnp.concatenate([jnp.zeros((KW - 1, projected.shape[1]), jnp.bfloat16), projected], 0)
    summed = jnp.zeros(projected.shape, jnp.float32)
    for offset in range(KW):
        begin = KW - 1 - offset
        summed = summed + conv_weight[offset].astype(jnp.float32) * padded[begin:begin + length].astype(jnp.float32)
    return jax.nn.silu(summed).astype(jnp.bfloat16)

def reference(tokens, norm_gain, w_qkv, conv_weight, head_gain, w_out):
    highest = lax.Precision.HIGHEST
    tokens_f = tokens.astype(jnp.float32)
    normed = (tokens_f * lax.rsqrt(lax.optimization_barrier(jnp.mean(tokens_f * tokens_f, -1, keepdims=True)) + 1e-06) * norm_gain.astype(jnp.float32)).astype(jnp.bfloat16)
    projected = jnp.dot(normed, w_qkv, preferred_element_type=jnp.float32).astype(jnp.bfloat16)
    mixed = conv_silu(projected, conv_weight)
    length = mixed.shape[0]
    block_rows = min(512, TOK_DEV)
    count = length // block_rows
    query_rows = mixed[:, :D].reshape(count, block_rows, H, DH)
    key_rows = mixed[:, D:2 * D].reshape(count, block_rows, H, DH)
    value_rows = mixed[:, 2 * D:].reshape(count, block_rows, H, DH)
    causal = jnp.tril(jnp.ones((block_rows, block_rows), jnp.bool_))

    def advance(carried, blocks):
        query_f = blocks[0].astype(jnp.float32)
        key_f = blocks[1].astype(jnp.float32)
        value_f = blocks[2].astype(jnp.float32)
        carried_part = jnp.einsum('thd,hde->the', query_f, carried, precision=highest)
        scores = jnp.einsum('thd,shd->hts', query_f, key_f, precision=highest)
        scores = jnp.where(causal[None], scores, 0.0).astype(jnp.bfloat16)
        local_part = jnp.einsum('hts,she->the', scores.astype(jnp.float32), value_f, precision=highest)
        carried = carried + jnp.einsum('thd,the->hde', key_f, value_f, precision=highest)
        return (carried, carried_part + local_part)
    _, attended = lax.scan(advance, jnp.zeros((H, DH, DH), jnp.float32), (query_rows, key_rows, value_rows))
    attended = attended.reshape(length, H, DH)
    scaled = attended * lax.rsqrt(lax.optimization_barrier(jnp.mean(attended * attended, -1, keepdims=True)) + 1e-05)
    headed = (scaled.reshape(length, D) * head_gain.astype(jnp.float32)).astype(jnp.bfloat16)
    return jnp.dot(headed, w_out, preferred_element_type=jnp.float32).astype(jnp.bfloat16)
```

```python
import jax
import jax.numpy as jnp
from jax import lax
from jax.sharding import Mesh
from jax.sharding import PartitionSpec as P

H = 8
DH = 128
KW = 4
BLOCK = 512


def split_bf16(x):
    hi = x.astype(jnp.bfloat16)
    lo = (x - hi.astype(jnp.float32)).astype(jnp.bfloat16)
    return hi, lo


def earlier_sum(gathered, axis):
    place = lax.axis_index(axis)
    count = gathered.shape[0]
    mask = (lax.iota(jnp.int32, count) < place).astype(jnp.float32)
    values = gathered.astype(jnp.float32)
    before = jnp.sum(values * mask[:, None, None, None], 0)
    return before, jnp.sum(values, 0)


def local(tokens, norm_gain, w_qkv, conv_weight, head_gain, w_out):
    rows, width = tokens.shape
    tokens_f = tokens.astype(jnp.float32)
    scale = lax.rsqrt(jnp.mean(tokens_f * tokens_f, -1, keepdims=True) + 1e-06)
    normed = (tokens_f * scale * norm_gain).astype(jnp.bfloat16)

    slabs = w_qkv.shape[1] // DH
    projected = jnp.einsum(
        "td,dje->jte", normed, w_qkv.reshape(width, slabs, DH), preferred_element_type=jnp.float32
    ).astype(jnp.bfloat16)

    seq_axes = ("sy", "sz")
    count = lax.axis_size("sy") * lax.axis_size("sz")
    earlier_rows = lax.ppermute(
        projected[:, rows - (KW - 1) :, :], seq_axes, [(i, i + 1) for i in range(count - 1)]
    )
    padded = jnp.concatenate([earlier_rows, projected], 1)
    taps = conv_weight.reshape(KW, slabs, 1, DH)
    summed = jnp.zeros(projected.shape, jnp.float32)
    for offset in range(KW):
        begin = KW - 1 - offset
        summed = summed + taps[offset] * padded[:, begin : begin + rows].astype(jnp.float32)
    mixed = jax.nn.silu(summed).astype(jnp.bfloat16)

    block = min(BLOCK, rows)
    nb = rows // block
    query = mixed[:H].reshape(H, nb, block, DH)
    key = mixed[H : 2 * H].reshape(H, nb, block, DH)
    value = mixed[2 * H :].reshape(H, nb, block, DH)

    block_states = jnp.einsum("hbsd,hbse->bhde", key, value, preferred_element_type=jnp.float32)
    inner = jnp.concatenate(
        [jnp.zeros_like(block_states[:1]), jnp.cumsum(block_states, 0)[:-1]], 0
    )
    state = jnp.sum(block_states, 0)

    zbefore, row_total = earlier_sum(lax.all_gather(state.astype(jnp.bfloat16), "sz"), "sz")
    ybefore, _ = earlier_sum(lax.all_gather(row_total.astype(jnp.bfloat16), "sy"), "sy")
    prefix = ybefore + zbefore

    causal = jnp.tril(jnp.ones((block, block), jnp.bool_))
    scores = jnp.einsum("hbtd,hbsd->hbts", query, key, preferred_element_type=jnp.float32)
    scores = jnp.where(causal, scores, 0.0).astype(jnp.bfloat16)
    local_part = jnp.einsum("hbts,hbse->hbte", scores, value, preferred_element_type=jnp.float32)

    carried = prefix[None] + inner
    carried_hi, carried_lo = split_bf16(carried)
    carried_part = jnp.einsum(
        "hbtd,bhde->hbte", query, carried_hi, preferred_element_type=jnp.float32
    ) + jnp.einsum("hbtd,bhde->hbte", query, carried_lo, preferred_element_type=jnp.float32)
    attended = (local_part + carried_part).reshape(H, rows, DH)

    scaled = attended * lax.rsqrt(jnp.mean(attended * attended, -1, keepdims=True) + 1e-05)
    headed = (scaled * head_gain.reshape(H, 1, DH)).astype(jnp.bfloat16)
    out = jnp.einsum(
        "hte,hen->tn", headed, w_out.reshape(H, DH, width), preferred_element_type=jnp.float32
    )
    return out.astype(jnp.bfloat16)


def solution(mesh):
    seq = mesh.shape["seq"]
    inner = 4 if seq % 4 == 0 else 1
    grid = Mesh(
        mesh.devices.reshape(mesh.shape["trace"], seq // inner, inner), ("trace", "sy", "sz")
    )
    rows = P(("trace", "sy", "sz"), None)
    placed = (rows, P(), P(), P(), P(), P())
    return jax.shard_map(local, mesh=grid, in_specs=placed, out_specs=rows, check_vma=False)
```

```python
import jax
import jax.numpy as jnp
from jax import lax
from jax.sharding import Mesh
from jax.sharding import PartitionSpec as P

H = 8
DH = 128
KW = 4
BLOCK = 512


def split_bf16(x):
    hi = lax.reduce_precision(x, exponent_bits=8, mantissa_bits=7)
    return hi.astype(jnp.bfloat16), (x - hi).astype(jnp.bfloat16)


def ring_earlier(x, axis):
    count = lax.axis_size(axis)
    place = lax.axis_index(axis)
    forward = [(i, (i + 1) % count) for i in range(count)]
    backward = [(i, (i - 1) % count) for i in range(count)]
    from_prev = lax.ppermute(x, axis, forward)
    from_next = lax.ppermute(x, axis, backward)
    half = x.shape[0] // 2
    from_far = jnp.concatenate(
        [lax.ppermute(from_prev[:half], axis, forward), lax.ppermute(from_next[half:], axis, backward)],
        0,
    )
    before = jnp.zeros(x.shape, jnp.float32)
    total = x.astype(jnp.float32)
    for offset, part in ((-1, from_prev), (1, from_next), (2, from_far)):
        part = part.astype(jnp.float32)
        earlier = ((place + offset) % count < place).astype(jnp.float32)
        before = before + earlier * part
        total = total + part
    return before, total


def local(tokens, norm_gain, w_qkv, conv_weight, head_gain, w_out):
    rows, width = tokens.shape
    tokens_f = tokens.astype(jnp.float32)
    scale = lax.rsqrt(jnp.mean(tokens_f * tokens_f, -1, keepdims=True) + 1e-06)
    normed = (tokens_f * scale * norm_gain).astype(jnp.bfloat16)

    slabs = w_qkv.shape[1] // DH
    projected = jnp.einsum(
        "td,dje->jte", normed, w_qkv.reshape(width, slabs, DH), preferred_element_type=jnp.float32
    ).astype(jnp.bfloat16)

    seq_axes = ("sy", "sz")
    count = lax.axis_size("sy") * lax.axis_size("sz")
    earlier_rows = lax.ppermute(
        projected[:, rows - (KW - 1) :, :], seq_axes, [(i, i + 1) for i in range(count - 1)]
    )
    padded = jnp.concatenate([earlier_rows, projected], 1)
    taps = conv_weight.reshape(KW, slabs, 1, DH)
    summed = jnp.zeros(projected.shape, jnp.float32)
    for offset in range(KW):
        begin = KW - 1 - offset
        summed = summed + taps[offset] * padded[:, begin : begin + rows].astype(jnp.float32)
    mixed = jax.nn.silu(summed).astype(jnp.bfloat16)

    block = min(BLOCK, rows)
    nb = rows // block
    query = mixed[:H].reshape(H, nb, block, DH)
    key = mixed[H : 2 * H].reshape(H, nb, block, DH)
    value = mixed[2 * H :].reshape(H, nb, block, DH)

    block_states = jnp.einsum("hbsd,hbse->bhde", key, value, preferred_element_type=jnp.float32)
    inner = jnp.concatenate(
        [jnp.zeros_like(block_states[:1]), jnp.cumsum(block_states, 0)[:-1]], 0
    )
    state = jnp.sum(block_states, 0)

    zbefore, row_total = ring_earlier(state.astype(jnp.bfloat16), "sz")
    ybefore, _ = ring_earlier(row_total.astype(jnp.bfloat16), "sy")
    prefix = ybefore + zbefore

    causal = jnp.tril(jnp.ones((block, block), jnp.bool_))
    scores = jnp.einsum("hbtd,hbsd->hbts", query, key, preferred_element_type=jnp.float32)
    scores = jnp.where(causal, scores, 0.0).astype(jnp.bfloat16)
    local_part = jnp.einsum("hbts,hbse->hbte", scores, value, preferred_element_type=jnp.float32)

    carried = prefix[None] + inner
    carried_hi, carried_lo = split_bf16(carried)
    carried_part = jnp.einsum(
        "hbtd,bhde->hbte", query, carried_hi, preferred_element_type=jnp.float32
    ) + jnp.einsum("hbtd,bhde->hbte", query, carried_lo, preferred_element_type=jnp.float32)
    attended = (local_part + carried_part).reshape(H, rows, DH)

    scaled = attended * lax.rsqrt(jnp.mean(attended * attended, -1, keepdims=True) + 1e-05)
    headed = (scaled * head_gain.reshape(H, 1, DH)).astype(jnp.bfloat16)
    out = jnp.einsum(
        "hte,hen->tn", headed, w_out.reshape(H, DH, width), preferred_element_type=jnp.float32
    )
    return out.astype(jnp.bfloat16)


def solution(mesh):
    seq = mesh.shape["seq"]
    inner = 4 if seq % 4 == 0 else 1
    grid = Mesh(
        mesh.devices.reshape(mesh.shape["trace"], seq // inner, inner), ("trace", "sy", "sz")
    )
    rows = P(("trace", "sy", "sz"), None)
    placed = (rows, P(), P(), P(), P(), P())
    return jax.shard_map(local, mesh=grid, in_specs=placed, out_specs=rows, check_vma=False)
```

```python
import jax
import jax.numpy as jnp
from jax import lax
from jax.experimental import pallas as pl
from jax.experimental.pallas import tpu as pltpu
from jax.sharding import Mesh
from jax.sharding import PartitionSpec as P

H = 8
DH = 128
KW = 4
BLOCK = 512
PAD = 8


def split_bf16(x):
    hi = lax.reduce_precision(x, exponent_bits=8, mantissa_bits=7)
    return hi.astype(jnp.bfloat16), (x - hi).astype(jnp.bfloat16)


def ring_earlier(x, axis):
    count = lax.axis_size(axis)
    place = lax.axis_index(axis)
    forward = [(i, (i + 1) % count) for i in range(count)]
    backward = [(i, (i - 1) % count) for i in range(count)]
    from_prev = lax.ppermute(x, axis, forward)
    from_next = lax.ppermute(x, axis, backward)
    half = x.shape[0] // 2
    from_far = jnp.concatenate(
        [lax.ppermute(from_prev[:half], axis, forward), lax.ppermute(from_next[half:], axis, backward)],
        0,
    )
    before = jnp.zeros(x.shape, jnp.float32)
    total = x.astype(jnp.float32)
    for offset, part in ((-1, from_prev), (1, from_next), (2, from_far)):
        part = part.astype(jnp.float32)
        earlier = ((place + offset) % count < place).astype(jnp.float32)
        before = before + earlier * part
        total = total + part
    return before, total


def conv_kernel(pq, pk, pv, eq, ek, ev, tq, tk, tv, oq, ok, ov, state_ref, buf):
    rows = pq.shape[0]
    for proj, early, taps, out in ((pq, eq, tq, oq), (pk, ek, tk, ok), (pv, ev, tv, ov)):
        buf[0:PAD, :] = early[...].astype(jnp.float32)
        buf[PAD:, :] = proj[...].astype(jnp.float32)
        summed = jnp.zeros((rows, DH), jnp.float32)
        for offset in range(KW):
            summed = summed + taps[offset : offset + 1, :] * buf[pl.ds(PAD - offset, rows), :]
        out[...] = (summed * jax.nn.sigmoid(summed)).astype(out.dtype)
    state_ref[...] = lax.dot_general(
        ok[...], ov[...], (((0,), (0,)), ((), ())), preferred_element_type=jnp.float32
    )


def local_kernel(q_ref, k_ref, v_ref, out_ref):
    rows = q_ref.shape[0]
    block = min(BLOCK, rows)
    causal = lax.broadcasted_iota(jnp.int32, (block, block), 0) >= lax.broadcasted_iota(
        jnp.int32, (block, block), 1
    )
    inner = jnp.zeros((DH, DH), jnp.float32)
    for b in range(rows // block):
        span = pl.ds(b * block, block)
        query, key, value = q_ref[span, :], k_ref[span, :], v_ref[span, :]
        scores = lax.dot_general(
            query, key, (((1,), (1,)), ((), ())), preferred_element_type=jnp.float32
        )
        scores = jnp.where(causal, scores, 0.0).astype(jnp.bfloat16)
        part = jnp.dot(scores, value, preferred_element_type=jnp.float32)
        if b > 0:
            hi, lo = split_bf16(inner)
            part = part + jnp.dot(query, hi, preferred_element_type=jnp.float32)
            part = part + jnp.dot(query, lo, preferred_element_type=jnp.float32)
        out_ref[span, :] = part
        inner = inner + lax.dot_general(
            key, value, (((0,), (0,)), ((), ())), preferred_element_type=jnp.float32
        )


def out_kernel(q_ref, local_ref, prefix_ref, gain_ref, w_ref, out_ref, acc):
    head = pl.program_id(0)
    hi, lo = split_bf16(prefix_ref[...])
    query = q_ref[...]
    attended = local_ref[...] + jnp.dot(query, hi, preferred_element_type=jnp.float32)
    attended = attended + jnp.dot(query, lo, preferred_element_type=jnp.float32)
    scaled = attended * lax.rsqrt(jnp.mean(attended * attended, -1, keepdims=True) + 1e-05)
    headed = (scaled * gain_ref[...]).astype(jnp.bfloat16)
    part = jnp.dot(headed, w_ref[...], preferred_element_type=jnp.float32)

    @pl.when(head == 0)
    def _():
        acc[...] = part

    @pl.when(head > 0)
    def _():
        acc[...] += part

    @pl.when(head == pl.num_programs(0) - 1)
    def _():
        out_ref[...] = acc[...].astype(out_ref.dtype)


def slab(shift, rows, cols):
    return pl.BlockSpec((None, rows, cols), lambda h: (h + shift, 0, 0))


def local(tokens, norm_gain, w_qkv, conv_weight, head_gain, w_out):
    rows, width = tokens.shape
    tokens_f = tokens.astype(jnp.float32)
    scale = lax.rsqrt(jnp.mean(tokens_f * tokens_f, -1, keepdims=True) + 1e-06)
    normed = (tokens_f * scale * norm_gain).astype(jnp.bfloat16)

    slabs = w_qkv.shape[1] // DH
    projected = jnp.einsum(
        "td,dje->jte", normed, w_qkv.reshape(width, slabs, DH), preferred_element_type=jnp.float32
    ).astype(jnp.bfloat16)

    seq_axes = ("sy", "sz")
    count = lax.axis_size("sy") * lax.axis_size("sz")
    earlier_rows = lax.ppermute(
        projected[:, rows - (KW - 1) :, :], seq_axes, [(i, i + 1) for i in range(count - 1)]
    )
    earlier_rows = jnp.pad(earlier_rows, ((0, 0), (PAD - (KW - 1), 0), (0, 0)))
    taps = jnp.pad(
        conv_weight.reshape(KW, slabs, DH).transpose(1, 0, 2), ((0, 0), (0, PAD - KW), (0, 0))
    )

    mixed_shape = jax.ShapeDtypeStruct((H, rows, DH), jnp.bfloat16)
    query, key, value, state = pl.pallas_call(
        conv_kernel,
        grid=(H,),
        in_specs=[slab(0, rows, DH), slab(H, rows, DH), slab(2 * H, rows, DH)]
        + [slab(0, PAD, DH), slab(H, PAD, DH), slab(2 * H, PAD, DH)]
        + [slab(0, PAD, DH), slab(H, PAD, DH), slab(2 * H, PAD, DH)],
        out_specs=[slab(0, rows, DH)] * 3 + [slab(0, DH, DH)],
        out_shape=[mixed_shape] * 3 + [jax.ShapeDtypeStruct((H, DH, DH), jnp.float32)],
        scratch_shapes=[pltpu.VMEM((rows + PAD, DH), jnp.float32)],
        cost_estimate=pl.CostEstimate(
            flops=H * (3 * rows * DH * 12 + 2 * rows * DH * DH),
            transcendentals=H * 3 * rows * DH,
            bytes_accessed=H * 3 * rows * DH * 4,
        ),
    )(projected, projected, projected, earlier_rows, earlier_rows, earlier_rows, taps, taps, taps)

    block = min(BLOCK, rows)
    local_part = pl.pallas_call(
        local_kernel,
        grid=(H,),
        in_specs=[slab(0, rows, DH)] * 3,
        out_specs=slab(0, rows, DH),
        out_shape=jax.ShapeDtypeStruct((H, rows, DH), jnp.float32),
        cost_estimate=pl.CostEstimate(
            flops=H * (4 * rows * block * DH + 6 * rows * DH * DH),
            transcendentals=0,
            bytes_accessed=H * rows * DH * 10,
        ),
    )(query, key, value)

    zbefore, row_total = ring_earlier(state.astype(jnp.bfloat16), "sz")
    ybefore, _ = ring_earlier(row_total.astype(jnp.bfloat16), "sy")
    prefix = ybefore + zbefore

    out = pl.pallas_call(
        out_kernel,
        grid=(H,),
        in_specs=[
            slab(0, rows, DH),
            slab(0, rows, DH),
            slab(0, DH, DH),
            slab(0, 1, DH),
            slab(0, DH, width),
        ],
        out_specs=pl.BlockSpec((rows, width), lambda h: (0, 0)),
        out_shape=jax.ShapeDtypeStruct((rows, width), jnp.bfloat16),
        scratch_shapes=[pltpu.VMEM((rows, width), jnp.float32)],
        cost_estimate=pl.CostEstimate(
            flops=H * (4 * rows * DH * DH + 2 * rows * DH * width),
            transcendentals=H * rows,
            bytes_accessed=H * rows * DH * 6 + width * width * 2 + rows * width * 2,
        ),
    )(query, local_part, prefix, head_gain.reshape(H, 1, DH), w_out.reshape(H, DH, width))
    return out


def solution(mesh):
    seq = mesh.shape["seq"]
    inner = 4 if seq % 4 == 0 else 1
    grid = Mesh(
        mesh.devices.reshape(mesh.shape["trace"], seq // inner, inner), ("trace", "sy", "sz")
    )
    rows = P(("trace", "sy", "sz"), None)
    placed = (rows, P(), P(), P(), P(), P())
    return jax.shard_map(local, mesh=grid, in_specs=placed, out_specs=rows, check_vma=False)
```

```python
import jax
import jax.numpy as jnp
from jax import lax
from jax.experimental import pallas as pl
from jax.experimental.pallas import tpu as pltpu
from jax.sharding import Mesh
from jax.sharding import PartitionSpec as P

H = 8
DH = 128
KW = 4
BLOCK = 512
PAD = 8


def split_bf16(x):
    hi = lax.reduce_precision(x, exponent_bits=8, mantissa_bits=7)
    return hi.astype(jnp.bfloat16), (x - hi).astype(jnp.bfloat16)


def ring_earlier(x, axis):
    count = lax.axis_size(axis)
    place = lax.axis_index(axis)
    forward = [(i, (i + 1) % count) for i in range(count)]
    backward = [(i, (i - 1) % count) for i in range(count)]
    from_prev = lax.ppermute(x, axis, forward)
    from_next = lax.ppermute(x, axis, backward)
    half = x.shape[0] // 2
    from_far = jnp.concatenate(
        [lax.ppermute(from_prev[:half], axis, forward), lax.ppermute(from_next[half:], axis, backward)],
        0,
    )
    before = jnp.zeros(x.shape, jnp.float32)
    total = x.astype(jnp.float32)
    for offset, part in ((-1, from_prev), (1, from_next), (2, from_far)):
        part = part.astype(jnp.float32)
        earlier = ((place + offset) % count < place).astype(jnp.float32)
        before = before + earlier * part
        total = total + part
    return before, total


def conv_kernel(pq, pk, pv, eq, ek, ev, tq, tk, tv, oq, ok, ov, state_ref, buf):
    rows = pq.shape[0]
    for proj, early, taps, out in ((pq, eq, tq, oq), (pk, ek, tk, ok), (pv, ev, tv, ov)):
        buf[0:PAD, :] = early[...].astype(jnp.float32)
        buf[PAD:, :] = proj[...].astype(jnp.float32)
        summed = jnp.zeros((rows, DH), jnp.float32)
        for offset in range(KW):
            summed = summed + taps[offset : offset + 1, :] * buf[pl.ds(PAD - offset, rows), :]
        out[...] = (summed * jax.nn.sigmoid(summed)).astype(out.dtype)
    state_ref[...] = lax.dot_general(
        ok[...], ov[...], (((0,), (0,)), ((), ())), preferred_element_type=jnp.float32
    )


def local_kernel(q_ref, k_ref, v_ref, out_ref):
    rows = q_ref.shape[0]
    block = min(BLOCK, rows)
    causal = lax.broadcasted_iota(jnp.int32, (block, block), 0) >= lax.broadcasted_iota(
        jnp.int32, (block, block), 1
    )
    inner = jnp.zeros((DH, DH), jnp.float32)
    for b in range(rows // block):
        span = pl.ds(b * block, block)
        query, key, value = q_ref[span, :], k_ref[span, :], v_ref[span, :]
        scores = lax.dot_general(
            query, key, (((1,), (1,)), ((), ())), preferred_element_type=jnp.float32
        )
        scores = jnp.where(causal, scores, 0.0).astype(jnp.bfloat16)
        part = jnp.dot(scores, value, preferred_element_type=jnp.float32)
        if b > 0:
            hi, lo = split_bf16(inner)
            part = part + jnp.dot(query, hi, preferred_element_type=jnp.float32)
            part = part + jnp.dot(query, lo, preferred_element_type=jnp.float32)
        out_ref[span, :] = part
        inner = inner + lax.dot_general(
            key, value, (((0,), (0,)), ((), ())), preferred_element_type=jnp.float32
        )


def head_kernel(q_ref, local_ref, prefix_ref, gain_ref, out_ref):
    hi, lo = split_bf16(prefix_ref[...])
    query = q_ref[...]
    attended = local_ref[...] + jnp.dot(query, hi, preferred_element_type=jnp.float32)
    attended = attended + jnp.dot(query, lo, preferred_element_type=jnp.float32)
    scaled = attended * lax.rsqrt(jnp.mean(attended * attended, -1, keepdims=True) + 1e-05)
    out_ref[...] = (scaled * gain_ref[...]).astype(out_ref.dtype)


def slab(shift, rows, cols):
    return pl.BlockSpec((None, rows, cols), lambda h: (h + shift, 0, 0))


def local(tokens, norm_gain, w_qkv, conv_weight, head_gain, w_out):
    rows, width = tokens.shape
    tokens_f = tokens.astype(jnp.float32)
    scale = lax.rsqrt(jnp.mean(tokens_f * tokens_f, -1, keepdims=True) + 1e-06)
    normed = (tokens_f * scale * norm_gain).astype(jnp.bfloat16)

    slabs = w_qkv.shape[1] // DH
    projected = jnp.einsum(
        "td,dje->jte", normed, w_qkv.reshape(width, slabs, DH), preferred_element_type=jnp.float32
    ).astype(jnp.bfloat16)

    seq_axes = ("sy", "sz")
    count = lax.axis_size("sy") * lax.axis_size("sz")
    earlier_rows = lax.ppermute(
        projected[:, rows - (KW - 1) :, :], seq_axes, [(i, i + 1) for i in range(count - 1)]
    )
    earlier_rows = jnp.pad(earlier_rows, ((0, 0), (PAD - (KW - 1), 0), (0, 0)))
    taps = jnp.pad(
        conv_weight.reshape(KW, slabs, DH).transpose(1, 0, 2), ((0, 0), (0, PAD - KW), (0, 0))
    )

    mixed_shape = jax.ShapeDtypeStruct((H, rows, DH), jnp.bfloat16)
    query, key, value, state = pl.pallas_call(
        conv_kernel,
        grid=(H,),
        in_specs=[slab(0, rows, DH), slab(H, rows, DH), slab(2 * H, rows, DH)]
        + [slab(0, PAD, DH), slab(H, PAD, DH), slab(2 * H, PAD, DH)]
        + [slab(0, PAD, DH), slab(H, PAD, DH), slab(2 * H, PAD, DH)],
        out_specs=[slab(0, rows, DH)] * 3 + [slab(0, DH, DH)],
        out_shape=[mixed_shape] * 3 + [jax.ShapeDtypeStruct((H, DH, DH), jnp.float32)],
        scratch_shapes=[pltpu.VMEM((rows + PAD, DH), jnp.float32)],
        cost_estimate=pl.CostEstimate(
            flops=H * (3 * rows * DH * 12 + 2 * rows * DH * DH),
            transcendentals=H * 3 * rows * DH,
            bytes_accessed=H * 3 * rows * DH * 4,
        ),
    )(projected, projected, projected, earlier_rows, earlier_rows, earlier_rows, taps, taps, taps)

    block = min(BLOCK, rows)
    group = 2

    def local_call(first):
        return pl.pallas_call(
            local_kernel,
            grid=(group,),
            in_specs=[slab(first, rows, DH)] * 3,
            out_specs=slab(0, rows, DH),
            out_shape=jax.ShapeDtypeStruct((group, rows, DH), jnp.float32),
            cost_estimate=pl.CostEstimate(
                flops=group * (4 * rows * block * DH + 6 * rows * DH * DH),
                transcendentals=0,
                bytes_accessed=group * rows * DH * 10,
            ),
        )(query, key, value)

    local_part = jnp.concatenate([local_call(g) for g in range(0, H, group)], 0)

    zbefore, row_total = ring_earlier(state.astype(jnp.bfloat16), "sz")
    ybefore, _ = ring_earlier(row_total.astype(jnp.bfloat16), "sy")
    prefix = ybefore + zbefore

    headed = pl.pallas_call(
        head_kernel,
        grid=(H,),
        in_specs=[slab(0, rows, DH), slab(0, rows, DH), slab(0, DH, DH), slab(0, 1, DH)],
        out_specs=slab(0, rows, DH),
        out_shape=jax.ShapeDtypeStruct((H, rows, DH), jnp.bfloat16),
        cost_estimate=pl.CostEstimate(
            flops=H * 4 * rows * DH * DH, transcendentals=H * rows, bytes_accessed=H * rows * DH * 8
        ),
    )(query, local_part, prefix, head_gain.reshape(H, 1, DH))
    out = jnp.einsum(
        "hte,hen->tn", headed, w_out.reshape(H, DH, width), preferred_element_type=jnp.float32
    )
    return out.astype(jnp.bfloat16)


def solution(mesh):
    seq = mesh.shape["seq"]
    inner = 4 if seq % 4 == 0 else 1
    grid = Mesh(
        mesh.devices.reshape(mesh.shape["trace"], seq // inner, inner), ("trace", "sy", "sz")
    )
    rows = P(("trace", "sy", "sz"), None)
    placed = (rows, P(), P(), P(), P(), P())
    return jax.shard_map(local, mesh=grid, in_specs=placed, out_specs=rows, check_vma=False)
```

```python
import jax
import jax.numpy as jnp
from jax import lax
from jax.experimental import pallas as pl
from jax.experimental.pallas import tpu as pltpu
from jax.sharding import Mesh
from jax.sharding import PartitionSpec as P

H = 8
DH = 128
KW = 4
BLOCK = 512
PAD = 8


def split_bf16(x):
    hi = lax.reduce_precision(x, exponent_bits=8, mantissa_bits=7)
    return hi.astype(jnp.bfloat16), (x - hi).astype(jnp.bfloat16)


def gather_earlier(x, axis):
    count = lax.axis_size(axis)
    place = lax.axis_index(axis)
    gathered = lax.all_to_all(jnp.broadcast_to(x, (count,) + x.shape), axis, 0, 0)
    values = gathered.astype(jnp.float32)
    earlier = (lax.iota(jnp.int32, count) < place).astype(jnp.float32)
    return jnp.sum(values * earlier[:, None, None, None], 0), jnp.sum(values, 0)


def conv_kernel(pq, pk, pv, eq, ek, ev, tq, tk, tv, oq, ok, ov, state_ref, buf):
    rows = pq.shape[0]
    for proj, early, taps, out in ((pq, eq, tq, oq), (pk, ek, tk, ok), (pv, ev, tv, ov)):
        buf[0:PAD, :] = early[...].astype(jnp.float32)
        buf[PAD:, :] = proj[...].astype(jnp.float32)
        summed = jnp.zeros((rows, DH), jnp.float32)
        for offset in range(KW):
            summed = summed + taps[offset : offset + 1, :] * buf[pl.ds(PAD - offset, rows), :]
        out[...] = (summed * jax.nn.sigmoid(summed)).astype(out.dtype)
    state_ref[...] = lax.dot_general(
        ok[...], ov[...], (((0,), (0,)), ((), ())), preferred_element_type=jnp.float32
    )


def local_kernel(q_ref, k_ref, v_ref, out_ref):
    rows = q_ref.shape[0]
    block = min(BLOCK, rows)
    causal = lax.broadcasted_iota(jnp.int32, (block, block), 0) >= lax.broadcasted_iota(
        jnp.int32, (block, block), 1
    )
    inner = jnp.zeros((DH, DH), jnp.float32)
    for b in range(rows // block):
        span = pl.ds(b * block, block)
        query, key, value = q_ref[span, :], k_ref[span, :], v_ref[span, :]
        scores = lax.dot_general(
            query, key, (((1,), (1,)), ((), ())), preferred_element_type=jnp.float32
        )
        scores = jnp.where(causal, scores, 0.0).astype(jnp.bfloat16)
        part = jnp.dot(scores, value, preferred_element_type=jnp.float32)
        if b > 0:
            hi, lo = split_bf16(inner)
            part = part + jnp.dot(query, hi, preferred_element_type=jnp.float32)
            part = part + jnp.dot(query, lo, preferred_element_type=jnp.float32)
        out_ref[span, :] = part
        inner = inner + lax.dot_general(
            key, value, (((0,), (0,)), ((), ())), preferred_element_type=jnp.float32
        )


def out_kernel(q_ref, local_ref, prefix_ref, gain_ref, w_ref, out_ref, acc):
    head = pl.program_id(0)
    hi, lo = split_bf16(prefix_ref[...])
    query = q_ref[...]
    attended = local_ref[...] + jnp.dot(query, hi, preferred_element_type=jnp.float32)
    attended = attended + jnp.dot(query, lo, preferred_element_type=jnp.float32)
    scaled = attended * lax.rsqrt(jnp.mean(attended * attended, -1, keepdims=True) + 1e-05)
    headed = (scaled * gain_ref[...]).astype(jnp.bfloat16)
    part = jnp.dot(headed, w_ref[...], preferred_element_type=jnp.float32)

    @pl.when(head == 0)
    def _():
        acc[...] = part

    @pl.when(head > 0)
    def _():
        acc[...] += part

    @pl.when(head == pl.num_programs(0) - 1)
    def _():
        out_ref[...] = acc[...].astype(out_ref.dtype)


def slab(shift, rows, cols):
    return pl.BlockSpec((None, rows, cols), lambda h: (h + shift, 0, 0))


def local(tokens, norm_gain, w_qkv, conv_weight, head_gain, w_out):
    rows, width = tokens.shape
    tokens_f = tokens.astype(jnp.float32)
    scale = lax.rsqrt(jnp.mean(tokens_f * tokens_f, -1, keepdims=True) + 1e-06)
    normed = (tokens_f * scale * norm_gain).astype(jnp.bfloat16)

    slabs = w_qkv.shape[1] // DH
    projected = jnp.einsum(
        "td,dje->jte", normed, w_qkv.reshape(width, slabs, DH), preferred_element_type=jnp.float32
    ).astype(jnp.bfloat16)

    seq_axes = ("sy", "sz")
    count = lax.axis_size("sy") * lax.axis_size("sz")
    earlier_rows = lax.ppermute(
        projected[:, rows - (KW - 1) :, :], seq_axes, [(i, i + 1) for i in range(count - 1)]
    )
    earlier_rows = jnp.pad(earlier_rows, ((0, 0), (PAD - (KW - 1), 0), (0, 0)))
    taps = jnp.pad(
        conv_weight.reshape(KW, slabs, DH).transpose(1, 0, 2), ((0, 0), (0, PAD - KW), (0, 0))
    )

    mixed_shape = jax.ShapeDtypeStruct((H, rows, DH), jnp.bfloat16)
    query, key, value, state = pl.pallas_call(
        conv_kernel,
        grid=(H,),
        in_specs=[slab(0, rows, DH), slab(H, rows, DH), slab(2 * H, rows, DH)]
        + [slab(0, PAD, DH), slab(H, PAD, DH), slab(2 * H, PAD, DH)]
        + [slab(0, PAD, DH), slab(H, PAD, DH), slab(2 * H, PAD, DH)],
        out_specs=[slab(0, rows, DH)] * 3 + [slab(0, DH, DH)],
        out_shape=[mixed_shape] * 3 + [jax.ShapeDtypeStruct((H, DH, DH), jnp.float32)],
        scratch_shapes=[pltpu.VMEM((rows + PAD, DH), jnp.float32)],
        cost_estimate=pl.CostEstimate(
            flops=H * (3 * rows * DH * 12 + 2 * rows * DH * DH),
            transcendentals=H * 3 * rows * DH,
            bytes_accessed=H * 3 * rows * DH * 4,
        ),
    )(projected, projected, projected, earlier_rows, earlier_rows, earlier_rows, taps, taps, taps)

    block = min(BLOCK, rows)
    local_part = pl.pallas_call(
        local_kernel,
        grid=(H,),
        in_specs=[slab(0, rows, DH)] * 3,
        out_specs=slab(0, rows, DH),
        out_shape=jax.ShapeDtypeStruct((H, rows, DH), jnp.float32),
        cost_estimate=pl.CostEstimate(
            flops=H * (4 * rows * block * DH + 6 * rows * DH * DH),
            transcendentals=0,
            bytes_accessed=H * rows * DH * 10,
        ),
    )(query, key, value)

    zbefore, row_total = gather_earlier(state.astype(jnp.bfloat16), "sz")
    ybefore, _ = gather_earlier(row_total.astype(jnp.bfloat16), "sy")
    prefix = ybefore + zbefore

    out = pl.pallas_call(
        out_kernel,
        grid=(H,),
        in_specs=[
            slab(0, rows, DH),
            slab(0, rows, DH),
            slab(0, DH, DH),
            slab(0, 1, DH),
            slab(0, DH, width),
        ],
        out_specs=pl.BlockSpec((rows, width), lambda h: (0, 0)),
        out_shape=jax.ShapeDtypeStruct((rows, width), jnp.bfloat16),
        scratch_shapes=[pltpu.VMEM((rows, width), jnp.float32)],
        cost_estimate=pl.CostEstimate(
            flops=H * (4 * rows * DH * DH + 2 * rows * DH * width),
            transcendentals=H * rows,
            bytes_accessed=H * rows * DH * 6 + width * width * 2 + rows * width * 2,
        ),
    )(query, local_part, prefix, head_gain.reshape(H, 1, DH), w_out.reshape(H, DH, width))
    return out


def solution(mesh):
    seq = mesh.shape["seq"]
    inner = 4 if seq % 4 == 0 else 1
    grid = Mesh(
        mesh.devices.reshape(mesh.shape["trace"], seq // inner, inner), ("trace", "sy", "sz")
    )
    rows = P(("trace", "sy", "sz"), None)
    placed = (rows, P(), P(), P(), P(), P())
    return jax.shard_map(local, mesh=grid, in_specs=placed, out_specs=rows, check_vma=False)
```

```python
import jax
import jax.numpy as jnp
from jax import lax
from jax.experimental import pallas as pl
from jax.experimental.pallas import tpu as pltpu
from jax.sharding import Mesh
from jax.sharding import PartitionSpec as P

H = 8
DH = 128
KW = 4
BLOCK = 512
PAD = 8


def split_bf16(x):
    hi = lax.reduce_precision(x, exponent_bits=8, mantissa_bits=7)
    return hi.astype(jnp.bfloat16), (x - hi).astype(jnp.bfloat16)


def ring_sum(messages, axis, weight=None):
    count = lax.axis_size(axis)
    total = None
    for offset, message in messages.items():
        pairs = [(i, (i + offset) % count) for i in range(count)]
        part = lax.ppermute(message.astype(jnp.bfloat16), axis, pairs).astype(jnp.float32)
        if weight is not None:
            part = weight(offset) * part
        total = part if total is None else total + part
    return total


def before_mask(axis, offset):
    count = lax.axis_size(axis)
    place = lax.axis_index(axis)
    return (place < (place + offset) % count).astype(jnp.float32)


def after_mask(axis, offset):
    count = lax.axis_size(axis)
    place = lax.axis_index(axis)
    return ((place - offset) % count < place).astype(jnp.float32)


def earlier_states(state):
    offsets = (1, -1, 2)
    half = state.shape[0] // 2
    first, second = state[:half], state[half:]
    both = lambda o: jnp.stack([after_mask("sz", o), jnp.float32(1.0)])[:, None, None, None]
    row = ring_sum({o: first for o in offsets}, "sz", both)
    row_before, row_total = row[0], row[1] + first
    rows_before = ring_sum({o: row_total for o in offsets}, "sy", lambda o: after_mask("sy", o))
    column_before = ring_sum({o: second for o in offsets}, "sy", lambda o: after_mask("sy", o))
    mixed_before = column_before + ring_sum(
        {o: column_before + second * before_mask("sz", o) for o in offsets}, "sz"
    )
    return jnp.concatenate([row_before + rows_before, mixed_before], 0)


def conv_kernel(pq, pk, pv, eq, ek, ev, tq, tk, tv, oq, ok, ov, state_ref, buf):
    rows = pq.shape[0]
    for proj, early, taps, out in ((pq, eq, tq, oq), (pk, ek, tk, ok), (pv, ev, tv, ov)):
        buf[0:PAD, :] = early[...].astype(jnp.float32)
        buf[PAD:, :] = proj[...].astype(jnp.float32)
        summed = jnp.zeros((rows, DH), jnp.float32)
        for offset in range(KW):
            summed = summed + taps[offset : offset + 1, :] * buf[pl.ds(PAD - offset, rows), :]
        out[...] = (summed * jax.nn.sigmoid(summed)).astype(out.dtype)
    state_ref[...] = lax.dot_general(
        ok[...], ov[...], (((0,), (0,)), ((), ())), preferred_element_type=jnp.float32
    )


def local_kernel(q_ref, k_ref, v_ref, out_ref):
    rows = q_ref.shape[0]
    block = min(BLOCK, rows)
    causal = lax.broadcasted_iota(jnp.int32, (block, block), 0) >= lax.broadcasted_iota(
        jnp.int32, (block, block), 1
    )
    inner = jnp.zeros((DH, DH), jnp.float32)
    for b in range(rows // block):
        span = pl.ds(b * block, block)
        query, key, value = q_ref[span, :], k_ref[span, :], v_ref[span, :]
        scores = lax.dot_general(
            query, key, (((1,), (1,)), ((), ())), preferred_element_type=jnp.float32
        )
        scores = jnp.where(causal, scores, 0.0).astype(jnp.bfloat16)
        part = jnp.dot(scores, value, preferred_element_type=jnp.float32)
        if b > 0:
            hi, lo = split_bf16(inner)
            part = part + jnp.dot(query, hi, preferred_element_type=jnp.float32)
            part = part + jnp.dot(query, lo, preferred_element_type=jnp.float32)
        out_ref[span, :] = part
        inner = inner + lax.dot_general(
            key, value, (((0,), (0,)), ((), ())), preferred_element_type=jnp.float32
        )


def out_kernel(q_ref, local_ref, prefix_ref, gain_ref, w_ref, out_ref, acc):
    head = pl.program_id(0)
    hi, lo = split_bf16(prefix_ref[...])
    query = q_ref[...]
    attended = local_ref[...] + jnp.dot(query, hi, preferred_element_type=jnp.float32)
    attended = attended + jnp.dot(query, lo, preferred_element_type=jnp.float32)
    scaled = attended * lax.rsqrt(jnp.mean(attended * attended, -1, keepdims=True) + 1e-05)
    headed = (scaled * gain_ref[...]).astype(jnp.bfloat16)
    part = jnp.dot(headed, w_ref[...], preferred_element_type=jnp.float32)

    @pl.when(head == 0)
    def _():
        acc[...] = part

    @pl.when(head > 0)
    def _():
        acc[...] += part

    @pl.when(head == pl.num_programs(0) - 1)
    def _():
        out_ref[...] = acc[...].astype(out_ref.dtype)


def slab(shift, rows, cols):
    return pl.BlockSpec((None, rows, cols), lambda h: (h + shift, 0, 0))


def local(tokens, norm_gain, w_qkv, conv_weight, head_gain, w_out):
    rows, width = tokens.shape
    tokens_f = tokens.astype(jnp.float32)
    scale = lax.rsqrt(jnp.mean(tokens_f * tokens_f, -1, keepdims=True) + 1e-06)
    normed = (tokens_f * scale * norm_gain).astype(jnp.bfloat16)

    slabs = w_qkv.shape[1] // DH
    projected = jnp.einsum(
        "td,dje->jte", normed, w_qkv.reshape(width, slabs, DH), preferred_element_type=jnp.float32
    ).astype(jnp.bfloat16)

    seq_axes = ("sy", "sz")
    count = lax.axis_size("sy") * lax.axis_size("sz")
    earlier_rows = lax.ppermute(
        projected[:, rows - (KW - 1) :, :], seq_axes, [(i, i + 1) for i in range(count - 1)]
    )
    earlier_rows = jnp.pad(earlier_rows, ((0, 0), (PAD - (KW - 1), 0), (0, 0)))
    taps = jnp.pad(
        conv_weight.reshape(KW, slabs, DH).transpose(1, 0, 2), ((0, 0), (0, PAD - KW), (0, 0))
    )

    mixed_shape = jax.ShapeDtypeStruct((H, rows, DH), jnp.bfloat16)
    query, key, value, state = pl.pallas_call(
        conv_kernel,
        grid=(H,),
        in_specs=[slab(0, rows, DH), slab(H, rows, DH), slab(2 * H, rows, DH)]
        + [slab(0, PAD, DH), slab(H, PAD, DH), slab(2 * H, PAD, DH)]
        + [slab(0, PAD, DH), slab(H, PAD, DH), slab(2 * H, PAD, DH)],
        out_specs=[slab(0, rows, DH)] * 3 + [slab(0, DH, DH)],
        out_shape=[mixed_shape] * 3 + [jax.ShapeDtypeStruct((H, DH, DH), jnp.float32)],
        scratch_shapes=[pltpu.VMEM((rows + PAD, DH), jnp.float32)],
        cost_estimate=pl.CostEstimate(
            flops=H * (3 * rows * DH * 12 + 2 * rows * DH * DH),
            transcendentals=H * 3 * rows * DH,
            bytes_accessed=H * 3 * rows * DH * 4,
        ),
    )(projected, projected, projected, earlier_rows, earlier_rows, earlier_rows, taps, taps, taps)

    block = min(BLOCK, rows)
    local_part = pl.pallas_call(
        local_kernel,
        grid=(H,),
        in_specs=[slab(0, rows, DH)] * 3,
        out_specs=slab(0, rows, DH),
        out_shape=jax.ShapeDtypeStruct((H, rows, DH), jnp.float32),
        cost_estimate=pl.CostEstimate(
            flops=H * (4 * rows * block * DH + 6 * rows * DH * DH),
            transcendentals=0,
            bytes_accessed=H * rows * DH * 10,
        ),
    )(query, key, value)

    prefix = earlier_states(state)

    out = pl.pallas_call(
        out_kernel,
        grid=(H,),
        in_specs=[
            slab(0, rows, DH),
            slab(0, rows, DH),
            slab(0, DH, DH),
            slab(0, 1, DH),
            slab(0, DH, width),
        ],
        out_specs=pl.BlockSpec((rows, width), lambda h: (0, 0)),
        out_shape=jax.ShapeDtypeStruct((rows, width), jnp.bfloat16),
        scratch_shapes=[pltpu.VMEM((rows, width), jnp.float32)],
        cost_estimate=pl.CostEstimate(
            flops=H * (4 * rows * DH * DH + 2 * rows * DH * width),
            transcendentals=H * rows,
            bytes_accessed=H * rows * DH * 6 + width * width * 2 + rows * width * 2,
        ),
    )(query, local_part, prefix, head_gain.reshape(H, 1, DH), w_out.reshape(H, DH, width))
    return out


def solution(mesh):
    seq = mesh.shape["seq"]
    inner = 4 if seq % 4 == 0 else 1
    grid = Mesh(
        mesh.devices.reshape(mesh.shape["trace"], seq // inner, inner), ("trace", "sy", "sz")
    )
    rows = P(("trace", "sy", "sz"), None)
    placed = (rows, P(), P(), P(), P(), P())
    return jax.shard_map(local, mesh=grid, in_specs=placed, out_specs=rows, check_vma=False)
```

```python
import functools

import jax
import jax.numpy as jnp
from jax import lax
from jax.experimental import pallas as pl
from jax.experimental.pallas import tpu as pltpu
from jax.sharding import Mesh
from jax.sharding import PartitionSpec as P

H = 8
DH = 128
KW = 4
BLOCK = 512
PAD = 8


def split_bf16(x):
    hi = lax.reduce_precision(x, exponent_bits=8, mantissa_bits=7)
    return hi.astype(jnp.bfloat16), (x - hi).astype(jnp.bfloat16)


def ring_sum(messages, axis, weight=None):
    count = lax.axis_size(axis)
    total = None
    for offset, message in messages.items():
        pairs = [(i, (i + offset) % count) for i in range(count)]
        part = lax.ppermute(message.astype(jnp.bfloat16), axis, pairs).astype(jnp.float32)
        if weight is not None:
            part = weight(offset) * part
        total = part if total is None else total + part
    return total


def before_mask(axis, offset):
    count = lax.axis_size(axis)
    place = lax.axis_index(axis)
    return (place < (place + offset) % count).astype(jnp.float32)


def after_mask(axis, offset):
    count = lax.axis_size(axis)
    place = lax.axis_index(axis)
    return ((place - offset) % count < place).astype(jnp.float32)


def earlier_states(state):
    offsets = (1, -1, 2)
    half = state.shape[0] // 2
    first, second = state[:half], state[half:]
    both = lambda o: jnp.stack([after_mask("sz", o), jnp.float32(1.0)])[:, None, None, None]
    row = ring_sum({o: first for o in offsets}, "sz", both)
    row_before, row_total = row[0], row[1] + first
    rows_before = ring_sum({o: row_total for o in offsets}, "sy", lambda o: after_mask("sy", o))
    column_before = ring_sum({o: second for o in offsets}, "sy", lambda o: after_mask("sy", o))
    mixed_before = column_before + ring_sum(
        {o: column_before + second * before_mask("sz", o) for o in offsets}, "sz"
    )
    return jnp.concatenate([row_before + rows_before, mixed_before], 0)


def conv_kernel(count, with_state, *refs):
    projs, earlies, tapss = refs[:count], refs[count : 2 * count], refs[2 * count : 3 * count]
    outs, buf = refs[3 * count : 4 * count], refs[-1]
    rows = projs[0].shape[0]
    for proj, early, taps, out in zip(projs, earlies, tapss, outs):
        buf[0:PAD, :] = early[...].astype(jnp.float32)
        buf[PAD:, :] = proj[...].astype(jnp.float32)
        summed = jnp.zeros((rows, DH), jnp.float32)
        for offset in range(KW):
            summed = summed + taps[offset : offset + 1, :] * buf[pl.ds(PAD - offset, rows), :]
        out[...] = (summed * jax.nn.sigmoid(summed)).astype(out.dtype)
    if with_state:
        refs[4 * count][...] = lax.dot_general(
            outs[0][...], outs[1][...], (((0,), (0,)), ((), ())), preferred_element_type=jnp.float32
        )


def conv_call(projected, earlier, taps, shifts, base, with_state):
    count = len(shifts)
    rows = projected.shape[1]
    mixed = jax.ShapeDtypeStruct((H, rows, DH), jnp.bfloat16)
    out_specs = [slab(0, rows, DH)] * count
    out_shape = [mixed] * count
    if with_state:
        out_specs.append(slab(0, DH, DH))
        out_shape.append(jax.ShapeDtypeStruct((H, DH, DH), jnp.float32))
    return pl.pallas_call(
        functools.partial(conv_kernel, count, with_state),
        grid=(H,),
        in_specs=[slab(shift, rows, DH) for shift in shifts]
        + [slab(base + shift, PAD, DH) for shift in shifts] * 2,
        out_specs=out_specs,
        out_shape=out_shape,
        scratch_shapes=[pltpu.VMEM((rows + PAD, DH), jnp.float32)],
        cost_estimate=pl.CostEstimate(
            flops=H * count * rows * DH * (12 + 2 * DH),
            transcendentals=H * count * rows * DH,
            bytes_accessed=H * count * rows * DH * 4,
        ),
    )(*([projected] * count + [earlier] * count + [taps] * count))


def local_kernel(q_ref, k_ref, v_ref, out_ref):
    rows = q_ref.shape[0]
    block = min(BLOCK, rows)
    causal = lax.broadcasted_iota(jnp.int32, (block, block), 0) >= lax.broadcasted_iota(
        jnp.int32, (block, block), 1
    )
    inner = jnp.zeros((DH, DH), jnp.float32)
    for b in range(rows // block):
        span = pl.ds(b * block, block)
        query, key, value = q_ref[span, :], k_ref[span, :], v_ref[span, :]
        scores = lax.dot_general(
            query, key, (((1,), (1,)), ((), ())), preferred_element_type=jnp.float32
        )
        scores = jnp.where(causal, scores, 0.0).astype(jnp.bfloat16)
        part = jnp.dot(scores, value, preferred_element_type=jnp.float32)
        if b > 0:
            hi, lo = split_bf16(inner)
            part = part + jnp.dot(query, hi, preferred_element_type=jnp.float32)
            part = part + jnp.dot(query, lo, preferred_element_type=jnp.float32)
        out_ref[span, :] = part
        inner = inner + lax.dot_general(
            key, value, (((0,), (0,)), ((), ())), preferred_element_type=jnp.float32
        )


def out_kernel(q_ref, local_ref, prefix_ref, gain_ref, w_ref, out_ref, acc):
    head = pl.program_id(0)
    hi, lo = split_bf16(prefix_ref[...])
    query = q_ref[...]
    attended = local_ref[...] + jnp.dot(query, hi, preferred_element_type=jnp.float32)
    attended = attended + jnp.dot(query, lo, preferred_element_type=jnp.float32)
    scaled = attended * lax.rsqrt(jnp.mean(attended * attended, -1, keepdims=True) + 1e-05)
    headed = (scaled * gain_ref[...]).astype(jnp.bfloat16)
    part = jnp.dot(headed, w_ref[...], preferred_element_type=jnp.float32)

    @pl.when(head == 0)
    def _():
        acc[...] = part

    @pl.when(head > 0)
    def _():
        acc[...] += part

    @pl.when(head == pl.num_programs(0) - 1)
    def _():
        out_ref[...] = acc[...].astype(out_ref.dtype)


def slab(shift, rows, cols):
    return pl.BlockSpec((None, rows, cols), lambda h: (h + shift, 0, 0))


def local(tokens, norm_gain, w_qkv, conv_weight, head_gain, w_out):
    rows, width = tokens.shape
    seq_axes = ("sy", "sz")
    count = lax.axis_size("sy") * lax.axis_size("sz")
    earlier_tokens = lax.ppermute(
        tokens[rows - (KW - 1) :], seq_axes, [(i, i + 1) for i in range(count - 1)]
    )
    earlier_tokens = jnp.pad(earlier_tokens, ((PAD - (KW - 1), 0), (0, 0)))

    def input_norm(values):
        values_f = values.astype(jnp.float32)
        scale = lax.rsqrt(jnp.mean(values_f * values_f, -1, keepdims=True) + 1e-06)
        return (values_f * scale * norm_gain).astype(jnp.bfloat16)

    slabs = w_qkv.shape[1] // DH
    weights = w_qkv.reshape(width, slabs, DH)

    def project(values, first, last):
        return jnp.einsum(
            "td,dje->jte", values, weights[:, first:last], preferred_element_type=jnp.float32
        ).astype(jnp.bfloat16)

    normed = input_norm(tokens)
    earlier_rows = project(input_norm(earlier_tokens), 0, slabs)
    taps = jnp.pad(
        conv_weight.reshape(KW, slabs, DH).transpose(1, 0, 2), ((0, 0), (0, PAD - KW), (0, 0))
    )

    kv_projected = project(normed, H, slabs)
    key, value, state = conv_call(kv_projected, earlier_rows, taps, (0, H), H, True)
    prefix = earlier_states(state)

    q_projected = project(normed, 0, H)
    (query,) = conv_call(q_projected, earlier_rows, taps, (0,), 0, False)

    block = min(BLOCK, rows)
    local_part = pl.pallas_call(
        local_kernel,
        grid=(H,),
        in_specs=[slab(0, rows, DH)] * 3,
        out_specs=slab(0, rows, DH),
        out_shape=jax.ShapeDtypeStruct((H, rows, DH), jnp.float32),
        cost_estimate=pl.CostEstimate(
            flops=H * (4 * rows * block * DH + 6 * rows * DH * DH),
            transcendentals=0,
            bytes_accessed=H * rows * DH * 10,
        ),
    )(query, key, value)

    out = pl.pallas_call(
        out_kernel,
        grid=(H,),
        in_specs=[
            slab(0, rows, DH),
            slab(0, rows, DH),
            slab(0, DH, DH),
            slab(0, 1, DH),
            slab(0, DH, width),
        ],
        out_specs=pl.BlockSpec((rows, width), lambda h: (0, 0)),
        out_shape=jax.ShapeDtypeStruct((rows, width), jnp.bfloat16),
        scratch_shapes=[pltpu.VMEM((rows, width), jnp.float32)],
        cost_estimate=pl.CostEstimate(
            flops=H * (4 * rows * DH * DH + 2 * rows * DH * width),
            transcendentals=H * rows,
            bytes_accessed=H * rows * DH * 6 + width * width * 2 + rows * width * 2,
        ),
    )(query, local_part, prefix, head_gain.reshape(H, 1, DH), w_out.reshape(H, DH, width))
    return out


def solution(mesh):
    seq = mesh.shape["seq"]
    inner = 4 if seq % 4 == 0 else 1
    grid = Mesh(
        mesh.devices.reshape(mesh.shape["trace"], seq // inner, inner), ("trace", "sy", "sz")
    )
    rows = P(("trace", "sy", "sz"), None)
    placed = (rows, P(), P(), P(), P(), P())
    return jax.shard_map(local, mesh=grid, in_specs=placed, out_specs=rows, check_vma=False)
```

```python
import functools

import jax
import jax.numpy as jnp
from jax import lax
from jax.experimental import pallas as pl
from jax.experimental.pallas import tpu as pltpu
from jax.sharding import Mesh
from jax.sharding import PartitionSpec as P

H = 8
DH = 128
KW = 4
BLOCK = 512
PAD = 8


def split_bf16(x):
    hi = lax.reduce_precision(x, exponent_bits=8, mantissa_bits=7)
    return hi.astype(jnp.bfloat16), (x - hi).astype(jnp.bfloat16)


def gather_earlier(x, axis):
    count = lax.axis_size(axis)
    place = lax.axis_index(axis)
    gathered = lax.all_to_all(jnp.broadcast_to(x, (count,) + x.shape), axis, 0, 0)
    values = gathered.astype(jnp.float32)
    earlier = (lax.iota(jnp.int32, count) < place).astype(jnp.float32)
    return jnp.sum(values * earlier[:, None, None, None], 0), jnp.sum(values, 0)


def conv_kernel(count, with_state, *refs):
    projs, earlies, tapss = refs[:count], refs[count : 2 * count], refs[2 * count : 3 * count]
    outs, buf = refs[3 * count : 4 * count], refs[-1]
    rows = projs[0].shape[0]
    for proj, early, taps, out in zip(projs, earlies, tapss, outs):
        buf[0:PAD, :] = early[...].astype(jnp.float32)
        buf[PAD:, :] = proj[...].astype(jnp.float32)
        summed = jnp.zeros((rows, DH), jnp.float32)
        for offset in range(KW):
            summed = summed + taps[offset : offset + 1, :] * buf[pl.ds(PAD - offset, rows), :]
        out[...] = (summed * jax.nn.sigmoid(summed)).astype(out.dtype)
    if with_state:
        refs[4 * count][...] = lax.dot_general(
            outs[0][...], outs[1][...], (((0,), (0,)), ((), ())), preferred_element_type=jnp.float32
        )


def conv_call(projected, earlier, taps, shifts, base, with_state):
    count = len(shifts)
    rows = projected.shape[1]
    mixed = jax.ShapeDtypeStruct((H, rows, DH), jnp.bfloat16)
    out_specs = [slab(0, rows, DH)] * count
    out_shape = [mixed] * count
    if with_state:
        out_specs.append(slab(0, DH, DH))
        out_shape.append(jax.ShapeDtypeStruct((H, DH, DH), jnp.float32))
    return pl.pallas_call(
        functools.partial(conv_kernel, count, with_state),
        grid=(H,),
        in_specs=[slab(shift, rows, DH) for shift in shifts]
        + [slab(base + shift, PAD, DH) for shift in shifts] * 2,
        out_specs=out_specs,
        out_shape=out_shape,
        scratch_shapes=[pltpu.VMEM((rows + PAD, DH), jnp.float32)],
        cost_estimate=pl.CostEstimate(
            flops=H * count * rows * DH * (12 + 2 * DH),
            transcendentals=H * count * rows * DH,
            bytes_accessed=H * count * rows * DH * 4,
        ),
    )(*([projected] * count + [earlier] * count + [taps] * count))


def local_kernel(q_ref, k_ref, v_ref, out_ref):
    rows = q_ref.shape[0]
    block = min(BLOCK, rows)
    causal = lax.broadcasted_iota(jnp.int32, (block, block), 0) >= lax.broadcasted_iota(
        jnp.int32, (block, block), 1
    )
    inner = jnp.zeros((DH, DH), jnp.float32)
    for b in range(rows // block):
        span = pl.ds(b * block, block)
        query, key, value = q_ref[span, :], k_ref[span, :], v_ref[span, :]
        scores = lax.dot_general(
            query, key, (((1,), (1,)), ((), ())), preferred_element_type=jnp.float32
        )
        scores = jnp.where(causal, scores, 0.0).astype(jnp.bfloat16)
        part = jnp.dot(scores, value, preferred_element_type=jnp.float32)
        if b > 0:
            hi, lo = split_bf16(inner)
            part = part + jnp.dot(query, hi, preferred_element_type=jnp.float32)
            part = part + jnp.dot(query, lo, preferred_element_type=jnp.float32)
        out_ref[span, :] = part
        inner = inner + lax.dot_general(
            key, value, (((0,), (0,)), ((), ())), preferred_element_type=jnp.float32
        )


def out_kernel(q_ref, local_ref, prefix_ref, gain_ref, w_ref, out_ref, acc):
    head = pl.program_id(0)
    hi, lo = split_bf16(prefix_ref[...])
    query = q_ref[...]
    attended = local_ref[...] + jnp.dot(query, hi, preferred_element_type=jnp.float32)
    attended = attended + jnp.dot(query, lo, preferred_element_type=jnp.float32)
    scaled = attended * lax.rsqrt(jnp.mean(attended * attended, -1, keepdims=True) + 1e-05)
    headed = (scaled * gain_ref[...]).astype(jnp.bfloat16)
    part = jnp.dot(headed, w_ref[...], preferred_element_type=jnp.float32)

    @pl.when(head == 0)
    def _():
        acc[...] = part

    @pl.when(head > 0)
    def _():
        acc[...] += part

    @pl.when(head == pl.num_programs(0) - 1)
    def _():
        out_ref[...] = acc[...].astype(out_ref.dtype)


def slab(shift, rows, cols):
    return pl.BlockSpec((None, rows, cols), lambda h: (h + shift, 0, 0))


def local(tokens, norm_gain, w_qkv, conv_weight, head_gain, w_out):
    rows, width = tokens.shape
    tokens_f = tokens.astype(jnp.float32)
    scale = lax.rsqrt(jnp.mean(tokens_f * tokens_f, -1, keepdims=True) + 1e-06)
    normed = (tokens_f * scale * norm_gain).astype(jnp.bfloat16)

    slabs = w_qkv.shape[1] // DH
    projected = jnp.einsum(
        "td,dje->jte", normed, w_qkv.reshape(width, slabs, DH), preferred_element_type=jnp.float32
    ).astype(jnp.bfloat16)

    seq_axes = ("sy", "sz")
    count = lax.axis_size("sy") * lax.axis_size("sz")
    earlier_rows = lax.ppermute(
        projected[:, rows - (KW - 1) :, :], seq_axes, [(i, i + 1) for i in range(count - 1)]
    )
    earlier_rows = jnp.pad(earlier_rows, ((0, 0), (PAD - (KW - 1), 0), (0, 0)))
    taps = jnp.pad(
        conv_weight.reshape(KW, slabs, DH).transpose(1, 0, 2), ((0, 0), (0, PAD - KW), (0, 0))
    )

    key, value, state = conv_call(projected, earlier_rows, taps, (H, 2 * H), 0, True)
    zbefore, row_total = gather_earlier(state.astype(jnp.bfloat16), "sz")
    ybefore, _ = gather_earlier(row_total.astype(jnp.bfloat16), "sy")
    prefix = ybefore + zbefore

    (query,) = conv_call(projected, earlier_rows, taps, (0,), 0, False)

    block = min(BLOCK, rows)
    local_part = pl.pallas_call(
        local_kernel,
        grid=(H,),
        in_specs=[slab(0, rows, DH)] * 3,
        out_specs=slab(0, rows, DH),
        out_shape=jax.ShapeDtypeStruct((H, rows, DH), jnp.float32),
        cost_estimate=pl.CostEstimate(
            flops=H * (4 * rows * block * DH + 6 * rows * DH * DH),
            transcendentals=0,
            bytes_accessed=H * rows * DH * 10,
        ),
    )(query, key, value)

    out = pl.pallas_call(
        out_kernel,
        grid=(H,),
        in_specs=[
            slab(0, rows, DH),
            slab(0, rows, DH),
            slab(0, DH, DH),
            slab(0, 1, DH),
            slab(0, DH, width),
        ],
        out_specs=pl.BlockSpec((rows, width), lambda h: (0, 0)),
        out_shape=jax.ShapeDtypeStruct((rows, width), jnp.bfloat16),
        scratch_shapes=[pltpu.VMEM((rows, width), jnp.float32)],
        cost_estimate=pl.CostEstimate(
            flops=H * (4 * rows * DH * DH + 2 * rows * DH * width),
            transcendentals=H * rows,
            bytes_accessed=H * rows * DH * 6 + width * width * 2 + rows * width * 2,
        ),
    )(query, local_part, prefix, head_gain.reshape(H, 1, DH), w_out.reshape(H, DH, width))
    return out


def solution(mesh):
    seq = mesh.shape["seq"]
    inner = 4 if seq % 4 == 0 else 1
    grid = Mesh(
        mesh.devices.reshape(mesh.shape["trace"], seq // inner, inner), ("trace", "sy", "sz")
    )
    rows = P(("trace", "sy", "sz"), None)
    placed = (rows, P(), P(), P(), P(), P())
    return jax.shard_map(local, mesh=grid, in_specs=placed, out_specs=rows, check_vma=False)
```

```python
import jax
import jax.numpy as jnp
from jax import lax
from jax.experimental import pallas as pl
from jax.experimental.pallas import tpu as pltpu
from jax.sharding import Mesh
from jax.sharding import PartitionSpec as P

H = 8
DH = 128
KW = 4
BLOCK = 512
PAD = 8


def split_bf16(x):
    hi = lax.reduce_precision(x, exponent_bits=8, mantissa_bits=7)
    return hi.astype(jnp.bfloat16), (x - hi).astype(jnp.bfloat16)


def gather_earlier(x, axis):
    count = lax.axis_size(axis)
    place = lax.axis_index(axis)
    gathered = lax.all_to_all(jnp.broadcast_to(x, (count,) + x.shape), axis, 0, 0)
    values = gathered.astype(jnp.float32)
    earlier = (lax.iota(jnp.int32, count) < place).astype(jnp.float32)
    return jnp.sum(values * earlier[:, None, None, None], 0), jnp.sum(values, 0)


def conv_kernel(pq, pk, pv, eq, ek, ev, tq, tk, tv, oq, ok, ov, state_ref, buf):
    rows = pq.shape[0]
    for proj, early, taps, out in ((pq, eq, tq, oq), (pk, ek, tk, ok), (pv, ev, tv, ov)):
        buf[0:PAD, :] = early[...].astype(jnp.float32)
        buf[PAD:, :] = proj[...].astype(jnp.float32)
        summed = jnp.zeros((rows, DH), jnp.float32)
        for offset in range(KW):
            summed = summed + taps[offset : offset + 1, :] * buf[pl.ds(PAD - offset, rows), :]
        out[...] = (summed * jax.nn.sigmoid(summed)).astype(out.dtype)
    state_ref[...] = lax.dot_general(
        ok[...], ov[...], (((0,), (0,)), ((), ())), preferred_element_type=jnp.float32
    )


def local_kernel(q_ref, k_ref, v_ref, out_ref):
    rows = q_ref.shape[0]
    block = min(BLOCK, rows)
    causal = lax.broadcasted_iota(jnp.int32, (block, block), 0) >= lax.broadcasted_iota(
        jnp.int32, (block, block), 1
    )
    inner = jnp.zeros((DH, DH), jnp.float32)
    for b in range(rows // block):
        span = pl.ds(b * block, block)
        query, key, value = q_ref[span, :], k_ref[span, :], v_ref[span, :]
        scores = lax.dot_general(
            query, key, (((1,), (1,)), ((), ())), preferred_element_type=jnp.float32
        )
        scores = jnp.where(causal, scores, 0.0).astype(jnp.bfloat16)
        part = jnp.dot(scores, value, preferred_element_type=jnp.float32)
        if b > 0:
            hi, lo = split_bf16(inner)
            part = part + jnp.dot(query, hi, preferred_element_type=jnp.float32)
            part = part + jnp.dot(query, lo, preferred_element_type=jnp.float32)
        out_ref[span, :] = part
        inner = inner + lax.dot_general(
            key, value, (((0,), (0,)), ((), ())), preferred_element_type=jnp.float32
        )


def out_kernel(q_ref, local_ref, prefix_ref, gain_ref, w_ref, out_ref, headed):
    for head in range(q_ref.shape[0]):
        hi, lo = split_bf16(prefix_ref[head])
        query = q_ref[head]
        attended = local_ref[head] + jnp.dot(query, hi, preferred_element_type=jnp.float32)
        attended = attended + jnp.dot(query, lo, preferred_element_type=jnp.float32)
        scaled = attended * lax.rsqrt(jnp.mean(attended * attended, -1, keepdims=True) + 1e-05)
        headed[:, head * DH : (head + 1) * DH] = (scaled * gain_ref[head]).astype(headed.dtype)
    out_ref[...] = jnp.dot(
        headed[...], w_ref[...], preferred_element_type=jnp.float32
    ).astype(out_ref.dtype)


def slab(shift, rows, cols):
    return pl.BlockSpec((None, rows, cols), lambda h: (h + shift, 0, 0))


def local(tokens, norm_gain, w_qkv, conv_weight, head_gain, w_out):
    rows, width = tokens.shape
    tokens_f = tokens.astype(jnp.float32)
    scale = lax.rsqrt(jnp.mean(tokens_f * tokens_f, -1, keepdims=True) + 1e-06)
    normed = (tokens_f * scale * norm_gain).astype(jnp.bfloat16)

    slabs = w_qkv.shape[1] // DH
    projected = jnp.einsum(
        "td,dje->jte", normed, w_qkv.reshape(width, slabs, DH), preferred_element_type=jnp.float32
    ).astype(jnp.bfloat16)

    seq_axes = ("sy", "sz")
    count = lax.axis_size("sy") * lax.axis_size("sz")
    earlier_rows = lax.ppermute(
        projected[:, rows - (KW - 1) :, :], seq_axes, [(i, i + 1) for i in range(count - 1)]
    )
    earlier_rows = jnp.pad(earlier_rows, ((0, 0), (PAD - (KW - 1), 0), (0, 0)))
    taps = jnp.pad(
        conv_weight.reshape(KW, slabs, DH).transpose(1, 0, 2), ((0, 0), (0, PAD - KW), (0, 0))
    )

    mixed_shape = jax.ShapeDtypeStruct((H, rows, DH), jnp.bfloat16)
    query, key, value, state = pl.pallas_call(
        conv_kernel,
        grid=(H,),
        in_specs=[slab(0, rows, DH), slab(H, rows, DH), slab(2 * H, rows, DH)]
        + [slab(0, PAD, DH), slab(H, PAD, DH), slab(2 * H, PAD, DH)]
        + [slab(0, PAD, DH), slab(H, PAD, DH), slab(2 * H, PAD, DH)],
        out_specs=[slab(0, rows, DH)] * 3 + [slab(0, DH, DH)],
        out_shape=[mixed_shape] * 3 + [jax.ShapeDtypeStruct((H, DH, DH), jnp.float32)],
        scratch_shapes=[pltpu.VMEM((rows + PAD, DH), jnp.float32)],
        cost_estimate=pl.CostEstimate(
            flops=H * (3 * rows * DH * 12 + 2 * rows * DH * DH),
            transcendentals=H * 3 * rows * DH,
            bytes_accessed=H * 3 * rows * DH * 4,
        ),
    )(projected, projected, projected, earlier_rows, earlier_rows, earlier_rows, taps, taps, taps)

    block = min(BLOCK, rows)
    local_part = pl.pallas_call(
        local_kernel,
        grid=(H,),
        in_specs=[slab(0, rows, DH)] * 3,
        out_specs=slab(0, rows, DH),
        out_shape=jax.ShapeDtypeStruct((H, rows, DH), jnp.float32),
        cost_estimate=pl.CostEstimate(
            flops=H * (4 * rows * block * DH + 6 * rows * DH * DH),
            transcendentals=0,
            bytes_accessed=H * rows * DH * 10,
        ),
    )(query, key, value)

    zbefore, row_total = gather_earlier(state.astype(jnp.bfloat16), "sz")
    ybefore, _ = gather_earlier(row_total.astype(jnp.bfloat16), "sy")
    prefix = ybefore + zbefore

    tile = min(256, rows)
    out = pl.pallas_call(
        out_kernel,
        grid=(rows // tile,),
        in_specs=[
            pl.BlockSpec((H, tile, DH), lambda i: (0, i, 0)),
            pl.BlockSpec((H, tile, DH), lambda i: (0, i, 0)),
            pl.BlockSpec((H, DH, DH), lambda i: (0, 0, 0)),
            pl.BlockSpec((H, 1, DH), lambda i: (0, 0, 0)),
            pl.BlockSpec((width, width), lambda i: (0, 0)),
        ],
        out_specs=pl.BlockSpec((tile, width), lambda i: (i, 0)),
        out_shape=jax.ShapeDtypeStruct((rows, width), jnp.bfloat16),
        scratch_shapes=[pltpu.VMEM((tile, H * DH), jnp.bfloat16)],
        cost_estimate=pl.CostEstimate(
            flops=H * 4 * rows * DH * DH + 2 * rows * width * width,
            transcendentals=H * rows,
            bytes_accessed=H * rows * DH * 6 + width * width * 2 + rows * width * 2,
        ),
    )(query, local_part, prefix, head_gain.reshape(H, 1, DH), w_out)
    return out


def solution(mesh):
    seq = mesh.shape["seq"]
    inner = 4 if seq % 4 == 0 else 1
    grid = Mesh(
        mesh.devices.reshape(mesh.shape["trace"], seq // inner, inner), ("trace", "sy", "sz")
    )
    rows = P(("trace", "sy", "sz"), None)
    placed = (rows, P(), P(), P(), P(), P())
    return jax.shard_map(local, mesh=grid, in_specs=placed, out_specs=rows, check_vma=False)
```

```python
import jax
import jax.numpy as jnp
from jax import lax
from jax.experimental import pallas as pl
from jax.experimental.pallas import tpu as pltpu
from jax.sharding import Mesh
from jax.sharding import PartitionSpec as P

H = 8
DH = 128
KW = 4
BLOCK = 512
PAD = 8


def split_bf16(x):
    hi = lax.reduce_precision(x, exponent_bits=8, mantissa_bits=7)
    return hi.astype(jnp.bfloat16), (x - hi).astype(jnp.bfloat16)


def earlier_states(state):
    count = lax.axis_size("sz")
    rows_count = lax.axis_size("sy")
    quarters = state.astype(jnp.bfloat16).reshape((count, -1) + state.shape[1:])
    mine = lax.all_to_all(quarters, "sz", 0, 0).astype(jnp.float32)
    before = [jnp.zeros_like(mine[0])]
    for z in range(1, count):
        before.append(before[-1] + mine[z - 1])
    row_total = before[-1] + mine[count - 1]
    totals = lax.all_to_all(
        jnp.broadcast_to(row_total.astype(jnp.bfloat16), (rows_count,) + row_total.shape), "sy", 0, 0
    ).astype(jnp.float32)
    earlier = (lax.iota(jnp.int32, rows_count) < lax.axis_index("sy")).astype(jnp.float32)
    rows_before = jnp.sum(totals * earlier[:, None, None, None], 0)
    finished = jnp.stack(before) + rows_before
    prefix = lax.all_to_all(finished.astype(jnp.bfloat16), "sz", 0, 0)
    return prefix.reshape(state.shape).astype(jnp.float32)


def conv_kernel(pq, pk, pv, eq, ek, ev, tq, tk, tv, oq, ok, ov, state_ref, buf):
    rows = pq.shape[0]
    for proj, early, taps, out in ((pq, eq, tq, oq), (pk, ek, tk, ok), (pv, ev, tv, ov)):
        buf[0:PAD, :] = early[...].astype(jnp.float32)
        buf[PAD:, :] = proj[...].astype(jnp.float32)
        summed = jnp.zeros((rows, DH), jnp.float32)
        for offset in range(KW):
            summed = summed + taps[offset : offset + 1, :] * buf[pl.ds(PAD - offset, rows), :]
        out[...] = (summed * jax.nn.sigmoid(summed)).astype(out.dtype)
    state_ref[...] = lax.dot_general(
        ok[...], ov[...], (((0,), (0,)), ((), ())), preferred_element_type=jnp.float32
    )


def local_kernel(q_ref, k_ref, v_ref, out_ref):
    rows = q_ref.shape[0]
    block = min(BLOCK, rows)
    causal = lax.broadcasted_iota(jnp.int32, (block, block), 0) >= lax.broadcasted_iota(
        jnp.int32, (block, block), 1
    )
    inner = jnp.zeros((DH, DH), jnp.float32)
    for b in range(rows // block):
        span = pl.ds(b * block, block)
        query, key, value = q_ref[span, :], k_ref[span, :], v_ref[span, :]
        scores = lax.dot_general(
            query, key, (((1,), (1,)), ((), ())), preferred_element_type=jnp.float32
        )
        scores = jnp.where(causal, scores, 0.0).astype(jnp.bfloat16)
        part = jnp.dot(scores, value, preferred_element_type=jnp.float32)
        if b > 0:
            hi, lo = split_bf16(inner)
            part = part + jnp.dot(query, hi, preferred_element_type=jnp.float32)
            part = part + jnp.dot(query, lo, preferred_element_type=jnp.float32)
        out_ref[span, :] = part
        inner = inner + lax.dot_general(
            key, value, (((0,), (0,)), ((), ())), preferred_element_type=jnp.float32
        )


def out_kernel(q_ref, local_ref, prefix_ref, gain_ref, w_ref, out_ref, headed):
    for head in range(q_ref.shape[0]):
        hi, lo = split_bf16(prefix_ref[head])
        query = q_ref[head]
        attended = local_ref[head] + jnp.dot(query, hi, preferred_element_type=jnp.float32)
        attended = attended + jnp.dot(query, lo, preferred_element_type=jnp.float32)
        scaled = attended * lax.rsqrt(jnp.mean(attended * attended, -1, keepdims=True) + 1e-05)
        headed[:, head * DH : (head + 1) * DH] = (scaled * gain_ref[head]).astype(headed.dtype)
    out_ref[...] = jnp.dot(
        headed[...], w_ref[...], preferred_element_type=jnp.float32
    ).astype(out_ref.dtype)


def slab(shift, rows, cols):
    return pl.BlockSpec((None, rows, cols), lambda h: (h + shift, 0, 0))


def local(tokens, norm_gain, w_qkv, conv_weight, head_gain, w_out):
    rows, width = tokens.shape
    tokens_f = tokens.astype(jnp.float32)
    scale = lax.rsqrt(jnp.mean(tokens_f * tokens_f, -1, keepdims=True) + 1e-06)
    normed = (tokens_f * scale * norm_gain).astype(jnp.bfloat16)

    slabs = w_qkv.shape[1] // DH
    projected = jnp.einsum(
        "td,dje->jte", normed, w_qkv.reshape(width, slabs, DH), preferred_element_type=jnp.float32
    ).astype(jnp.bfloat16)

    seq_axes = ("sy", "sz")
    count = lax.axis_size("sy") * lax.axis_size("sz")
    earlier_rows = lax.ppermute(
        projected[:, rows - (KW - 1) :, :], seq_axes, [(i, i + 1) for i in range(count - 1)]
    )
    earlier_rows = jnp.pad(earlier_rows, ((0, 0), (PAD - (KW - 1), 0), (0, 0)))
    taps = jnp.pad(
        conv_weight.reshape(KW, slabs, DH).transpose(1, 0, 2), ((0, 0), (0, PAD - KW), (0, 0))
    )

    mixed_shape = jax.ShapeDtypeStruct((H, rows, DH), jnp.bfloat16)
    query, key, value, state = pl.pallas_call(
        conv_kernel,
        grid=(H,),
        in_specs=[slab(0, rows, DH), slab(H, rows, DH), slab(2 * H, rows, DH)]
        + [slab(0, PAD, DH), slab(H, PAD, DH), slab(2 * H, PAD, DH)]
        + [slab(0, PAD, DH), slab(H, PAD, DH), slab(2 * H, PAD, DH)],
        out_specs=[slab(0, rows, DH)] * 3 + [slab(0, DH, DH)],
        out_shape=[mixed_shape] * 3 + [jax.ShapeDtypeStruct((H, DH, DH), jnp.float32)],
        scratch_shapes=[pltpu.VMEM((rows + PAD, DH), jnp.float32)],
        cost_estimate=pl.CostEstimate(
            flops=H * (3 * rows * DH * 12 + 2 * rows * DH * DH),
            transcendentals=H * 3 * rows * DH,
            bytes_accessed=H * 3 * rows * DH * 4,
        ),
    )(projected, projected, projected, earlier_rows, earlier_rows, earlier_rows, taps, taps, taps)

    block = min(BLOCK, rows)
    local_part = pl.pallas_call(
        local_kernel,
        grid=(H,),
        in_specs=[slab(0, rows, DH)] * 3,
        out_specs=slab(0, rows, DH),
        out_shape=jax.ShapeDtypeStruct((H, rows, DH), jnp.float32),
        cost_estimate=pl.CostEstimate(
            flops=H * (4 * rows * block * DH + 6 * rows * DH * DH),
            transcendentals=0,
            bytes_accessed=H * rows * DH * 10,
        ),
    )(query, key, value)

    prefix = earlier_states(state)

    tile = min(256, rows)
    out = pl.pallas_call(
        out_kernel,
        grid=(rows // tile,),
        in_specs=[
            pl.BlockSpec((H, tile, DH), lambda i: (0, i, 0)),
            pl.BlockSpec((H, tile, DH), lambda i: (0, i, 0)),
            pl.BlockSpec((H, DH, DH), lambda i: (0, 0, 0)),
            pl.BlockSpec((H, 1, DH), lambda i: (0, 0, 0)),
            pl.BlockSpec((width, width), lambda i: (0, 0)),
        ],
        out_specs=pl.BlockSpec((tile, width), lambda i: (i, 0)),
        out_shape=jax.ShapeDtypeStruct((rows, width), jnp.bfloat16),
        scratch_shapes=[pltpu.VMEM((tile, H * DH), jnp.bfloat16)],
        cost_estimate=pl.CostEstimate(
            flops=H * 4 * rows * DH * DH + 2 * rows * width * width,
            transcendentals=H * rows,
            bytes_accessed=H * rows * DH * 6 + width * width * 2 + rows * width * 2,
        ),
    )(query, local_part, prefix, head_gain.reshape(H, 1, DH), w_out)
    return out


def solution(mesh):
    seq = mesh.shape["seq"]
    inner = 4 if seq % 4 == 0 else 1
    grid = Mesh(
        mesh.devices.reshape(mesh.shape["trace"], seq // inner, inner), ("trace", "sy", "sz")
    )
    rows = P(("trace", "sy", "sz"), None)
    placed = (rows, P(), P(), P(), P(), P())
    return jax.shard_map(local, mesh=grid, in_specs=placed, out_specs=rows, check_vma=False)
```

```python
import jax
import jax.numpy as jnp
from jax import lax
from jax.experimental import pallas as pl
from jax.experimental.pallas import tpu as pltpu
from jax.sharding import Mesh
from jax.sharding import PartitionSpec as P

H = 8
DH = 128
KW = 4
BLOCK = 512
PAD = 8
LEAD = 16


def split_bf16(x):
    hi = lax.reduce_precision(x, exponent_bits=8, mantissa_bits=7)
    return hi.astype(jnp.bfloat16), (x - hi).astype(jnp.bfloat16)


def gather_earlier(x, axis):
    count = lax.axis_size(axis)
    place = lax.axis_index(axis)
    gathered = lax.all_to_all(jnp.broadcast_to(x, (count,) + x.shape), axis, 0, 0)
    values = gathered.astype(jnp.float32)
    earlier = (lax.iota(jnp.int32, count) < place).astype(jnp.float32)
    return jnp.sum(values * earlier[:, None, None, None], 0), jnp.sum(values, 0)


def conv_kernel(pq, pk, pv, tq, tk, tv, oq, ok, ov, state_ref, buf):
    rows = oq.shape[0]
    for proj, taps, out in ((pq, tq, oq), (pk, tk, ok), (pv, tv, ov)):
        buf[...] = proj[...].astype(jnp.float32)
        summed = jnp.zeros((rows, DH), jnp.float32)
        for offset in range(KW):
            summed = summed + taps[offset : offset + 1, :] * buf[pl.ds(LEAD - offset, rows), :]
        out[...] = (summed * jax.nn.sigmoid(summed)).astype(out.dtype)
    state_ref[...] = lax.dot_general(
        ok[...], ov[...], (((0,), (0,)), ((), ())), preferred_element_type=jnp.float32
    )


def local_kernel(q_ref, k_ref, v_ref, out_ref):
    rows = q_ref.shape[0]
    block = min(BLOCK, rows)
    causal = lax.broadcasted_iota(jnp.int32, (block, block), 0) >= lax.broadcasted_iota(
        jnp.int32, (block, block), 1
    )
    inner = jnp.zeros((DH, DH), jnp.float32)
    for b in range(rows // block):
        span = pl.ds(b * block, block)
        query, key, value = q_ref[span, :], k_ref[span, :], v_ref[span, :]
        scores = lax.dot_general(
            query, key, (((1,), (1,)), ((), ())), preferred_element_type=jnp.float32
        )
        scores = jnp.where(causal, scores, 0.0).astype(jnp.bfloat16)
        part = jnp.dot(scores, value, preferred_element_type=jnp.float32)
        if b > 0:
            hi, lo = split_bf16(inner)
            part = part + jnp.dot(query, hi, preferred_element_type=jnp.float32)
            part = part + jnp.dot(query, lo, preferred_element_type=jnp.float32)
        out_ref[span, :] = part
        inner = inner + lax.dot_general(
            key, value, (((0,), (0,)), ((), ())), preferred_element_type=jnp.float32
        )


def out_kernel(q_ref, local_ref, prefix_ref, gain_ref, w_ref, out_ref, headed):
    for head in range(q_ref.shape[0]):
        hi, lo = split_bf16(prefix_ref[head])
        query = q_ref[head]
        attended = local_ref[head] + jnp.dot(query, hi, preferred_element_type=jnp.float32)
        attended = attended + jnp.dot(query, lo, preferred_element_type=jnp.float32)
        scaled = attended * lax.rsqrt(jnp.mean(attended * attended, -1, keepdims=True) + 1e-05)
        headed[:, head * DH : (head + 1) * DH] = (scaled * gain_ref[head]).astype(headed.dtype)
    out_ref[...] = jnp.dot(
        headed[...], w_ref[...], preferred_element_type=jnp.float32
    ).astype(out_ref.dtype)


def slab(shift, rows, cols):
    return pl.BlockSpec((None, rows, cols), lambda h: (h + shift, 0, 0))


def local(tokens, norm_gain, w_qkv, conv_weight, head_gain, w_out):
    rows, width = tokens.shape
    seq_axes = ("sy", "sz")
    count = lax.axis_size("sy") * lax.axis_size("sz")
    earlier_tokens = lax.ppermute(
        tokens[rows - (KW - 1) :], seq_axes, [(i, i + 1) for i in range(count - 1)]
    )
    extended = jnp.concatenate(
        [jnp.zeros((LEAD - (KW - 1), width), tokens.dtype), earlier_tokens, tokens], 0
    )
    tokens_f = extended.astype(jnp.float32)
    scale = lax.rsqrt(jnp.mean(tokens_f * tokens_f, -1, keepdims=True) + 1e-06)
    normed = (tokens_f * scale * norm_gain).astype(jnp.bfloat16)

    slabs = w_qkv.shape[1] // DH
    projected = jnp.einsum(
        "td,dje->jte", normed, w_qkv.reshape(width, slabs, DH), preferred_element_type=jnp.float32
    ).astype(jnp.bfloat16)
    taps = jnp.pad(
        conv_weight.reshape(KW, slabs, DH).transpose(1, 0, 2), ((0, 0), (0, PAD - KW), (0, 0))
    )

    mixed_shape = jax.ShapeDtypeStruct((H, rows, DH), jnp.bfloat16)
    longer = rows + LEAD
    query, key, value, state = pl.pallas_call(
        conv_kernel,
        grid=(H,),
        in_specs=[slab(0, longer, DH), slab(H, longer, DH), slab(2 * H, longer, DH)]
        + [slab(0, PAD, DH), slab(H, PAD, DH), slab(2 * H, PAD, DH)],
        out_specs=[slab(0, rows, DH)] * 3 + [slab(0, DH, DH)],
        out_shape=[mixed_shape] * 3 + [jax.ShapeDtypeStruct((H, DH, DH), jnp.float32)],
        scratch_shapes=[pltpu.VMEM((longer, DH), jnp.float32)],
        cost_estimate=pl.CostEstimate(
            flops=H * (3 * rows * DH * 12 + 2 * rows * DH * DH),
            transcendentals=H * 3 * rows * DH,
            bytes_accessed=H * 3 * rows * DH * 4,
        ),
    )(projected, projected, projected, taps, taps, taps)

    block = min(BLOCK, rows)
    local_part = pl.pallas_call(
        local_kernel,
        grid=(H,),
        in_specs=[slab(0, rows, DH)] * 3,
        out_specs=slab(0, rows, DH),
        out_shape=jax.ShapeDtypeStruct((H, rows, DH), jnp.float32),
        cost_estimate=pl.CostEstimate(
            flops=H * (4 * rows * block * DH + 6 * rows * DH * DH),
            transcendentals=0,
            bytes_accessed=H * rows * DH * 10,
        ),
    )(query, key, value)

    zbefore, row_total = gather_earlier(state.astype(jnp.bfloat16), "sz")
    ybefore, _ = gather_earlier(row_total.astype(jnp.bfloat16), "sy")
    prefix = ybefore + zbefore

    tile = min(256, rows)
    out = pl.pallas_call(
        out_kernel,
        grid=(rows // tile,),
        in_specs=[
            pl.BlockSpec((H, tile, DH), lambda i: (0, i, 0)),
            pl.BlockSpec((H, tile, DH), lambda i: (0, i, 0)),
            pl.BlockSpec((H, DH, DH), lambda i: (0, 0, 0)),
            pl.BlockSpec((H, 1, DH), lambda i: (0, 0, 0)),
            pl.BlockSpec((width, width), lambda i: (0, 0)),
        ],
        out_specs=pl.BlockSpec((tile, width), lambda i: (i, 0)),
        out_shape=jax.ShapeDtypeStruct((rows, width), jnp.bfloat16),
        scratch_shapes=[pltpu.VMEM((tile, H * DH), jnp.bfloat16)],
        cost_estimate=pl.CostEstimate(
            flops=H * 4 * rows * DH * DH + 2 * rows * width * width,
            transcendentals=H * rows,
            bytes_accessed=H * rows * DH * 6 + width * width * 2 + rows * width * 2,
        ),
    )(query, local_part, prefix, head_gain.reshape(H, 1, DH), w_out)
    return out


def solution(mesh):
    seq = mesh.shape["seq"]
    inner = 4 if seq % 4 == 0 else 1
    grid = Mesh(
        mesh.devices.reshape(mesh.shape["trace"], seq // inner, inner), ("trace", "sy", "sz")
    )
    rows = P(("trace", "sy", "sz"), None)
    placed = (rows, P(), P(), P(), P(), P())
    return jax.shard_map(local, mesh=grid, in_specs=placed, out_specs=rows, check_vma=False)
```

```python
import jax
import jax.numpy as jnp
from jax import lax
from jax.experimental import pallas as pl
from jax.experimental.pallas import tpu as pltpu
from jax.sharding import Mesh
from jax.sharding import PartitionSpec as P

H = 8
DH = 128
KW = 4
BLOCK = 512
PAD = 8


def split_bf16(x):
    hi = lax.reduce_precision(x, exponent_bits=8, mantissa_bits=7)
    return hi.astype(jnp.bfloat16), (x - hi).astype(jnp.bfloat16)


def gather_earlier(x, axis):
    count = lax.axis_size(axis)
    place = lax.axis_index(axis)
    gathered = lax.all_to_all(jnp.broadcast_to(x, (count,) + x.shape), axis, 0, 0)
    values = gathered.astype(jnp.float32)
    earlier = (lax.iota(jnp.int32, count) < place).astype(jnp.float32)
    return jnp.sum(values * earlier[:, None, None, None], 0), jnp.sum(values, 0)


def conv_kernel(pq, pk, pv, eq, ek, ev, tq, tk, tv, oq, ok, ov, state_ref, buf):
    rows = pq.shape[0]
    for proj, early, taps, out in ((pq, eq, tq, oq), (pk, ek, tk, ok), (pv, ev, tv, ov)):
        buf[PAD - (KW - 1) : PAD, :] = early[...].astype(jnp.float32)
        buf[PAD:, :] = proj[...].astype(jnp.float32)
        summed = jnp.zeros((rows, DH), jnp.float32)
        for offset in range(KW):
            summed = summed + taps[offset : offset + 1, :] * buf[pl.ds(PAD - offset, rows), :]
        out[...] = (summed * (0.5 + 0.5 * jnp.tanh(0.5 * summed))).astype(out.dtype)
    state_ref[...] = lax.dot_general(
        ok[...], ov[...], (((0,), (0,)), ((), ())), preferred_element_type=jnp.float32
    ).astype(state_ref.dtype)


def local_kernel(q_ref, k_ref, v_ref, out_ref):
    rows = q_ref.shape[0]
    block = min(BLOCK, rows)
    causal = lax.broadcasted_iota(jnp.int32, (block, block), 0) >= lax.broadcasted_iota(
        jnp.int32, (block, block), 1
    )
    inner = jnp.zeros((DH, DH), jnp.float32)
    for b in range(rows // block):
        span = pl.ds(b * block, block)
        query, key, value = q_ref[span, :], k_ref[span, :], v_ref[span, :]
        scores = lax.dot_general(
            query, key, (((1,), (1,)), ((), ())), preferred_element_type=jnp.float32
        )
        scores = jnp.where(causal, scores, 0.0).astype(jnp.bfloat16)
        part = jnp.dot(scores, value, preferred_element_type=jnp.float32)
        if b > 0:
            hi, lo = split_bf16(inner)
            part = part + jnp.dot(query, hi, preferred_element_type=jnp.float32)
            part = part + jnp.dot(query, lo, preferred_element_type=jnp.float32)
        out_ref[span, :] = part
        inner = inner + lax.dot_general(
            key, value, (((0,), (0,)), ((), ())), preferred_element_type=jnp.float32
        )


def out_kernel(q_ref, local_ref, prefix_ref, gain_ref, w_ref, out_ref, headed):
    for head in range(q_ref.shape[0]):
        hi, lo = split_bf16(prefix_ref[head])
        query = q_ref[head]
        attended = local_ref[head] + jnp.dot(query, hi, preferred_element_type=jnp.float32)
        attended = attended + jnp.dot(query, lo, preferred_element_type=jnp.float32)
        scaled = attended * lax.rsqrt(jnp.mean(attended * attended, -1, keepdims=True) + 1e-05)
        headed[:, head * DH : (head + 1) * DH] = (scaled * gain_ref[head]).astype(headed.dtype)
    out_ref[...] = jnp.dot(
        headed[...], w_ref[...], preferred_element_type=jnp.float32
    ).astype(out_ref.dtype)


def slab(shift, rows, cols):
    return pl.BlockSpec((None, rows, cols), lambda h: (h + shift, 0, 0))


def local(tokens, norm_gain, w_qkv, conv_weight, head_gain, w_out):
    rows, width = tokens.shape
    tokens_f = tokens.astype(jnp.float32)
    scale = lax.rsqrt(jnp.mean(tokens_f * tokens_f, -1, keepdims=True) + 1e-06)
    normed = (tokens_f * scale * norm_gain).astype(jnp.bfloat16)

    slabs = w_qkv.shape[1] // DH
    projected = jnp.einsum(
        "td,dje->jte", normed, w_qkv.reshape(width, slabs, DH), preferred_element_type=jnp.float32
    ).astype(jnp.bfloat16)

    seq_axes = ("sy", "sz")
    count = lax.axis_size("sy") * lax.axis_size("sz")
    earlier_rows = lax.ppermute(
        projected[:, rows - (KW - 1) :, :], seq_axes, [(i, i + 1) for i in range(count - 1)]
    )
    taps = conv_weight.reshape(KW, slabs, DH).transpose(1, 0, 2)

    mixed_shape = jax.ShapeDtypeStruct((H, rows, DH), jnp.bfloat16)
    query, key, value, state = pl.pallas_call(
        conv_kernel,
        grid=(H,),
        in_specs=[slab(0, rows, DH), slab(H, rows, DH), slab(2 * H, rows, DH)]
        + [slab(0, KW - 1, DH), slab(H, KW - 1, DH), slab(2 * H, KW - 1, DH)]
        + [slab(0, KW, DH), slab(H, KW, DH), slab(2 * H, KW, DH)],
        out_specs=[slab(0, rows, DH)] * 3 + [slab(0, DH, DH)],
        out_shape=[mixed_shape] * 3 + [jax.ShapeDtypeStruct((H, DH, DH), jnp.bfloat16)],
        scratch_shapes=[pltpu.VMEM((rows + PAD, DH), jnp.float32)],
        cost_estimate=pl.CostEstimate(
            flops=H * (3 * rows * DH * 12 + 2 * rows * DH * DH),
            transcendentals=H * 3 * rows * DH,
            bytes_accessed=H * 3 * rows * DH * 4,
        ),
    )(projected, projected, projected, earlier_rows, earlier_rows, earlier_rows, taps, taps, taps)

    block = min(BLOCK, rows)
    local_part = pl.pallas_call(
        local_kernel,
        grid=(H,),
        in_specs=[slab(0, rows, DH)] * 3,
        out_specs=slab(0, rows, DH),
        out_shape=jax.ShapeDtypeStruct((H, rows, DH), jnp.float32),
        cost_estimate=pl.CostEstimate(
            flops=H * (4 * rows * block * DH + 6 * rows * DH * DH),
            transcendentals=0,
            bytes_accessed=H * rows * DH * 10,
        ),
    )(query, key, value)

    zbefore, row_total = gather_earlier(state, "sz")
    ybefore, _ = gather_earlier(row_total.astype(jnp.bfloat16), "sy")
    prefix = ybefore + zbefore

    tile = min(256, rows)
    out = pl.pallas_call(
        out_kernel,
        grid=(rows // tile,),
        in_specs=[
            pl.BlockSpec((H, tile, DH), lambda i: (0, i, 0)),
            pl.BlockSpec((H, tile, DH), lambda i: (0, i, 0)),
            pl.BlockSpec((H, DH, DH), lambda i: (0, 0, 0)),
            pl.BlockSpec((H, 1, DH), lambda i: (0, 0, 0)),
            pl.BlockSpec((width, width), lambda i: (0, 0)),
        ],
        out_specs=pl.BlockSpec((tile, width), lambda i: (i, 0)),
        out_shape=jax.ShapeDtypeStruct((rows, width), jnp.bfloat16),
        scratch_shapes=[pltpu.VMEM((tile, H * DH), jnp.bfloat16)],
        cost_estimate=pl.CostEstimate(
            flops=H * 4 * rows * DH * DH + 2 * rows * width * width,
            transcendentals=H * rows,
            bytes_accessed=H * rows * DH * 6 + width * width * 2 + rows * width * 2,
        ),
    )(query, local_part, prefix, head_gain.reshape(H, 1, DH), w_out)
    return out


def solution(mesh):
    seq = mesh.shape["seq"]
    inner = 4 if seq % 4 == 0 else 1
    grid = Mesh(
        mesh.devices.reshape(mesh.shape["trace"], seq // inner, inner), ("trace", "sy", "sz")
    )
    rows = P(("trace", "sy", "sz"), None)
    placed = (rows, P(), P(), P(), P(), P())
    return jax.shard_map(local, mesh=grid, in_specs=placed, out_specs=rows, check_vma=False)
```

```python
import jax
import jax.numpy as jnp
from jax import lax
from jax.experimental import pallas as pl
from jax.experimental.pallas import tpu as pltpu
from jax.sharding import Mesh
from jax.sharding import PartitionSpec as P

H = 8
DH = 128
KW = 4
BLOCK = 512
PAD = 8


def split_bf16(x):
    hi = lax.reduce_precision(x, exponent_bits=8, mantissa_bits=7)
    return hi.astype(jnp.bfloat16), (x - hi).astype(jnp.bfloat16)


def earlier_states(state):
    count = lax.axis_size("sz")
    rows_count = lax.axis_size("sy")
    quarters = state.astype(jnp.bfloat16).reshape((count, -1) + state.shape[1:])
    mine = lax.all_to_all(quarters, "sz", 0, 0).astype(jnp.float32)
    before = [jnp.zeros_like(mine[0])]
    for z in range(1, count):
        before.append(before[-1] + mine[z - 1])
    row_total = before[-1] + mine[count - 1]
    row = lax.axis_index("sy")
    later_row = (row < lax.iota(jnp.int32, rows_count)).astype(jnp.float32)
    same_row = (row == lax.iota(jnp.int32, rows_count)).astype(jnp.float32)
    messages = (
        later_row[:, None, None, None, None] * row_total[None, None]
        + same_row[:, None, None, None, None] * jnp.stack(before)[None]
    )
    received = lax.all_to_all(
        messages.astype(jnp.bfloat16).reshape((rows_count * count,) + row_total.shape),
        ("sy", "sz"),
        0,
        0,
    )
    received = received.reshape((rows_count, count) + row_total.shape).astype(jnp.float32)
    return jnp.sum(received, 0).reshape(state.shape)


def conv_kernel(pq, pk, pv, eq, ek, ev, tq, tk, tv, oq, ok, ov, state_ref, buf):
    rows = pq.shape[0]
    for proj, early, taps, out in ((pq, eq, tq, oq), (pk, ek, tk, ok), (pv, ev, tv, ov)):
        buf[0:PAD, :] = early[...].astype(jnp.float32)
        buf[PAD:, :] = proj[...].astype(jnp.float32)
        summed = jnp.zeros((rows, DH), jnp.float32)
        for offset in range(KW):
            summed = summed + taps[offset : offset + 1, :] * buf[pl.ds(PAD - offset, rows), :]
        out[...] = (summed * jax.nn.sigmoid(summed)).astype(out.dtype)
    state_ref[...] = lax.dot_general(
        ok[...], ov[...], (((0,), (0,)), ((), ())), preferred_element_type=jnp.float32
    )


def local_kernel(q_ref, k_ref, v_ref, out_ref):
    rows = q_ref.shape[0]
    block = min(BLOCK, rows)
    causal = lax.broadcasted_iota(jnp.int32, (block, block), 0) >= lax.broadcasted_iota(
        jnp.int32, (block, block), 1
    )
    inner = jnp.zeros((DH, DH), jnp.float32)
    for b in range(rows // block):
        span = pl.ds(b * block, block)
        query, key, value = q_ref[span, :], k_ref[span, :], v_ref[span, :]
        scores = lax.dot_general(
            query, key, (((1,), (1,)), ((), ())), preferred_element_type=jnp.float32
        )
        scores = jnp.where(causal, scores, 0.0).astype(jnp.bfloat16)
        part = jnp.dot(scores, value, preferred_element_type=jnp.float32)
        if b > 0:
            hi, lo = split_bf16(inner)
            part = part + jnp.dot(query, hi, preferred_element_type=jnp.float32)
            part = part + jnp.dot(query, lo, preferred_element_type=jnp.float32)
        out_ref[span, :] = part
        inner = inner + lax.dot_general(
            key, value, (((0,), (0,)), ((), ())), preferred_element_type=jnp.float32
        )


def out_kernel(q_ref, local_ref, prefix_ref, gain_ref, w_ref, out_ref, headed):
    for head in range(q_ref.shape[0]):
        hi, lo = split_bf16(prefix_ref[head])
        query = q_ref[head]
        attended = local_ref[head] + jnp.dot(query, hi, preferred_element_type=jnp.float32)
        attended = attended + jnp.dot(query, lo, preferred_element_type=jnp.float32)
        scaled = attended * lax.rsqrt(jnp.mean(attended * attended, -1, keepdims=True) + 1e-05)
        headed[:, head * DH : (head + 1) * DH] = (scaled * gain_ref[head]).astype(headed.dtype)
    out_ref[...] = jnp.dot(
        headed[...], w_ref[...], preferred_element_type=jnp.float32
    ).astype(out_ref.dtype)


def slab(shift, rows, cols):
    return pl.BlockSpec((None, rows, cols), lambda h: (h + shift, 0, 0))


def local(tokens, norm_gain, w_qkv, conv_weight, head_gain, w_out):
    rows, width = tokens.shape
    tokens_f = tokens.astype(jnp.float32)
    scale = lax.rsqrt(jnp.mean(tokens_f * tokens_f, -1, keepdims=True) + 1e-06)
    normed = (tokens_f * scale * norm_gain).astype(jnp.bfloat16)

    slabs = w_qkv.shape[1] // DH
    projected = jnp.einsum(
        "td,dje->jte", normed, w_qkv.reshape(width, slabs, DH), preferred_element_type=jnp.float32
    ).astype(jnp.bfloat16)

    seq_axes = ("sy", "sz")
    count = lax.axis_size("sy") * lax.axis_size("sz")
    earlier_rows = lax.ppermute(
        projected[:, rows - (KW - 1) :, :], seq_axes, [(i, i + 1) for i in range(count - 1)]
    )
    earlier_rows = jnp.pad(earlier_rows, ((0, 0), (PAD - (KW - 1), 0), (0, 0)))
    taps = jnp.pad(
        conv_weight.reshape(KW, slabs, DH).transpose(1, 0, 2), ((0, 0), (0, PAD - KW), (0, 0))
    )

    mixed_shape = jax.ShapeDtypeStruct((H, rows, DH), jnp.bfloat16)
    query, key, value, state = pl.pallas_call(
        conv_kernel,
        grid=(H,),
        in_specs=[slab(0, rows, DH), slab(H, rows, DH), slab(2 * H, rows, DH)]
        + [slab(0, PAD, DH), slab(H, PAD, DH), slab(2 * H, PAD, DH)]
        + [slab(0, PAD, DH), slab(H, PAD, DH), slab(2 * H, PAD, DH)],
        out_specs=[slab(0, rows, DH)] * 3 + [slab(0, DH, DH)],
        out_shape=[mixed_shape] * 3 + [jax.ShapeDtypeStruct((H, DH, DH), jnp.float32)],
        scratch_shapes=[pltpu.VMEM((rows + PAD, DH), jnp.float32)],
        cost_estimate=pl.CostEstimate(
            flops=H * (3 * rows * DH * 12 + 2 * rows * DH * DH),
            transcendentals=H * 3 * rows * DH,
            bytes_accessed=H * 3 * rows * DH * 4,
        ),
    )(projected, projected, projected, earlier_rows, earlier_rows, earlier_rows, taps, taps, taps)

    block = min(BLOCK, rows)
    local_part = pl.pallas_call(
        local_kernel,
        grid=(H,),
        in_specs=[slab(0, rows, DH)] * 3,
        out_specs=slab(0, rows, DH),
        out_shape=jax.ShapeDtypeStruct((H, rows, DH), jnp.float32),
        cost_estimate=pl.CostEstimate(
            flops=H * (4 * rows * block * DH + 6 * rows * DH * DH),
            transcendentals=0,
            bytes_accessed=H * rows * DH * 10,
        ),
    )(query, key, value)

    prefix = earlier_states(state)

    tile = min(256, rows)
    out = pl.pallas_call(
        out_kernel,
        grid=(rows // tile,),
        in_specs=[
            pl.BlockSpec((H, tile, DH), lambda i: (0, i, 0)),
            pl.BlockSpec((H, tile, DH), lambda i: (0, i, 0)),
            pl.BlockSpec((H, DH, DH), lambda i: (0, 0, 0)),
            pl.BlockSpec((H, 1, DH), lambda i: (0, 0, 0)),
            pl.BlockSpec((width, width), lambda i: (0, 0)),
        ],
        out_specs=pl.BlockSpec((tile, width), lambda i: (i, 0)),
        out_shape=jax.ShapeDtypeStruct((rows, width), jnp.bfloat16),
        scratch_shapes=[pltpu.VMEM((tile, H * DH), jnp.bfloat16)],
        cost_estimate=pl.CostEstimate(
            flops=H * 4 * rows * DH * DH + 2 * rows * width * width,
            transcendentals=H * rows,
            bytes_accessed=H * rows * DH * 6 + width * width * 2 + rows * width * 2,
        ),
    )(query, local_part, prefix, head_gain.reshape(H, 1, DH), w_out)
    return out


def solution(mesh):
    seq = mesh.shape["seq"]
    inner = 4 if seq % 4 == 0 else 1
    grid = Mesh(
        mesh.devices.reshape(mesh.shape["trace"], seq // inner, inner), ("trace", "sy", "sz")
    )
    rows = P(("trace", "sy", "sz"), None)
    placed = (rows, P(), P(), P(), P(), P())
    return jax.shard_map(local, mesh=grid, in_specs=placed, out_specs=rows, check_vma=False)
```

```python
import functools

import jax
import jax.numpy as jnp
from jax import lax
from jax.experimental import pallas as pl
from jax.experimental.pallas import tpu as pltpu
from jax.sharding import Mesh
from jax.sharding import PartitionSpec as P

H = 8
DH = 128
KW = 4
BLOCK = 512
PAD = 8


def split_bf16(x):
    hi = lax.reduce_precision(x, exponent_bits=8, mantissa_bits=7)
    return hi.astype(jnp.bfloat16), (x - hi).astype(jnp.bfloat16)


def earlier_states(state, before_second=None):
    count = lax.axis_size("sz")
    rows_count = lax.axis_size("sy")
    quarters = state.astype(jnp.bfloat16).reshape((count, -1) + state.shape[1:])
    mine = lax.all_to_all(quarters, "sz", 0, 0).astype(jnp.float32)
    before = [jnp.zeros_like(mine[0])]
    for z in range(1, count):
        before.append(before[-1] + mine[z - 1])
    row_total = before[-1] + mine[count - 1]
    row = lax.axis_index("sy")
    later_row = (row < lax.iota(jnp.int32, rows_count)).astype(jnp.float32)
    same_row = (row == lax.iota(jnp.int32, rows_count)).astype(jnp.float32)
    messages = (
        later_row[:, None, None, None, None] * row_total[None, None]
        + same_row[:, None, None, None, None] * jnp.stack(before)[None]
    )
    messages = messages.astype(jnp.bfloat16)
    if before_second is not None:
        messages, before_second = lax.optimization_barrier((messages, before_second()))
    received = lax.all_to_all(
        messages.reshape((rows_count * count,) + row_total.shape),
        ("sy", "sz"),
        0,
        0,
    )
    received = received.reshape((rows_count, count) + row_total.shape).astype(jnp.float32)
    return jnp.sum(received, 0).reshape(state.shape), before_second


def conv_kernel(count, with_state, *refs):
    projs, earlies, tapss = refs[:count], refs[count : 2 * count], refs[2 * count : 3 * count]
    outs, buf = refs[3 * count : 4 * count], refs[-1]
    rows = projs[0].shape[0]
    for proj, early, taps, out in zip(projs, earlies, tapss, outs):
        buf[0:PAD, :] = early[...].astype(jnp.float32)
        buf[PAD:, :] = proj[...].astype(jnp.float32)
        summed = jnp.zeros((rows, DH), jnp.float32)
        for offset in range(KW):
            summed = summed + taps[offset : offset + 1, :] * buf[pl.ds(PAD - offset, rows), :]
        out[...] = (summed * jax.nn.sigmoid(summed)).astype(out.dtype)
    if with_state:
        refs[4 * count][...] = lax.dot_general(
            outs[0][...], outs[1][...], (((0,), (0,)), ((), ())), preferred_element_type=jnp.float32
        )


def conv_call(projected, earlier, taps, shifts, base, with_state):
    count = len(shifts)
    rows = projected.shape[1]
    mixed = jax.ShapeDtypeStruct((H, rows, DH), jnp.bfloat16)
    out_specs = [slab(0, rows, DH)] * count
    out_shape = [mixed] * count
    if with_state:
        out_specs.append(slab(0, DH, DH))
        out_shape.append(jax.ShapeDtypeStruct((H, DH, DH), jnp.float32))
    return pl.pallas_call(
        functools.partial(conv_kernel, count, with_state),
        grid=(H,),
        in_specs=[slab(shift, rows, DH) for shift in shifts]
        + [slab(base + shift, PAD, DH) for shift in shifts] * 2,
        out_specs=out_specs,
        out_shape=out_shape,
        scratch_shapes=[pltpu.VMEM((rows + PAD, DH), jnp.float32)],
        cost_estimate=pl.CostEstimate(
            flops=H * count * rows * DH * (12 + 2 * DH),
            transcendentals=H * count * rows * DH,
            bytes_accessed=H * count * rows * DH * 4,
        ),
    )(*([projected] * count + [earlier] * count + [taps] * count))


def local_kernel(q_ref, k_ref, v_ref, out_ref):
    rows = q_ref.shape[0]
    block = min(BLOCK, rows)
    causal = lax.broadcasted_iota(jnp.int32, (block, block), 0) >= lax.broadcasted_iota(
        jnp.int32, (block, block), 1
    )
    inner = jnp.zeros((DH, DH), jnp.float32)
    for b in range(rows // block):
        span = pl.ds(b * block, block)
        query, key, value = q_ref[span, :], k_ref[span, :], v_ref[span, :]
        scores = lax.dot_general(
            query, key, (((1,), (1,)), ((), ())), preferred_element_type=jnp.float32
        )
        scores = jnp.where(causal, scores, 0.0).astype(jnp.bfloat16)
        part = jnp.dot(scores, value, preferred_element_type=jnp.float32)
        if b > 0:
            hi, lo = split_bf16(inner)
            part = part + jnp.dot(query, hi, preferred_element_type=jnp.float32)
            part = part + jnp.dot(query, lo, preferred_element_type=jnp.float32)
        out_ref[span, :] = part
        inner = inner + lax.dot_general(
            key, value, (((0,), (0,)), ((), ())), preferred_element_type=jnp.float32
        )


def out_kernel(q_ref, local_ref, prefix_ref, gain_ref, w_ref, out_ref, headed):
    for head in range(q_ref.shape[0]):
        hi, lo = split_bf16(prefix_ref[head])
        query = q_ref[head]
        attended = local_ref[head] + jnp.dot(query, hi, preferred_element_type=jnp.float32)
        attended = attended + jnp.dot(query, lo, preferred_element_type=jnp.float32)
        scaled = attended * lax.rsqrt(jnp.mean(attended * attended, -1, keepdims=True) + 1e-05)
        headed[:, head * DH : (head + 1) * DH] = (scaled * gain_ref[head]).astype(headed.dtype)
    out_ref[...] = jnp.dot(
        headed[...], w_ref[...], preferred_element_type=jnp.float32
    ).astype(out_ref.dtype)


def slab(shift, rows, cols):
    return pl.BlockSpec((None, rows, cols), lambda h: (h + shift, 0, 0))


def local(tokens, norm_gain, w_qkv, conv_weight, head_gain, w_out):
    rows, width = tokens.shape
    tokens_f = tokens.astype(jnp.float32)
    scale = lax.rsqrt(jnp.mean(tokens_f * tokens_f, -1, keepdims=True) + 1e-06)
    normed = (tokens_f * scale * norm_gain).astype(jnp.bfloat16)

    slabs = w_qkv.shape[1] // DH
    projected = jnp.einsum(
        "td,dje->jte", normed, w_qkv.reshape(width, slabs, DH), preferred_element_type=jnp.float32
    ).astype(jnp.bfloat16)

    seq_axes = ("sy", "sz")
    count = lax.axis_size("sy") * lax.axis_size("sz")
    earlier_rows = lax.ppermute(
        projected[:, rows - (KW - 1) :, :], seq_axes, [(i, i + 1) for i in range(count - 1)]
    )
    earlier_rows = jnp.pad(earlier_rows, ((0, 0), (PAD - (KW - 1), 0), (0, 0)))
    taps = jnp.pad(
        conv_weight.reshape(KW, slabs, DH).transpose(1, 0, 2), ((0, 0), (0, PAD - KW), (0, 0))
    )

    key, value, state = conv_call(projected, earlier_rows, taps, (H, 2 * H), 0, True)
    prefix, (query,) = earlier_states(
        state, lambda: conv_call(projected, earlier_rows, taps, (0,), 0, False)
    )

    block = min(BLOCK, rows)
    local_part = pl.pallas_call(
        local_kernel,
        grid=(H,),
        in_specs=[slab(0, rows, DH)] * 3,
        out_specs=slab(0, rows, DH),
        out_shape=jax.ShapeDtypeStruct((H, rows, DH), jnp.float32),
        cost_estimate=pl.CostEstimate(
            flops=H * (4 * rows * block * DH + 6 * rows * DH * DH),
            transcendentals=0,
            bytes_accessed=H * rows * DH * 10,
        ),
    )(query, key, value)

    tile = min(256, rows)
    out = pl.pallas_call(
        out_kernel,
        grid=(rows // tile,),
        in_specs=[
            pl.BlockSpec((H, tile, DH), lambda i: (0, i, 0)),
            pl.BlockSpec((H, tile, DH), lambda i: (0, i, 0)),
            pl.BlockSpec((H, DH, DH), lambda i: (0, 0, 0)),
            pl.BlockSpec((H, 1, DH), lambda i: (0, 0, 0)),
            pl.BlockSpec((width, width), lambda i: (0, 0)),
        ],
        out_specs=pl.BlockSpec((tile, width), lambda i: (i, 0)),
        out_shape=jax.ShapeDtypeStruct((rows, width), jnp.bfloat16),
        scratch_shapes=[pltpu.VMEM((tile, H * DH), jnp.bfloat16)],
        cost_estimate=pl.CostEstimate(
            flops=H * 4 * rows * DH * DH + 2 * rows * width * width,
            transcendentals=H * rows,
            bytes_accessed=H * rows * DH * 6 + width * width * 2 + rows * width * 2,
        ),
    )(query, local_part, prefix, head_gain.reshape(H, 1, DH), w_out)
    return out


def solution(mesh):
    seq = mesh.shape["seq"]
    inner = 4 if seq % 4 == 0 else 1
    grid = Mesh(
        mesh.devices.reshape(mesh.shape["trace"], seq // inner, inner), ("trace", "sy", "sz")
    )
    rows = P(("trace", "sy", "sz"), None)
    placed = (rows, P(), P(), P(), P(), P())
    return jax.shard_map(local, mesh=grid, in_specs=placed, out_specs=rows, check_vma=False)
```

```python
import jax
import jax.numpy as jnp
from jax import lax
from jax.experimental import pallas as pl
from jax.experimental.pallas import tpu as pltpu
from jax.sharding import Mesh
from jax.sharding import PartitionSpec as P

H = 8
DH = 128
KW = 4
BLOCK = 512
PAD = 8


def split_bf16(x):
    hi = lax.reduce_precision(x, exponent_bits=8, mantissa_bits=7)
    return hi.astype(jnp.bfloat16), (x - hi).astype(jnp.bfloat16)


def earlier_states(state):
    count = lax.axis_size("sz")
    rows_count = lax.axis_size("sy")
    quarters = state.astype(jnp.bfloat16).reshape((count, -1) + state.shape[1:])
    mine = lax.all_to_all(quarters, "sz", 0, 0).astype(jnp.float32)
    before = [jnp.zeros_like(mine[0])]
    for z in range(1, count):
        before.append(before[-1] + mine[z - 1])
    row_total = before[-1] + mine[count - 1]
    row = lax.axis_index("sy")
    later_row = (row < lax.iota(jnp.int32, rows_count)).astype(jnp.float32)
    same_row = (row == lax.iota(jnp.int32, rows_count)).astype(jnp.float32)
    messages = (
        later_row[:, None, None, None, None] * row_total[None, None]
        + same_row[:, None, None, None, None] * jnp.stack(before)[None]
    )
    received = lax.all_to_all(
        messages.astype(jnp.bfloat16).reshape((rows_count * count,) + row_total.shape),
        ("sy", "sz"),
        0,
        0,
    )
    received = received.reshape((rows_count, count) + row_total.shape).astype(jnp.float32)
    return jnp.sum(received, 0).reshape(state.shape)


def conv_kernel(pq, pk, pv, eq, ek, ev, tq, tk, tv, oq, ok, ov, state_ref, buf):
    rows = pq.shape[0]
    for proj, early, taps, out in ((pq, eq, tq, oq), (pk, ek, tk, ok), (pv, ev, tv, ov)):
        buf[PAD - (KW - 1) : PAD, :] = early[...].astype(jnp.float32)
        buf[PAD:, :] = proj[...].astype(jnp.float32)
        summed = jnp.zeros((rows, DH), jnp.float32)
        for offset in range(KW):
            summed = summed + taps[offset : offset + 1, :] * buf[pl.ds(PAD - offset, rows), :]
        out[...] = (summed * jax.nn.sigmoid(summed)).astype(out.dtype)
    state_ref[...] = lax.dot_general(
        ok[...], ov[...], (((0,), (0,)), ((), ())), preferred_element_type=jnp.float32
    ).astype(state_ref.dtype)


def local_kernel(q_ref, k_ref, v_ref, out_ref):
    rows = q_ref.shape[0]
    block = min(BLOCK, rows)
    causal = lax.broadcasted_iota(jnp.int32, (block, block), 0) >= lax.broadcasted_iota(
        jnp.int32, (block, block), 1
    )
    inner = jnp.zeros((DH, DH), jnp.float32)
    for b in range(rows // block):
        span = pl.ds(b * block, block)
        query, key, value = q_ref[span, :], k_ref[span, :], v_ref[span, :]
        scores = lax.dot_general(
            query, key, (((1,), (1,)), ((), ())), preferred_element_type=jnp.float32
        )
        scores = jnp.where(causal, scores, 0.0).astype(jnp.bfloat16)
        part = jnp.dot(scores, value, preferred_element_type=jnp.float32)
        if b > 0:
            hi, lo = split_bf16(inner)
            part = part + jnp.dot(query, hi, preferred_element_type=jnp.float32)
            part = part + jnp.dot(query, lo, preferred_element_type=jnp.float32)
        out_ref[span, :] = part
        inner = inner + lax.dot_general(
            key, value, (((0,), (0,)), ((), ())), preferred_element_type=jnp.float32
        )


def out_kernel(q_ref, local_ref, prefix_ref, gain_ref, w_ref, out_ref, headed):
    for head in range(q_ref.shape[0]):
        hi, lo = split_bf16(prefix_ref[head])
        query = q_ref[head]
        attended = local_ref[head] + jnp.dot(query, hi, preferred_element_type=jnp.float32)
        attended = attended + jnp.dot(query, lo, preferred_element_type=jnp.float32)
        scaled = attended * lax.rsqrt(jnp.mean(attended * attended, -1, keepdims=True) + 1e-05)
        headed[:, head * DH : (head + 1) * DH] = (scaled * gain_ref[head]).astype(headed.dtype)
    out_ref[...] = jnp.dot(
        headed[...], w_ref[...], preferred_element_type=jnp.float32
    ).astype(out_ref.dtype)


def slab(shift, rows, cols):
    return pl.BlockSpec((None, rows, cols), lambda h: (h + shift, 0, 0))


def local(tokens, norm_gain, w_qkv, conv_weight, head_gain, w_out):
    rows, width = tokens.shape
    tokens_f = tokens.astype(jnp.float32)
    scale = lax.rsqrt(jnp.mean(tokens_f * tokens_f, -1, keepdims=True) + 1e-06)
    normed = (tokens_f * scale * norm_gain).astype(jnp.bfloat16)

    slabs = w_qkv.shape[1] // DH
    projected = jnp.einsum(
        "td,dje->jte", normed, w_qkv.reshape(width, slabs, DH), preferred_element_type=jnp.float32
    ).astype(jnp.bfloat16)

    seq_axes = ("sy", "sz")
    count = lax.axis_size("sy") * lax.axis_size("sz")
    earlier_rows = lax.ppermute(
        projected[:, rows - (KW - 1) :, :], seq_axes, [(i, i + 1) for i in range(count - 1)]
    )
    taps = conv_weight.reshape(KW, slabs, DH).transpose(1, 0, 2)

    mixed_shape = jax.ShapeDtypeStruct((H, rows, DH), jnp.bfloat16)
    query, key, value, state = pl.pallas_call(
        conv_kernel,
        grid=(H,),
        in_specs=[slab(0, rows, DH), slab(H, rows, DH), slab(2 * H, rows, DH)]
        + [slab(0, KW - 1, DH), slab(H, KW - 1, DH), slab(2 * H, KW - 1, DH)]
        + [slab(0, KW, DH), slab(H, KW, DH), slab(2 * H, KW, DH)],
        out_specs=[slab(0, rows, DH)] * 3 + [slab(0, DH, DH)],
        out_shape=[mixed_shape] * 3 + [jax.ShapeDtypeStruct((H, DH, DH), jnp.bfloat16)],
        scratch_shapes=[pltpu.VMEM((rows + PAD, DH), jnp.float32)],
        cost_estimate=pl.CostEstimate(
            flops=H * (3 * rows * DH * 12 + 2 * rows * DH * DH),
            transcendentals=H * 3 * rows * DH,
            bytes_accessed=H * 3 * rows * DH * 4,
        ),
    )(projected, projected, projected, earlier_rows, earlier_rows, earlier_rows, taps, taps, taps)

    block = min(BLOCK, rows)
    local_part = pl.pallas_call(
        local_kernel,
        grid=(H,),
        in_specs=[slab(0, rows, DH)] * 3,
        out_specs=slab(0, rows, DH),
        out_shape=jax.ShapeDtypeStruct((H, rows, DH), jnp.float32),
        cost_estimate=pl.CostEstimate(
            flops=H * (4 * rows * block * DH + 6 * rows * DH * DH),
            transcendentals=0,
            bytes_accessed=H * rows * DH * 10,
        ),
    )(query, key, value)

    prefix = earlier_states(state)

    tile = min(512, rows)
    out = pl.pallas_call(
        out_kernel,
        grid=(rows // tile,),
        in_specs=[
            pl.BlockSpec((H, tile, DH), lambda i: (0, i, 0)),
            pl.BlockSpec((H, tile, DH), lambda i: (0, i, 0)),
            pl.BlockSpec((H, DH, DH), lambda i: (0, 0, 0)),
            pl.BlockSpec((H, 1, DH), lambda i: (0, 0, 0)),
            pl.BlockSpec((width, width), lambda i: (0, 0)),
        ],
        out_specs=pl.BlockSpec((tile, width), lambda i: (i, 0)),
        out_shape=jax.ShapeDtypeStruct((rows, width), jnp.bfloat16),
        scratch_shapes=[pltpu.VMEM((tile, H * DH), jnp.bfloat16)],
        cost_estimate=pl.CostEstimate(
            flops=H * 4 * rows * DH * DH + 2 * rows * width * width,
            transcendentals=H * rows,
            bytes_accessed=H * rows * DH * 6 + width * width * 2 + rows * width * 2,
        ),
    )(query, local_part, prefix, head_gain.reshape(H, 1, DH), w_out)
    return out


def solution(mesh):
    seq = mesh.shape["seq"]
    inner = 4 if seq % 4 == 0 else 1
    grid = Mesh(
        mesh.devices.reshape(mesh.shape["trace"], seq // inner, inner), ("trace", "sy", "sz")
    )
    rows = P(("trace", "sy", "sz"), None)
    placed = (rows, P(), P(), P(), P(), P())
    return jax.shard_map(local, mesh=grid, in_specs=placed, out_specs=rows, check_vma=False)
```

```python
import jax
import jax.numpy as jnp
from jax import lax
from jax.experimental import pallas as pl
from jax.experimental.pallas import tpu as pltpu
from jax.sharding import Mesh
from jax.sharding import PartitionSpec as P

H = 8
DH = 128
KW = 4
BLOCK = 512
PAD = 8


def split_bf16(x):
    hi = lax.reduce_precision(x, exponent_bits=8, mantissa_bits=7)
    return hi.astype(jnp.bfloat16), (x - hi).astype(jnp.bfloat16)


def earlier_states(state):
    count = lax.axis_size("sz")
    rows_count = lax.axis_size("sy")
    quarters = state.astype(jnp.bfloat16).reshape((count, -1) + state.shape[1:])
    mine = lax.all_to_all(quarters, "sz", 0, 0).astype(jnp.float32)
    before = [jnp.zeros_like(mine[0])]
    for z in range(1, count):
        before.append(before[-1] + mine[z - 1])
    row_total = before[-1] + mine[count - 1]
    row = lax.axis_index("sy")
    later_row = (row < lax.iota(jnp.int32, rows_count)).astype(jnp.float32)
    same_row = (row == lax.iota(jnp.int32, rows_count)).astype(jnp.float32)
    messages = (
        later_row[:, None, None, None, None] * row_total[None, None]
        + same_row[:, None, None, None, None] * jnp.stack(before)[None]
    )
    received = lax.all_to_all(
        messages.astype(jnp.bfloat16).reshape((rows_count * count,) + row_total.shape),
        ("sy", "sz"),
        0,
        0,
    )
    return received.reshape((rows_count,) + state.shape)


def conv_kernel(pq, pk, pv, eq, ek, ev, tq, tk, tv, oq, ok, ov, state_ref, buf):
    rows = pq.shape[0]
    for proj, early, taps, out in ((pq, eq, tq, oq), (pk, ek, tk, ok), (pv, ev, tv, ov)):
        buf[PAD - (KW - 1) : PAD, :] = early[...].astype(jnp.float32)
        buf[PAD:, :] = proj[...].astype(jnp.float32)
        summed = jnp.zeros((rows, DH), jnp.float32)
        for offset in range(KW):
            summed = summed + taps[offset : offset + 1, :] * buf[pl.ds(PAD - offset, rows), :]
        out[...] = (summed * jax.nn.sigmoid(summed)).astype(out.dtype)
    state_ref[...] = lax.dot_general(
        ok[...], ov[...], (((0,), (0,)), ((), ())), preferred_element_type=jnp.float32
    ).astype(state_ref.dtype)


def local_kernel(q_ref, k_ref, v_ref, out_ref):
    rows = q_ref.shape[0]
    block = min(BLOCK, rows)
    causal = lax.broadcasted_iota(jnp.int32, (block, block), 0) >= lax.broadcasted_iota(
        jnp.int32, (block, block), 1
    )
    inner = jnp.zeros((DH, DH), jnp.float32)
    for b in range(rows // block):
        span = pl.ds(b * block, block)
        query, key, value = q_ref[span, :], k_ref[span, :], v_ref[span, :]
        scores = lax.dot_general(
            query, key, (((1,), (1,)), ((), ())), preferred_element_type=jnp.float32
        )
        scores = jnp.where(causal, scores, 0.0).astype(jnp.bfloat16)
        part = jnp.dot(scores, value, preferred_element_type=jnp.float32)
        if b > 0:
            hi, lo = split_bf16(inner)
            part = part + jnp.dot(query, hi, preferred_element_type=jnp.float32)
            part = part + jnp.dot(query, lo, preferred_element_type=jnp.float32)
        out_ref[span, :] = part
        inner = inner + lax.dot_general(
            key, value, (((0,), (0,)), ((), ())), preferred_element_type=jnp.float32
        )


def out_kernel(q_ref, local_ref, prefix_ref, gain_ref, w_ref, out_ref, headed):
    for head in range(q_ref.shape[0]):
        hi, lo = split_bf16(jnp.sum(prefix_ref[:, head].astype(jnp.float32), 0))
        query = q_ref[head]
        attended = local_ref[head] + jnp.dot(query, hi, preferred_element_type=jnp.float32)
        attended = attended + jnp.dot(query, lo, preferred_element_type=jnp.float32)
        scaled = attended * lax.rsqrt(jnp.mean(attended * attended, -1, keepdims=True) + 1e-05)
        headed[:, head * DH : (head + 1) * DH] = (scaled * gain_ref[head]).astype(headed.dtype)
    out_ref[...] = jnp.dot(
        headed[...], w_ref[...], preferred_element_type=jnp.float32
    ).astype(out_ref.dtype)


def slab(shift, rows, cols):
    return pl.BlockSpec((None, rows, cols), lambda h: (h + shift, 0, 0))


def local(tokens, norm_gain, w_qkv, conv_weight, head_gain, w_out):
    rows, width = tokens.shape
    tokens_f = tokens.astype(jnp.float32)
    scale = lax.rsqrt(jnp.mean(tokens_f * tokens_f, -1, keepdims=True) + 1e-06)
    normed = (tokens_f * scale * norm_gain).astype(jnp.bfloat16)

    slabs = w_qkv.shape[1] // DH
    projected = jnp.einsum(
        "td,dje->jte", normed, w_qkv.reshape(width, slabs, DH), preferred_element_type=jnp.float32
    ).astype(jnp.bfloat16)

    seq_axes = ("sy", "sz")
    count = lax.axis_size("sy") * lax.axis_size("sz")
    earlier_rows = lax.ppermute(
        projected[:, rows - (KW - 1) :, :], seq_axes, [(i, i + 1) for i in range(count - 1)]
    )
    taps = conv_weight.reshape(KW, slabs, DH).transpose(1, 0, 2)

    mixed_shape = jax.ShapeDtypeStruct((H, rows, DH), jnp.bfloat16)
    query, key, value, state = pl.pallas_call(
        conv_kernel,
        grid=(H,),
        in_specs=[slab(0, rows, DH), slab(H, rows, DH), slab(2 * H, rows, DH)]
        + [slab(0, KW - 1, DH), slab(H, KW - 1, DH), slab(2 * H, KW - 1, DH)]
        + [slab(0, KW, DH), slab(H, KW, DH), slab(2 * H, KW, DH)],
        out_specs=[slab(0, rows, DH)] * 3 + [slab(0, DH, DH)],
        out_shape=[mixed_shape] * 3 + [jax.ShapeDtypeStruct((H, DH, DH), jnp.bfloat16)],
        scratch_shapes=[pltpu.VMEM((rows + PAD, DH), jnp.float32)],
        cost_estimate=pl.CostEstimate(
            flops=H * (3 * rows * DH * 12 + 2 * rows * DH * DH),
            transcendentals=H * 3 * rows * DH,
            bytes_accessed=H * 3 * rows * DH * 4,
        ),
    )(projected, projected, projected, earlier_rows, earlier_rows, earlier_rows, taps, taps, taps)

    block = min(BLOCK, rows)
    local_part = pl.pallas_call(
        local_kernel,
        grid=(H,),
        in_specs=[slab(0, rows, DH)] * 3,
        out_specs=slab(0, rows, DH),
        out_shape=jax.ShapeDtypeStruct((H, rows, DH), jnp.float32),
        cost_estimate=pl.CostEstimate(
            flops=H * (4 * rows * block * DH + 6 * rows * DH * DH),
            transcendentals=0,
            bytes_accessed=H * rows * DH * 10,
        ),
    )(query, key, value)

    prefix = earlier_states(state)

    tile = min(512, rows)
    out = pl.pallas_call(
        out_kernel,
        grid=(rows // tile,),
        in_specs=[
            pl.BlockSpec((H, tile, DH), lambda i: (0, i, 0)),
            pl.BlockSpec((H, tile, DH), lambda i: (0, i, 0)),
            pl.BlockSpec(prefix.shape, lambda i: (0, 0, 0, 0)),
            pl.BlockSpec((H, 1, DH), lambda i: (0, 0, 0)),
            pl.BlockSpec((width, width), lambda i: (0, 0)),
        ],
        out_specs=pl.BlockSpec((tile, width), lambda i: (i, 0)),
        out_shape=jax.ShapeDtypeStruct((rows, width), jnp.bfloat16),
        scratch_shapes=[pltpu.VMEM((tile, H * DH), jnp.bfloat16)],
        cost_estimate=pl.CostEstimate(
            flops=H * 4 * rows * DH * DH + 2 * rows * width * width,
            transcendentals=H * rows,
            bytes_accessed=H * rows * DH * 6 + width * width * 2 + rows * width * 2,
        ),
    )(query, local_part, prefix, head_gain.reshape(H, 1, DH), w_out)
    return out


def solution(mesh):
    seq = mesh.shape["seq"]
    inner = 4 if seq % 4 == 0 else 1
    grid = Mesh(
        mesh.devices.reshape(mesh.shape["trace"], seq // inner, inner), ("trace", "sy", "sz")
    )
    rows = P(("trace", "sy", "sz"), None)
    placed = (rows, P(), P(), P(), P(), P())
    return jax.shard_map(local, mesh=grid, in_specs=placed, out_specs=rows, check_vma=False)
```

```python
import jax
import jax.numpy as jnp
from jax import lax
from jax.experimental import pallas as pl
from jax.experimental.pallas import tpu as pltpu
from jax.sharding import Mesh
from jax.sharding import PartitionSpec as P

H = 8
DH = 128
KW = 4
BLOCK = 512
PAD = 8


def split_bf16(x):
    hi = lax.reduce_precision(x, exponent_bits=8, mantissa_bits=7)
    return hi.astype(jnp.bfloat16), (x - hi).astype(jnp.bfloat16)


def earlier_states(state):
    count = lax.axis_size("sz")
    rows_count = lax.axis_size("sy")
    quarters = state.astype(jnp.bfloat16).reshape((count, -1) + state.shape[1:])
    mine = lax.all_to_all(quarters, "sz", 0, 0).astype(jnp.float32)
    before = [jnp.zeros_like(mine[0])]
    for z in range(1, count):
        before.append(before[-1] + mine[z - 1])
    row_total = before[-1] + mine[count - 1]
    row = lax.axis_index("sy")
    later_row = (row < lax.iota(jnp.int32, rows_count)).astype(jnp.float32)
    same_row = (row == lax.iota(jnp.int32, rows_count)).astype(jnp.float32)
    messages = (
        later_row[:, None, None, None, None] * row_total[None, None]
        + same_row[:, None, None, None, None] * jnp.stack(before)[None]
    )
    received = lax.all_to_all(
        messages.astype(jnp.bfloat16).reshape((rows_count * count,) + row_total.shape),
        ("sy", "sz"),
        0,
        0,
    )
    received = received.reshape((rows_count, count) + row_total.shape).astype(jnp.float32)
    return jnp.sum(received, 0).reshape(state.shape)


def conv_kernel(pq, pk, pv, eq, ek, ev, tq, tk, tv, oq, ok, ov, state_ref, buf):
    rows = pq.shape[0]
    for proj, early, taps, out in ((pq, eq, tq, oq), (pk, ek, tk, ok), (pv, ev, tv, ov)):
        buf[PAD - (KW - 1) : PAD, :] = early[...].astype(jnp.float32)
        current = proj[...].astype(jnp.float32)
        buf[PAD:, :] = current
        summed = taps[0:1, :] * current
        for offset in range(1, KW):
            summed = summed + taps[offset : offset + 1, :] * buf[pl.ds(PAD - offset, rows), :]
        out[...] = (summed * jax.nn.sigmoid(summed)).astype(out.dtype)
    state_ref[...] = lax.dot_general(
        ok[...], ov[...], (((0,), (0,)), ((), ())), preferred_element_type=jnp.float32
    ).astype(state_ref.dtype)


def local_kernel(q_ref, k_ref, v_ref, out_ref):
    rows = q_ref.shape[0]
    block = min(BLOCK, rows)
    causal = lax.broadcasted_iota(jnp.int32, (block, block), 0) >= lax.broadcasted_iota(
        jnp.int32, (block, block), 1
    )
    inner = jnp.zeros((DH, DH), jnp.float32)
    for b in range(rows // block):
        span = pl.ds(b * block, block)
        query, key, value = q_ref[span, :], k_ref[span, :], v_ref[span, :]
        scores = lax.dot_general(
            query, key, (((1,), (1,)), ((), ())), preferred_element_type=jnp.float32
        )
        scores = jnp.where(causal, scores, 0.0).astype(jnp.bfloat16)
        part = jnp.dot(scores, value, preferred_element_type=jnp.float32)
        if b > 0:
            hi, lo = split_bf16(inner)
            part = part + jnp.dot(query, hi, preferred_element_type=jnp.float32)
            part = part + jnp.dot(query, lo, preferred_element_type=jnp.float32)
        out_ref[span, :] = part
        inner = inner + lax.dot_general(
            key, value, (((0,), (0,)), ((), ())), preferred_element_type=jnp.float32
        )


def out_kernel(q_ref, local_ref, prefix_ref, gain_ref, w_ref, out_ref, headed):
    for head in range(q_ref.shape[0]):
        hi, lo = split_bf16(prefix_ref[head])
        both = jnp.dot(
            q_ref[head], jnp.concatenate([hi, lo], 1), preferred_element_type=jnp.float32
        )
        attended = local_ref[head] + both[:, :DH]
        attended = attended + both[:, DH:]
        scaled = attended * lax.rsqrt(jnp.mean(attended * attended, -1, keepdims=True) + 1e-05)
        headed[:, head * DH : (head + 1) * DH] = (scaled * gain_ref[head]).astype(headed.dtype)
    out_ref[...] = jnp.dot(
        headed[...], w_ref[...], preferred_element_type=jnp.float32
    ).astype(out_ref.dtype)


def slab(shift, rows, cols):
    return pl.BlockSpec((None, rows, cols), lambda h: (h + shift, 0, 0))


def local(tokens, norm_gain, w_qkv, conv_weight, head_gain, w_out):
    rows, width = tokens.shape
    tokens_f = tokens.astype(jnp.float32)
    scale = lax.rsqrt(jnp.mean(tokens_f * tokens_f, -1, keepdims=True) + 1e-06)
    normed = (tokens_f * scale * norm_gain).astype(jnp.bfloat16)

    slabs = w_qkv.shape[1] // DH
    projected = jnp.einsum(
        "td,dje->jte", normed, w_qkv.reshape(width, slabs, DH), preferred_element_type=jnp.float32
    ).astype(jnp.bfloat16)

    seq_axes = ("sy", "sz")
    count = lax.axis_size("sy") * lax.axis_size("sz")
    earlier_rows = lax.ppermute(
        projected[:, rows - (KW - 1) :, :], seq_axes, [(i, i + 1) for i in range(count - 1)]
    )
    taps = conv_weight.reshape(KW, slabs, DH).transpose(1, 0, 2)

    mixed_shape = jax.ShapeDtypeStruct((H, rows, DH), jnp.bfloat16)
    query, key, value, state = pl.pallas_call(
        conv_kernel,
        grid=(H,),
        in_specs=[slab(0, rows, DH), slab(H, rows, DH), slab(2 * H, rows, DH)]
        + [slab(0, KW - 1, DH), slab(H, KW - 1, DH), slab(2 * H, KW - 1, DH)]
        + [slab(0, KW, DH), slab(H, KW, DH), slab(2 * H, KW, DH)],
        out_specs=[slab(0, rows, DH)] * 3 + [slab(0, DH, DH)],
        out_shape=[mixed_shape] * 3 + [jax.ShapeDtypeStruct((H, DH, DH), jnp.bfloat16)],
        scratch_shapes=[pltpu.VMEM((rows + PAD, DH), jnp.float32)],
        cost_estimate=pl.CostEstimate(
            flops=H * (3 * rows * DH * 12 + 2 * rows * DH * DH),
            transcendentals=H * 3 * rows * DH,
            bytes_accessed=H * 3 * rows * DH * 4,
        ),
    )(projected, projected, projected, earlier_rows, earlier_rows, earlier_rows, taps, taps, taps)

    block = min(BLOCK, rows)
    local_part = pl.pallas_call(
        local_kernel,
        grid=(H,),
        in_specs=[slab(0, rows, DH)] * 3,
        out_specs=slab(0, rows, DH),
        out_shape=jax.ShapeDtypeStruct((H, rows, DH), jnp.float32),
        cost_estimate=pl.CostEstimate(
            flops=H * (4 * rows * block * DH + 6 * rows * DH * DH),
            transcendentals=0,
            bytes_accessed=H * rows * DH * 10,
        ),
    )(query, key, value)

    prefix = earlier_states(state)

    tile = min(512, rows)
    out = pl.pallas_call(
        out_kernel,
        grid=(rows // tile,),
        in_specs=[
            pl.BlockSpec((H, tile, DH), lambda i: (0, i, 0)),
            pl.BlockSpec((H, tile, DH), lambda i: (0, i, 0)),
            pl.BlockSpec((H, DH, DH), lambda i: (0, 0, 0)),
            pl.BlockSpec((H, 1, DH), lambda i: (0, 0, 0)),
            pl.BlockSpec((width, width), lambda i: (0, 0)),
        ],
        out_specs=pl.BlockSpec((tile, width), lambda i: (i, 0)),
        out_shape=jax.ShapeDtypeStruct((rows, width), jnp.bfloat16),
        scratch_shapes=[pltpu.VMEM((tile, H * DH), jnp.bfloat16)],
        cost_estimate=pl.CostEstimate(
            flops=H * 4 * rows * DH * DH + 2 * rows * width * width,
            transcendentals=H * rows,
            bytes_accessed=H * rows * DH * 6 + width * width * 2 + rows * width * 2,
        ),
    )(query, local_part, prefix, head_gain.reshape(H, 1, DH), w_out)
    return out


def solution(mesh):
    seq = mesh.shape["seq"]
    inner = 4 if seq % 4 == 0 else 1
    grid = Mesh(
        mesh.devices.reshape(mesh.shape["trace"], seq // inner, inner), ("trace", "sy", "sz")
    )
    rows = P(("trace", "sy", "sz"), None)
    placed = (rows, P(), P(), P(), P(), P())
    return jax.shard_map(local, mesh=grid, in_specs=placed, out_specs=rows, check_vma=False)
```

```python
import jax
import jax.numpy as jnp
from jax import lax
from jax.experimental import pallas as pl
from jax.experimental.pallas import tpu as pltpu
from jax.sharding import Mesh
from jax.sharding import PartitionSpec as P

H = 8
DH = 128
KW = 4
BLOCK = 512
PAD = 8
LEAD = 16


def split_bf16(x):
    hi = lax.reduce_precision(x, exponent_bits=8, mantissa_bits=7)
    return hi.astype(jnp.bfloat16), (x - hi).astype(jnp.bfloat16)


def earlier_states(state):
    count = lax.axis_size("sz")
    rows_count = lax.axis_size("sy")
    quarters = state.astype(jnp.bfloat16).reshape((count, -1) + state.shape[1:])
    mine = lax.all_to_all(quarters, "sz", 0, 0).astype(jnp.float32)
    before = [jnp.zeros_like(mine[0])]
    for z in range(1, count):
        before.append(before[-1] + mine[z - 1])
    row_total = before[-1] + mine[count - 1]
    row = lax.axis_index("sy")
    later_row = (row < lax.iota(jnp.int32, rows_count)).astype(jnp.float32)
    same_row = (row == lax.iota(jnp.int32, rows_count)).astype(jnp.float32)
    messages = (
        later_row[:, None, None, None, None] * row_total[None, None]
        + same_row[:, None, None, None, None] * jnp.stack(before)[None]
    )
    received = lax.all_to_all(
        messages.astype(jnp.bfloat16).reshape((rows_count * count,) + row_total.shape),
        ("sy", "sz"),
        0,
        0,
    )
    received = received.reshape((rows_count, count) + row_total.shape).astype(jnp.float32)
    return jnp.sum(received, 0).reshape(state.shape)


def conv_kernel(pq, pk, pv, eq, ek, ev, tq, tk, tv, oq, ok, ov, state_ref, buf):
    rows = pq.shape[0]
    for proj, early, taps, out in ((pq, eq, tq, oq), (pk, ek, tk, ok), (pv, ev, tv, ov)):
        buf[PAD - (KW - 1) : PAD, :] = early[LEAD - (KW - 1) :, :].astype(jnp.float32)
        buf[PAD:, :] = proj[...].astype(jnp.float32)
        summed = jnp.zeros((rows, DH), jnp.float32)
        for offset in range(KW):
            summed = summed + taps[offset : offset + 1, :] * buf[pl.ds(PAD - offset, rows), :]
        out[...] = (summed * jax.nn.sigmoid(summed)).astype(out.dtype)
    state_ref[...] = lax.dot_general(
        ok[...], ov[...], (((0,), (0,)), ((), ())), preferred_element_type=jnp.float32
    ).astype(state_ref.dtype)


def local_kernel(q_ref, k_ref, v_ref, out_ref):
    rows = q_ref.shape[0]
    block = min(BLOCK, rows)
    causal = lax.broadcasted_iota(jnp.int32, (block, block), 0) >= lax.broadcasted_iota(
        jnp.int32, (block, block), 1
    )
    inner = jnp.zeros((DH, DH), jnp.float32)
    for b in range(rows // block):
        span = pl.ds(b * block, block)
        query, key, value = q_ref[span, :], k_ref[span, :], v_ref[span, :]
        scores = lax.dot_general(
            query, key, (((1,), (1,)), ((), ())), preferred_element_type=jnp.float32
        )
        scores = jnp.where(causal, scores, 0.0).astype(jnp.bfloat16)
        part = jnp.dot(scores, value, preferred_element_type=jnp.float32)
        if b > 0:
            hi, lo = split_bf16(inner)
            part = part + jnp.dot(query, hi, preferred_element_type=jnp.float32)
            part = part + jnp.dot(query, lo, preferred_element_type=jnp.float32)
        out_ref[span, :] = part
        inner = inner + lax.dot_general(
            key, value, (((0,), (0,)), ((), ())), preferred_element_type=jnp.float32
        )


def out_kernel(q_ref, local_ref, prefix_ref, gain_ref, w_ref, out_ref, headed):
    for head in range(q_ref.shape[0]):
        hi, lo = split_bf16(prefix_ref[head])
        query = q_ref[head]
        attended = local_ref[head] + jnp.dot(query, hi, preferred_element_type=jnp.float32)
        attended = attended + jnp.dot(query, lo, preferred_element_type=jnp.float32)
        scaled = attended * lax.rsqrt(jnp.mean(attended * attended, -1, keepdims=True) + 1e-05)
        headed[:, head * DH : (head + 1) * DH] = (scaled * gain_ref[head]).astype(headed.dtype)
    out_ref[...] = jnp.dot(
        headed[...], w_ref[...], preferred_element_type=jnp.float32
    ).astype(out_ref.dtype)


def slab(shift, rows, cols):
    return pl.BlockSpec((None, rows, cols), lambda h: (h + shift, 0, 0))


def local(tokens, norm_gain, w_qkv, conv_weight, head_gain, w_out):
    rows, width = tokens.shape
    tokens_f = tokens.astype(jnp.float32)
    scale = lax.rsqrt(jnp.mean(tokens_f * tokens_f, -1, keepdims=True) + 1e-06)
    normed = (tokens_f * scale * norm_gain).astype(jnp.bfloat16)

    slabs = w_qkv.shape[1] // DH
    projected = jnp.einsum(
        "td,dje->jte", normed, w_qkv.reshape(width, slabs, DH), preferred_element_type=jnp.float32
    ).astype(jnp.bfloat16)

    seq_axes = ("sy", "sz")
    count = lax.axis_size("sy") * lax.axis_size("sz")
    earlier_rows = lax.ppermute(
        projected[:, rows - LEAD :, :], seq_axes, [(i, i + 1) for i in range(count - 1)]
    )
    taps = conv_weight.reshape(KW, slabs, DH).transpose(1, 0, 2)

    mixed_shape = jax.ShapeDtypeStruct((H, rows, DH), jnp.bfloat16)
    query, key, value, state = pl.pallas_call(
        conv_kernel,
        grid=(H,),
        in_specs=[slab(0, rows, DH), slab(H, rows, DH), slab(2 * H, rows, DH)]
        + [slab(0, LEAD, DH), slab(H, LEAD, DH), slab(2 * H, LEAD, DH)]
        + [slab(0, KW, DH), slab(H, KW, DH), slab(2 * H, KW, DH)],
        out_specs=[slab(0, rows, DH)] * 3 + [slab(0, DH, DH)],
        out_shape=[mixed_shape] * 3 + [jax.ShapeDtypeStruct((H, DH, DH), jnp.bfloat16)],
        scratch_shapes=[pltpu.VMEM((rows + PAD, DH), jnp.float32)],
        cost_estimate=pl.CostEstimate(
            flops=H * (3 * rows * DH * 12 + 2 * rows * DH * DH),
            transcendentals=H * 3 * rows * DH,
            bytes_accessed=H * 3 * rows * DH * 4,
        ),
    )(projected, projected, projected, earlier_rows, earlier_rows, earlier_rows, taps, taps, taps)

    block = min(BLOCK, rows)
    local_part = pl.pallas_call(
        local_kernel,
        grid=(H,),
        in_specs=[slab(0, rows, DH)] * 3,
        out_specs=slab(0, rows, DH),
        out_shape=jax.ShapeDtypeStruct((H, rows, DH), jnp.float32),
        cost_estimate=pl.CostEstimate(
            flops=H * (4 * rows * block * DH + 6 * rows * DH * DH),
            transcendentals=0,
            bytes_accessed=H * rows * DH * 10,
        ),
    )(query, key, value)

    prefix = earlier_states(state)

    tile = min(512, rows)
    out = pl.pallas_call(
        out_kernel,
        grid=(rows // tile,),
        in_specs=[
            pl.BlockSpec((H, tile, DH), lambda i: (0, i, 0)),
            pl.BlockSpec((H, tile, DH), lambda i: (0, i, 0)),
            pl.BlockSpec((H, DH, DH), lambda i: (0, 0, 0)),
            pl.BlockSpec((H, 1, DH), lambda i: (0, 0, 0)),
            pl.BlockSpec((width, width), lambda i: (0, 0)),
        ],
        out_specs=pl.BlockSpec((tile, width), lambda i: (i, 0)),
        out_shape=jax.ShapeDtypeStruct((rows, width), jnp.bfloat16),
        scratch_shapes=[pltpu.VMEM((tile, H * DH), jnp.bfloat16)],
        cost_estimate=pl.CostEstimate(
            flops=H * 4 * rows * DH * DH + 2 * rows * width * width,
            transcendentals=H * rows,
            bytes_accessed=H * rows * DH * 6 + width * width * 2 + rows * width * 2,
        ),
    )(query, local_part, prefix, head_gain.reshape(H, 1, DH), w_out)
    return out


def solution(mesh):
    seq = mesh.shape["seq"]
    inner = 4 if seq % 4 == 0 else 1
    grid = Mesh(
        mesh.devices.reshape(mesh.shape["trace"], seq // inner, inner), ("trace", "sy", "sz")
    )
    rows = P(("trace", "sy", "sz"), None)
    placed = (rows, P(), P(), P(), P(), P())
    return jax.shard_map(local, mesh=grid, in_specs=placed, out_specs=rows, check_vma=False)
```

```python
import jax
import jax.numpy as jnp
from jax import lax
from jax.experimental import pallas as pl
from jax.experimental.pallas import tpu as pltpu
from jax.sharding import Mesh
from jax.sharding import PartitionSpec as P

H = 8
DH = 128
KW = 4
BLOCK = 512
PAD = 8


def split_bf16(x):
    hi = lax.reduce_precision(x, exponent_bits=8, mantissa_bits=7)
    return hi.astype(jnp.bfloat16), (x - hi).astype(jnp.bfloat16)


def earlier_states(state):
    count = lax.axis_size("sz")
    rows_count = lax.axis_size("sy")
    quarters = state.astype(jnp.bfloat16).reshape((count, -1) + state.shape[1:])
    mine = lax.all_to_all(quarters, "sz", 0, 0).astype(jnp.float32)
    before = [jnp.zeros_like(mine[0])]
    for z in range(1, count):
        before.append(before[-1] + mine[z - 1])
    row_total = before[-1] + mine[count - 1]
    row = lax.axis_index("sy")
    later_row = (row < lax.iota(jnp.int32, rows_count)).astype(jnp.float32)
    same_row = (row == lax.iota(jnp.int32, rows_count)).astype(jnp.float32)
    messages = (
        later_row[:, None, None, None, None] * row_total[None, None]
        + same_row[:, None, None, None, None] * jnp.stack(before)[None]
    )
    received = lax.all_to_all(
        messages.astype(jnp.bfloat16).reshape((rows_count * count,) + row_total.shape),
        ("sy", "sz"),
        0,
        0,
    )
    received = received.reshape((rows_count, count) + row_total.shape).astype(jnp.float32)
    return jnp.sum(received, 0).reshape(state.shape)


def conv_kernel(pq, pk, pv, eq, ek, ev, tq, tk, tv, oq, ok, ov, state_ref, buf):
    rows = pq.shape[0]
    for proj, early, taps, out in ((pq, eq, tq, oq), (pk, ek, tk, ok), (pv, ev, tv, ov)):
        buf[PAD - (KW - 1) : PAD, :] = early[...].astype(jnp.float32)
        buf[PAD:, :] = proj[...].astype(jnp.float32)
        summed = jnp.zeros((rows, DH), jnp.float32)
        for offset in range(KW):
            summed = summed + taps[offset : offset + 1, :] * buf[pl.ds(PAD - offset, rows), :]
        out[...] = (summed * jax.nn.sigmoid(summed)).astype(out.dtype)
    state_ref[...] = lax.dot_general(
        ok[...], ov[...], (((0,), (0,)), ((), ())), preferred_element_type=jnp.float32
    ).astype(state_ref.dtype)


def local_kernel(q_ref, k_ref, v_ref, out_ref):
    rows = q_ref.shape[0]
    block = min(BLOCK, rows)
    causal = lax.broadcasted_iota(jnp.int32, (block, block), 0) >= lax.broadcasted_iota(
        jnp.int32, (block, block), 1
    )
    inner = jnp.zeros((DH, DH), jnp.float32)
    for b in range(rows // block):
        span = pl.ds(b * block, block)
        query, key, value = q_ref[span, :], k_ref[span, :], v_ref[span, :]
        scores = lax.dot_general(
            query, key, (((1,), (1,)), ((), ())), preferred_element_type=jnp.float32
        )
        scores = jnp.where(causal, scores, 0.0).astype(jnp.bfloat16)
        part = jnp.dot(scores, value, preferred_element_type=jnp.float32)
        if b > 0:
            hi, lo = split_bf16(inner)
            part = part + jnp.dot(query, hi, preferred_element_type=jnp.float32)
            part = part + jnp.dot(query, lo, preferred_element_type=jnp.float32)
        out_ref[span, :] = part
        inner = inner + lax.dot_general(
            key, value, (((0,), (0,)), ((), ())), preferred_element_type=jnp.float32
        )


def out_kernel(q_ref, local_ref, prefix_ref, gain_ref, w_ref, out_ref, headed):
    for head in range(q_ref.shape[0]):
        hi, lo = split_bf16(prefix_ref[head])
        query = q_ref[head]
        attended = local_ref[head] + jnp.dot(query, hi, preferred_element_type=jnp.float32)
        attended = attended + jnp.dot(query, lo, preferred_element_type=jnp.float32)
        scaled = attended * lax.rsqrt(jnp.mean(attended * attended, -1, keepdims=True) + 1e-05)
        headed[:, head * DH : (head + 1) * DH] = (scaled * gain_ref[head]).astype(headed.dtype)
    out_ref[...] = jnp.dot(
        headed[...], w_ref[...], preferred_element_type=jnp.float32
    ).astype(out_ref.dtype)


def slab(shift, rows, cols):
    return pl.BlockSpec((None, rows, cols), lambda h: (h + shift, 0, 0))


def local(tokens, norm_gain, w_qkv, conv_weight, head_gain, w_out):
    rows, width = tokens.shape
    tokens_f = tokens.astype(jnp.float32)
    scale = lax.rsqrt(jnp.mean(tokens_f * tokens_f, -1, keepdims=True) + 1e-06)
    normed = (tokens_f * scale * norm_gain).astype(jnp.bfloat16)

    slabs = w_qkv.shape[1] // DH
    projected = jnp.einsum(
        "td,dje->jte", normed, w_qkv.reshape(width, slabs, DH), preferred_element_type=jnp.float32
    ).astype(jnp.bfloat16)

    seq_axes = ("sy", "sz")
    count = lax.axis_size("sy") * lax.axis_size("sz")
    earlier_rows = lax.ppermute(
        projected[:, rows - (KW - 1) :, :], seq_axes, [(i, i + 1) for i in range(count - 1)]
    )
    taps = conv_weight.reshape(KW, slabs, DH).transpose(1, 0, 2)

    mixed_shape = jax.ShapeDtypeStruct((H, rows, DH), jnp.bfloat16)
    query, key, value, state = pl.pallas_call(
        conv_kernel,
        grid=(H,),
        in_specs=[slab(0, rows, DH), slab(H, rows, DH), slab(2 * H, rows, DH)]
        + [slab(0, KW - 1, DH), slab(H, KW - 1, DH), slab(2 * H, KW - 1, DH)]
        + [slab(0, KW, DH), slab(H, KW, DH), slab(2 * H, KW, DH)],
        out_specs=[slab(0, rows, DH)] * 3 + [slab(0, DH, DH)],
        out_shape=[mixed_shape] * 3 + [jax.ShapeDtypeStruct((H, DH, DH), jnp.bfloat16)],
        scratch_shapes=[pltpu.VMEM((rows + PAD, DH), jnp.float32)],
        compiler_params=pltpu.CompilerParams(vmem_limit_bytes=16 * 1024 * 1024),
        cost_estimate=pl.CostEstimate(
            flops=H * (3 * rows * DH * 12 + 2 * rows * DH * DH),
            transcendentals=H * 3 * rows * DH,
            bytes_accessed=H * 3 * rows * DH * 4,
        ),
    )(projected, projected, projected, earlier_rows, earlier_rows, earlier_rows, taps, taps, taps)

    block = min(BLOCK, rows)
    local_part = pl.pallas_call(
        local_kernel,
        grid=(H,),
        in_specs=[slab(0, rows, DH)] * 3,
        out_specs=slab(0, rows, DH),
        out_shape=jax.ShapeDtypeStruct((H, rows, DH), jnp.float32),
        cost_estimate=pl.CostEstimate(
            flops=H * (4 * rows * block * DH + 6 * rows * DH * DH),
            transcendentals=0,
            bytes_accessed=H * rows * DH * 10,
        ),
    )(query, key, value)

    prefix = earlier_states(state)

    tile = min(512, rows)
    out = pl.pallas_call(
        out_kernel,
        grid=(rows // tile,),
        in_specs=[
            pl.BlockSpec((H, tile, DH), lambda i: (0, i, 0)),
            pl.BlockSpec((H, tile, DH), lambda i: (0, i, 0)),
            pl.BlockSpec((H, DH, DH), lambda i: (0, 0, 0)),
            pl.BlockSpec((H, 1, DH), lambda i: (0, 0, 0)),
            pl.BlockSpec((width, width), lambda i: (0, 0)),
        ],
        out_specs=pl.BlockSpec((tile, width), lambda i: (i, 0)),
        out_shape=jax.ShapeDtypeStruct((rows, width), jnp.bfloat16),
        scratch_shapes=[pltpu.VMEM((tile, H * DH), jnp.bfloat16)],
        cost_estimate=pl.CostEstimate(
            flops=H * 4 * rows * DH * DH + 2 * rows * width * width,
            transcendentals=H * rows,
            bytes_accessed=H * rows * DH * 6 + width * width * 2 + rows * width * 2,
        ),
    )(query, local_part, prefix, head_gain.reshape(H, 1, DH), w_out)
    return out


def solution(mesh):
    seq = mesh.shape["seq"]
    inner = 4 if seq % 4 == 0 else 1
    grid = Mesh(
        mesh.devices.reshape(mesh.shape["trace"], seq // inner, inner), ("trace", "sy", "sz")
    )
    rows = P(("trace", "sy", "sz"), None)
    placed = (rows, P(), P(), P(), P(), P())
    return jax.shard_map(local, mesh=grid, in_specs=placed, out_specs=rows, check_vma=False)
```

```python
import jax
import jax.numpy as jnp
from jax import lax
from jax.experimental import pallas as pl
from jax.experimental.pallas import tpu as pltpu
from jax.sharding import Mesh
from jax.sharding import PartitionSpec as P

H = 8
DH = 128
KW = 4
BLOCK = 512
PAD = 8


def split_bf16(x):
    hi = lax.reduce_precision(x, exponent_bits=8, mantissa_bits=7)
    return hi.astype(jnp.bfloat16), (x - hi).astype(jnp.bfloat16)


def earlier_states(state):
    count = lax.axis_size("sz")
    rows_count = lax.axis_size("sy")
    quarters = state.astype(jnp.bfloat16).reshape((count, -1) + state.shape[1:])
    mine = lax.all_to_all(quarters, "sz", 0, 0).astype(jnp.float32)
    before = [jnp.zeros_like(mine[0])]
    for z in range(1, count):
        before.append(before[-1] + mine[z - 1])
    row_total = before[-1] + mine[count - 1]
    row = lax.axis_index("sy")
    later_row = (row < lax.iota(jnp.int32, rows_count)).astype(jnp.float32)
    same_row = (row == lax.iota(jnp.int32, rows_count)).astype(jnp.float32)
    messages = (
        later_row[:, None, None, None, None] * row_total[None, None]
        + same_row[:, None, None, None, None] * jnp.stack(before)[None]
    )
    received = lax.all_to_all(
        messages.astype(jnp.bfloat16).reshape((rows_count * count,) + row_total.shape),
        ("sy", "sz"),
        0,
        0,
    )
    received = received.reshape((rows_count, count) + row_total.shape).astype(jnp.float32)
    return jnp.sum(received, 0).reshape(state.shape)


def conv_kernel(pq, pk, pv, eq, ek, ev, tq, tk, tv, oq, ok, ov, state_ref, buf):
    rows = pq.shape[0]
    for proj, early, taps, out in ((pq, eq, tq, oq), (pk, ek, tk, ok), (pv, ev, tv, ov)):
        buf[PAD - (KW - 1) : PAD, :] = early[...].astype(jnp.float32)
        buf[PAD:, :] = proj[...].astype(jnp.float32)
        summed = jnp.zeros((rows, DH), jnp.float32)
        for offset in range(KW):
            summed = summed + taps[offset : offset + 1, :] * buf[pl.ds(PAD - offset, rows), :]
        out[...] = (summed * jax.nn.sigmoid(summed)).astype(out.dtype)
    state_ref[...] = lax.dot_general(
        ok[...], ov[...], (((0,), (0,)), ((), ())), preferred_element_type=jnp.float32
    ).astype(state_ref.dtype)


def local_kernel(q_ref, k_ref, v_ref, out_ref):
    rows = q_ref.shape[0]
    block = min(BLOCK, rows)
    causal = lax.broadcasted_iota(jnp.int32, (block, block), 0) >= lax.broadcasted_iota(
        jnp.int32, (block, block), 1
    )
    inner = jnp.zeros((DH, DH), jnp.float32)
    for b in range(rows // block):
        span = pl.ds(b * block, block)
        query, key, value = q_ref[span, :], k_ref[span, :], v_ref[span, :]
        scores = lax.dot_general(
            query, key, (((1,), (1,)), ((), ())), preferred_element_type=jnp.float32
        )
        scores = jnp.where(causal, scores, 0.0).astype(jnp.bfloat16)
        part = jnp.dot(scores, value, preferred_element_type=jnp.float32)
        if b > 0:
            hi, lo = split_bf16(inner)
            part = part + jnp.dot(query, hi, preferred_element_type=jnp.float32)
            part = part + jnp.dot(query, lo, preferred_element_type=jnp.float32)
        out_ref[span, :] = part
        inner = inner + lax.dot_general(
            key, value, (((0,), (0,)), ((), ())), preferred_element_type=jnp.float32
        )


def out_kernel(q_ref, local_ref, prefix_ref, gain_ref, w_ref, out_ref, headed):
    for head in range(q_ref.shape[0]):
        hi, lo = split_bf16(prefix_ref[head])
        query = q_ref[head]
        attended = local_ref[head] + jnp.dot(query, hi, preferred_element_type=jnp.float32)
        attended = attended + jnp.dot(query, lo, preferred_element_type=jnp.float32)
        scaled = attended * lax.rsqrt(jnp.mean(attended * attended, -1, keepdims=True) + 1e-05)
        headed[:, head * DH : (head + 1) * DH] = (scaled * gain_ref[head]).astype(headed.dtype)
    out_ref[...] = jnp.dot(
        headed[...], w_ref[...], preferred_element_type=jnp.float32
    ).astype(out_ref.dtype)


def slab(shift, rows, cols):
    return pl.BlockSpec((None, rows, cols), lambda h: (h + shift, 0, 0))


def local(tokens, norm_gain, w_qkv, conv_weight, head_gain, w_out):
    rows, width = tokens.shape
    tokens_f = tokens.astype(jnp.float32)
    scale = lax.rsqrt(jnp.mean(tokens_f * tokens_f, -1, keepdims=True) + 1e-06)
    normed = (tokens_f * scale * norm_gain).astype(jnp.bfloat16)

    slabs = w_qkv.shape[1] // DH
    projected = jnp.einsum(
        "td,dje->jte", normed, w_qkv.reshape(width, slabs, DH), preferred_element_type=jnp.float32
    ).astype(jnp.bfloat16)

    seq_axes = ("sy", "sz")
    count = lax.axis_size("sy") * lax.axis_size("sz")
    earlier_rows = lax.ppermute(
        projected[:, rows - (KW - 1) :, :], seq_axes, [(i, i + 1) for i in range(count - 1)]
    )
    taps = conv_weight.reshape(KW, slabs, DH).transpose(1, 0, 2)

    mixed_shape = jax.ShapeDtypeStruct((H, rows, DH), jnp.bfloat16)
    query, key, value, state = pl.pallas_call(
        conv_kernel,
        grid=(H,),
        in_specs=[slab(0, rows, DH), slab(H, rows, DH), slab(2 * H, rows, DH)]
        + [slab(0, KW - 1, DH), slab(H, KW - 1, DH), slab(2 * H, KW - 1, DH)]
        + [slab(0, KW, DH), slab(H, KW, DH), slab(2 * H, KW, DH)],
        out_specs=[slab(0, rows, DH)] * 3 + [slab(0, DH, DH)],
        out_shape=[mixed_shape] * 3 + [jax.ShapeDtypeStruct((H, DH, DH), jnp.bfloat16)],
        scratch_shapes=[pltpu.VMEM((rows + PAD, DH), jnp.float32)],
        cost_estimate=pl.CostEstimate(
            flops=H * (3 * rows * DH * 12 + 2 * rows * DH * DH),
            transcendentals=H * 3 * rows * DH,
            bytes_accessed=H * 3 * rows * DH * 4,
        ),
    )(projected, projected, projected, earlier_rows, earlier_rows, earlier_rows, taps, taps, taps)

    block = min(BLOCK, rows)
    local_part = pl.pallas_call(
        local_kernel,
        grid=(H,),
        in_specs=[slab(0, rows, DH)] * 3,
        out_specs=slab(0, rows, DH),
        out_shape=jax.ShapeDtypeStruct((H, rows, DH), jnp.float32),
        cost_estimate=pl.CostEstimate(
            flops=H * (4 * rows * block * DH + 6 * rows * DH * DH),
            transcendentals=0,
            bytes_accessed=H * rows * DH * 10,
        ),
    )(query, key, value)

    prefix = earlier_states(state)

    tile = min(512, rows)
    out = pl.pallas_call(
        out_kernel,
        grid=(rows // tile,),
        in_specs=[
            pl.BlockSpec((H, tile, DH), lambda i: (0, i, 0)),
            pl.BlockSpec((H, tile, DH), lambda i: (0, i, 0)),
            pl.BlockSpec((H, DH, DH), lambda i: (0, 0, 0)),
            pl.BlockSpec((H, 1, DH), lambda i: (0, 0, 0)),
            pl.BlockSpec((width, width), lambda i: (0, 0)),
        ],
        out_specs=pl.BlockSpec((tile, width), lambda i: (i, 0)),
        out_shape=jax.ShapeDtypeStruct((rows, width), jnp.bfloat16),
        scratch_shapes=[pltpu.VMEM((tile, H * DH), jnp.bfloat16)],
        compiler_params=pltpu.CompilerParams(vmem_limit_bytes=24 * 1024 * 1024),
        cost_estimate=pl.CostEstimate(
            flops=H * 4 * rows * DH * DH + 2 * rows * width * width,
            transcendentals=H * rows,
            bytes_accessed=H * rows * DH * 6 + width * width * 2 + rows * width * 2,
        ),
    )(query, local_part, prefix, head_gain.reshape(H, 1, DH), w_out)
    return out


def solution(mesh):
    seq = mesh.shape["seq"]
    inner = 4 if seq % 4 == 0 else 1
    grid = Mesh(
        mesh.devices.reshape(mesh.shape["trace"], seq // inner, inner), ("trace", "sy", "sz")
    )
    rows = P(("trace", "sy", "sz"), None)
    placed = (rows, P(), P(), P(), P(), P())
    return jax.shard_map(local, mesh=grid, in_specs=placed, out_specs=rows, check_vma=False)
```

```python
import functools

import jax
import jax.numpy as jnp
from jax import lax
from jax.experimental import pallas as pl
from jax.experimental.pallas import tpu as pltpu
from jax.sharding import Mesh
from jax.sharding import PartitionSpec as P

H = 8
DH = 128
KW = 4
BLOCK = 512
PAD = 8


def split_bf16(x):
    hi = lax.reduce_precision(x, exponent_bits=8, mantissa_bits=7)
    return hi.astype(jnp.bfloat16), (x - hi).astype(jnp.bfloat16)


def earlier_states(state, before_second):
    count = lax.axis_size("sz")
    rows_count = lax.axis_size("sy")
    quarters = state.astype(jnp.bfloat16).reshape((count, -1) + state.shape[1:])
    mine = lax.all_to_all(quarters, "sz", 0, 0).astype(jnp.float32)
    before = [jnp.zeros_like(mine[0])]
    for z in range(1, count):
        before.append(before[-1] + mine[z - 1])
    row_total = before[-1] + mine[count - 1]
    row = lax.axis_index("sy")
    later_row = (row < lax.iota(jnp.int32, rows_count)).astype(jnp.float32)
    same_row = (row == lax.iota(jnp.int32, rows_count)).astype(jnp.float32)
    messages = (
        later_row[:, None, None, None, None] * row_total[None, None]
        + same_row[:, None, None, None, None] * jnp.stack(before)[None]
    )
    messages, early_work = lax.optimization_barrier((messages.astype(jnp.bfloat16), before_second()))
    received = lax.all_to_all(
        messages.reshape((rows_count * count,) + row_total.shape),
        ("sy", "sz"),
        0,
        0,
    )
    received = received.reshape((rows_count, count) + row_total.shape).astype(jnp.float32)
    return jnp.sum(received, 0).reshape(state.shape), early_work


def conv_kernel(count, with_state, *refs):
    projs, earlies, tapss = refs[:count], refs[count : 2 * count], refs[2 * count : 3 * count]
    outs, buf = refs[3 * count : 4 * count], refs[-1]
    rows = projs[0].shape[0]
    for proj, early, taps, out in zip(projs, earlies, tapss, outs):
        buf[PAD - (KW - 1) : PAD, :] = early[...].astype(jnp.float32)
        buf[PAD:, :] = proj[...].astype(jnp.float32)
        summed = jnp.zeros((rows, DH), jnp.float32)
        for offset in range(KW):
            summed = summed + taps[offset : offset + 1, :] * buf[pl.ds(PAD - offset, rows), :]
        out[...] = (summed * jax.nn.sigmoid(summed)).astype(out.dtype)
    if with_state:
        refs[4 * count][...] = lax.dot_general(
            outs[0][...], outs[1][...], (((0,), (0,)), ((), ())), preferred_element_type=jnp.float32
        ).astype(jnp.bfloat16)


def conv_call(projected, earlier, taps, shifts, with_state):
    count = len(shifts)
    rows = projected.shape[1]
    out_specs = [slab(0, rows, DH)] * count
    out_shape = [jax.ShapeDtypeStruct((H, rows, DH), jnp.bfloat16)] * count
    if with_state:
        out_specs.append(slab(0, DH, DH))
        out_shape.append(jax.ShapeDtypeStruct((H, DH, DH), jnp.bfloat16))
    return pl.pallas_call(
        functools.partial(conv_kernel, count, with_state),
        grid=(H,),
        in_specs=[slab(shift, rows, DH) for shift in shifts]
        + [slab(shift, KW - 1, DH) for shift in shifts]
        + [slab(shift, KW, DH) for shift in shifts],
        out_specs=out_specs,
        out_shape=out_shape,
        scratch_shapes=[pltpu.VMEM((rows + PAD, DH), jnp.float32)],
        cost_estimate=pl.CostEstimate(
            flops=H * count * rows * DH * (12 + 2 * DH),
            transcendentals=H * count * rows * DH,
            bytes_accessed=H * count * rows * DH * 4,
        ),
    )(*([projected] * count + [earlier] * count + [taps] * count))


def local_kernel(q_ref, k_ref, v_ref, out_ref):
    rows = q_ref.shape[0]
    block = min(BLOCK, rows)
    causal = lax.broadcasted_iota(jnp.int32, (block, block), 0) >= lax.broadcasted_iota(
        jnp.int32, (block, block), 1
    )
    inner = jnp.zeros((DH, DH), jnp.float32)
    for b in range(rows // block):
        span = pl.ds(b * block, block)
        query, key, value = q_ref[span, :], k_ref[span, :], v_ref[span, :]
        scores = lax.dot_general(
            query, key, (((1,), (1,)), ((), ())), preferred_element_type=jnp.float32
        )
        scores = jnp.where(causal, scores, 0.0).astype(jnp.bfloat16)
        part = jnp.dot(scores, value, preferred_element_type=jnp.float32)
        if b > 0:
            hi, lo = split_bf16(inner)
            part = part + jnp.dot(query, hi, preferred_element_type=jnp.float32)
            part = part + jnp.dot(query, lo, preferred_element_type=jnp.float32)
        out_ref[span, :] = part
        inner = inner + lax.dot_general(
            key, value, (((0,), (0,)), ((), ())), preferred_element_type=jnp.float32
        )


def out_kernel(q_ref, local_ref, prefix_ref, gain_ref, w_ref, out_ref, headed):
    for head in range(q_ref.shape[0]):
        hi, lo = split_bf16(prefix_ref[head])
        query = q_ref[head]
        attended = local_ref[head] + jnp.dot(query, hi, preferred_element_type=jnp.float32)
        attended = attended + jnp.dot(query, lo, preferred_element_type=jnp.float32)
        scaled = attended * lax.rsqrt(jnp.mean(attended * attended, -1, keepdims=True) + 1e-05)
        headed[:, head * DH : (head + 1) * DH] = (scaled * gain_ref[head]).astype(headed.dtype)
    out_ref[...] = jnp.dot(
        headed[...], w_ref[...], preferred_element_type=jnp.float32
    ).astype(out_ref.dtype)


def slab(shift, rows, cols):
    return pl.BlockSpec((None, rows, cols), lambda h: (h + shift, 0, 0))


def local(tokens, norm_gain, w_qkv, conv_weight, head_gain, w_out):
    rows, width = tokens.shape
    tokens_f = tokens.astype(jnp.float32)
    scale = lax.rsqrt(jnp.mean(tokens_f * tokens_f, -1, keepdims=True) + 1e-06)
    normed = (tokens_f * scale * norm_gain).astype(jnp.bfloat16)

    slabs = w_qkv.shape[1] // DH
    projected = jnp.einsum(
        "td,dje->jte", normed, w_qkv.reshape(width, slabs, DH), preferred_element_type=jnp.float32
    ).astype(jnp.bfloat16)

    seq_axes = ("sy", "sz")
    count = lax.axis_size("sy") * lax.axis_size("sz")
    earlier_rows = lax.ppermute(
        projected[:, rows - (KW - 1) :, :], seq_axes, [(i, i + 1) for i in range(count - 1)]
    )
    taps = conv_weight.reshape(KW, slabs, DH).transpose(1, 0, 2)

    key, value, state = conv_call(projected, earlier_rows, taps, (H, 2 * H), True)
    prefix, (query,) = earlier_states(
        state, lambda: conv_call(projected, earlier_rows, taps, (0,), False)
    )

    block = min(BLOCK, rows)
    local_part = pl.pallas_call(
        local_kernel,
        grid=(H,),
        in_specs=[slab(0, rows, DH)] * 3,
        out_specs=slab(0, rows, DH),
        out_shape=jax.ShapeDtypeStruct((H, rows, DH), jnp.float32),
        cost_estimate=pl.CostEstimate(
            flops=H * (4 * rows * block * DH + 6 * rows * DH * DH),
            transcendentals=0,
            bytes_accessed=H * rows * DH * 10,
        ),
    )(query, key, value)

    tile = min(512, rows)
    out = pl.pallas_call(
        out_kernel,
        grid=(rows // tile,),
        in_specs=[
            pl.BlockSpec((H, tile, DH), lambda i: (0, i, 0)),
            pl.BlockSpec((H, tile, DH), lambda i: (0, i, 0)),
            pl.BlockSpec((H, DH, DH), lambda i: (0, 0, 0)),
            pl.BlockSpec((H, 1, DH), lambda i: (0, 0, 0)),
            pl.BlockSpec((width, width), lambda i: (0, 0)),
        ],
        out_specs=pl.BlockSpec((tile, width), lambda i: (i, 0)),
        out_shape=jax.ShapeDtypeStruct((rows, width), jnp.bfloat16),
        scratch_shapes=[pltpu.VMEM((tile, H * DH), jnp.bfloat16)],
        cost_estimate=pl.CostEstimate(
            flops=H * 4 * rows * DH * DH + 2 * rows * width * width,
            transcendentals=H * rows,
            bytes_accessed=H * rows * DH * 6 + width * width * 2 + rows * width * 2,
        ),
    )(query, local_part, prefix, head_gain.reshape(H, 1, DH), w_out)
    return out


def solution(mesh):
    seq = mesh.shape["seq"]
    inner = 4 if seq % 4 == 0 else 1
    grid = Mesh(
        mesh.devices.reshape(mesh.shape["trace"], seq // inner, inner), ("trace", "sy", "sz")
    )
    rows = P(("trace", "sy", "sz"), None)
    placed = (rows, P(), P(), P(), P(), P())
    return jax.shard_map(local, mesh=grid, in_specs=placed, out_specs=rows, check_vma=False)
```

```python
import jax
import jax.numpy as jnp
from jax import lax
from jax.experimental import pallas as pl
from jax.experimental.pallas import tpu as pltpu
from jax.sharding import Mesh
from jax.sharding import PartitionSpec as P

H = 8
DH = 128
KW = 4
BLOCK = 512
PAD = 8


def split_bf16(x):
    hi = lax.reduce_precision(x, exponent_bits=8, mantissa_bits=7)
    return hi.astype(jnp.bfloat16), (x - hi).astype(jnp.bfloat16)


def earlier_states(state):
    count = lax.axis_size("sz")
    rows_count = lax.axis_size("sy")
    quarters = state.astype(jnp.bfloat16).reshape((count, -1) + state.shape[1:])
    mine = lax.all_to_all(quarters, "sz", 0, 0).astype(jnp.float32)
    before = [jnp.zeros_like(mine[0])]
    for z in range(1, count):
        before.append(before[-1] + mine[z - 1])
    row_total = before[-1] + mine[count - 1]
    row = lax.axis_index("sy")
    later_row = (row < lax.iota(jnp.int32, rows_count)).astype(jnp.float32)
    same_row = (row == lax.iota(jnp.int32, rows_count)).astype(jnp.float32)
    messages = (
        later_row[:, None, None, None, None] * row_total[None, None]
        + same_row[:, None, None, None, None] * jnp.stack(before)[None]
    )
    received = lax.all_to_all(
        messages.astype(jnp.bfloat16).reshape((rows_count * count,) + row_total.shape),
        ("sy", "sz"),
        0,
        0,
    )
    received = received.reshape((rows_count, count) + row_total.shape).astype(jnp.float32)
    return jnp.sum(received, 0).reshape(state.shape)


def conv_kernel(pq, pk, pv, eq, ek, ev, tq, tk, tv, oq, ok, ov, state_ref, buf):
    rows = pq.shape[1]
    for g in range(pq.shape[0]):
        for proj, early, taps, out in ((pq, eq, tq, oq), (pk, ek, tk, ok), (pv, ev, tv, ov)):
            buf[PAD - (KW - 1) : PAD, :] = early[g].astype(jnp.float32)
            buf[PAD:, :] = proj[g].astype(jnp.float32)
            summed = jnp.zeros((rows, DH), jnp.float32)
            for offset in range(KW):
                summed = summed + taps[g, offset : offset + 1, :] * buf[pl.ds(PAD - offset, rows), :]
            out[g] = (summed * jax.nn.sigmoid(summed)).astype(out.dtype)
        state_ref[g] = lax.dot_general(
            ok[g], ov[g], (((0,), (0,)), ((), ())), preferred_element_type=jnp.float32
        ).astype(state_ref.dtype)


def group_slab(group, shift, rows, cols):
    return pl.BlockSpec((group, rows, cols), lambda h: (h + shift // group, 0, 0))


def local_kernel(q_ref, k_ref, v_ref, out_ref):
    rows = q_ref.shape[0]
    block = min(BLOCK, rows)
    causal = lax.broadcasted_iota(jnp.int32, (block, block), 0) >= lax.broadcasted_iota(
        jnp.int32, (block, block), 1
    )
    inner = jnp.zeros((DH, DH), jnp.float32)
    for b in range(rows // block):
        span = pl.ds(b * block, block)
        query, key, value = q_ref[span, :], k_ref[span, :], v_ref[span, :]
        scores = lax.dot_general(
            query, key, (((1,), (1,)), ((), ())), preferred_element_type=jnp.float32
        )
        scores = jnp.where(causal, scores, 0.0).astype(jnp.bfloat16)
        part = jnp.dot(scores, value, preferred_element_type=jnp.float32)
        if b > 0:
            hi, lo = split_bf16(inner)
            part = part + jnp.dot(query, hi, preferred_element_type=jnp.float32)
            part = part + jnp.dot(query, lo, preferred_element_type=jnp.float32)
        out_ref[span, :] = part
        inner = inner + lax.dot_general(
            key, value, (((0,), (0,)), ((), ())), preferred_element_type=jnp.float32
        )


def out_kernel(q_ref, local_ref, prefix_ref, gain_ref, w_ref, out_ref, headed):
    for head in range(q_ref.shape[0]):
        hi, lo = split_bf16(prefix_ref[head])
        query = q_ref[head]
        attended = local_ref[head] + jnp.dot(query, hi, preferred_element_type=jnp.float32)
        attended = attended + jnp.dot(query, lo, preferred_element_type=jnp.float32)
        scaled = attended * lax.rsqrt(jnp.mean(attended * attended, -1, keepdims=True) + 1e-05)
        headed[:, head * DH : (head + 1) * DH] = (scaled * gain_ref[head]).astype(headed.dtype)
    out_ref[...] = jnp.dot(
        headed[...], w_ref[...], preferred_element_type=jnp.float32
    ).astype(out_ref.dtype)


def slab(shift, rows, cols):
    return pl.BlockSpec((None, rows, cols), lambda h: (h + shift, 0, 0))


def local(tokens, norm_gain, w_qkv, conv_weight, head_gain, w_out):
    rows, width = tokens.shape
    tokens_f = tokens.astype(jnp.float32)
    scale = lax.rsqrt(jnp.mean(tokens_f * tokens_f, -1, keepdims=True) + 1e-06)
    normed = (tokens_f * scale * norm_gain).astype(jnp.bfloat16)

    slabs = w_qkv.shape[1] // DH
    projected = jnp.einsum(
        "td,dje->jte", normed, w_qkv.reshape(width, slabs, DH), preferred_element_type=jnp.float32
    ).astype(jnp.bfloat16)

    seq_axes = ("sy", "sz")
    count = lax.axis_size("sy") * lax.axis_size("sz")
    earlier_rows = lax.ppermute(
        projected[:, rows - (KW - 1) :, :], seq_axes, [(i, i + 1) for i in range(count - 1)]
    )
    taps = conv_weight.reshape(KW, slabs, DH).transpose(1, 0, 2)

    mixed_shape = jax.ShapeDtypeStruct((H, rows, DH), jnp.bfloat16)
    query, key, value, state = pl.pallas_call(
        conv_kernel,
        grid=(H // 2,),
        in_specs=[group_slab(2, shift, rows, DH) for shift in (0, H, 2 * H)]
        + [group_slab(2, shift, KW - 1, DH) for shift in (0, H, 2 * H)]
        + [group_slab(2, shift, KW, DH) for shift in (0, H, 2 * H)],
        out_specs=[group_slab(2, 0, rows, DH)] * 3 + [group_slab(2, 0, DH, DH)],
        out_shape=[mixed_shape] * 3 + [jax.ShapeDtypeStruct((H, DH, DH), jnp.bfloat16)],
        scratch_shapes=[pltpu.VMEM((rows + PAD, DH), jnp.float32)],
        cost_estimate=pl.CostEstimate(
            flops=H * (3 * rows * DH * 12 + 2 * rows * DH * DH),
            transcendentals=H * 3 * rows * DH,
            bytes_accessed=H * 3 * rows * DH * 4,
        ),
    )(projected, projected, projected, earlier_rows, earlier_rows, earlier_rows, taps, taps, taps)

    block = min(BLOCK, rows)
    local_part = pl.pallas_call(
        local_kernel,
        grid=(H,),
        in_specs=[slab(0, rows, DH)] * 3,
        out_specs=slab(0, rows, DH),
        out_shape=jax.ShapeDtypeStruct((H, rows, DH), jnp.float32),
        cost_estimate=pl.CostEstimate(
            flops=H * (4 * rows * block * DH + 6 * rows * DH * DH),
            transcendentals=0,
            bytes_accessed=H * rows * DH * 10,
        ),
    )(query, key, value)

    prefix = earlier_states(state)

    tile = min(512, rows)
    out = pl.pallas_call(
        out_kernel,
        grid=(rows // tile,),
        in_specs=[
            pl.BlockSpec((H, tile, DH), lambda i: (0, i, 0)),
            pl.BlockSpec((H, tile, DH), lambda i: (0, i, 0)),
            pl.BlockSpec((H, DH, DH), lambda i: (0, 0, 0)),
            pl.BlockSpec((H, 1, DH), lambda i: (0, 0, 0)),
            pl.BlockSpec((width, width), lambda i: (0, 0)),
        ],
        out_specs=pl.BlockSpec((tile, width), lambda i: (i, 0)),
        out_shape=jax.ShapeDtypeStruct((rows, width), jnp.bfloat16),
        scratch_shapes=[pltpu.VMEM((tile, H * DH), jnp.bfloat16)],
        cost_estimate=pl.CostEstimate(
            flops=H * 4 * rows * DH * DH + 2 * rows * width * width,
            transcendentals=H * rows,
            bytes_accessed=H * rows * DH * 6 + width * width * 2 + rows * width * 2,
        ),
    )(query, local_part, prefix, head_gain.reshape(H, 1, DH), w_out)
    return out


def solution(mesh):
    seq = mesh.shape["seq"]
    inner = 4 if seq % 4 == 0 else 1
    grid = Mesh(
        mesh.devices.reshape(mesh.shape["trace"], seq // inner, inner), ("trace", "sy", "sz")
    )
    rows = P(("trace", "sy", "sz"), None)
    placed = (rows, P(), P(), P(), P(), P())
    return jax.shard_map(local, mesh=grid, in_specs=placed, out_specs=rows, check_vma=False)
```

```python
import jax
import jax.numpy as jnp
from jax import lax
from jax.experimental import pallas as pl
from jax.experimental.pallas import tpu as pltpu
from jax.sharding import Mesh
from jax.sharding import PartitionSpec as P

H = 8
DH = 128
KW = 4
BLOCK = 512
PAD = 8


def split_bf16(x):
    hi = lax.reduce_precision(x, exponent_bits=8, mantissa_bits=7)
    return hi.astype(jnp.bfloat16), (x - hi).astype(jnp.bfloat16)


def earlier_states(state):
    count = lax.axis_size("sz")
    rows_count = lax.axis_size("sy")
    quarters = state.astype(jnp.bfloat16).reshape((count, -1) + state.shape[1:])
    mine = lax.all_to_all(quarters, "sz", 0, 0).astype(jnp.float32)
    before = [jnp.zeros_like(mine[0])]
    for z in range(1, count):
        before.append(before[-1] + mine[z - 1])
    row_total = before[-1] + mine[count - 1]
    row = lax.axis_index("sy")
    later_row = (row < lax.iota(jnp.int32, rows_count)).astype(jnp.float32)
    same_row = (row == lax.iota(jnp.int32, rows_count)).astype(jnp.float32)
    messages = (
        later_row[:, None, None, None, None] * row_total[None, None]
        + same_row[:, None, None, None, None] * jnp.stack(before)[None]
    )
    received = lax.all_to_all(
        messages.astype(jnp.bfloat16).reshape((rows_count * count,) + row_total.shape),
        ("sy", "sz"),
        0,
        0,
    )
    received = received.reshape((rows_count, count) + row_total.shape).astype(jnp.float32)
    return jnp.sum(received, 0).reshape(state.shape)


def conv_kernel(pq, pk, pv, eq, ek, ev, tq, tk, tv, oq, ok, ov, state_ref, buf):
    rows = pq.shape[1]
    for g in range(pq.shape[0]):
        for proj, early, taps, out in ((pq, eq, tq, oq), (pk, ek, tk, ok), (pv, ev, tv, ov)):
            buf[PAD - (KW - 1) : PAD, :] = early[g].astype(jnp.float32)
            buf[PAD:, :] = proj[g].astype(jnp.float32)
            summed = jnp.zeros((rows, DH), jnp.float32)
            for offset in range(KW):
                summed = summed + taps[g, offset : offset + 1, :] * buf[pl.ds(PAD - offset, rows), :]
            out[g] = (summed * jax.nn.sigmoid(summed)).astype(out.dtype)
        state_ref[g] = lax.dot_general(
            ok[g], ov[g], (((0,), (0,)), ((), ())), preferred_element_type=jnp.float32
        ).astype(state_ref.dtype)


def group_slab(group, shift, rows, cols):
    return pl.BlockSpec((group, rows, cols), lambda h: (h + shift // group, 0, 0))


def local_kernel(q_ref, k_ref, v_ref, out_ref):
    rows = q_ref.shape[0]
    block = min(BLOCK, rows)
    causal = lax.broadcasted_iota(jnp.int32, (block, block), 0) >= lax.broadcasted_iota(
        jnp.int32, (block, block), 1
    )
    inner = jnp.zeros((DH, DH), jnp.float32)
    for b in range(rows // block):
        span = pl.ds(b * block, block)
        query, key, value = q_ref[span, :], k_ref[span, :], v_ref[span, :]
        scores = lax.dot_general(
            query, key, (((1,), (1,)), ((), ())), preferred_element_type=jnp.float32
        )
        scores = jnp.where(causal, scores, 0.0).astype(jnp.bfloat16)
        part = jnp.dot(scores, value, preferred_element_type=jnp.float32)
        if b > 0:
            hi, lo = split_bf16(inner)
            part = part + jnp.dot(query, hi, preferred_element_type=jnp.float32)
            part = part + jnp.dot(query, lo, preferred_element_type=jnp.float32)
        out_ref[span, :] = part
        inner = inner + lax.dot_general(
            key, value, (((0,), (0,)), ((), ())), preferred_element_type=jnp.float32
        )


def out_kernel(q_ref, local_ref, prefix_ref, gain_ref, w_ref, out_ref, headed):
    for head in range(q_ref.shape[0]):
        hi, lo = split_bf16(prefix_ref[head])
        query = q_ref[head]
        attended = local_ref[head] + jnp.dot(query, hi, preferred_element_type=jnp.float32)
        attended = attended + jnp.dot(query, lo, preferred_element_type=jnp.float32)
        scaled = attended * lax.rsqrt(jnp.mean(attended * attended, -1, keepdims=True) + 1e-05)
        headed[:, head * DH : (head + 1) * DH] = (scaled * gain_ref[head]).astype(headed.dtype)
    out_ref[...] = jnp.dot(
        headed[...], w_ref[...], preferred_element_type=jnp.float32
    ).astype(out_ref.dtype)


def slab(shift, rows, cols):
    return pl.BlockSpec((None, rows, cols), lambda h: (h + shift, 0, 0))


def local(tokens, norm_gain, w_qkv, conv_weight, head_gain, w_out):
    rows, width = tokens.shape
    tokens_f = tokens.astype(jnp.float32)
    scale = lax.rsqrt(jnp.mean(tokens_f * tokens_f, -1, keepdims=True) + 1e-06)
    normed = (tokens_f * scale * norm_gain).astype(jnp.bfloat16)

    slabs = w_qkv.shape[1] // DH
    projected = jnp.einsum(
        "td,dje->jte", normed, w_qkv.reshape(width, slabs, DH), preferred_element_type=jnp.float32
    ).astype(jnp.bfloat16)

    seq_axes = ("sy", "sz")
    count = lax.axis_size("sy") * lax.axis_size("sz")
    earlier_rows = lax.ppermute(
        projected[:, rows - (KW - 1) :, :], seq_axes, [(i, i + 1) for i in range(count - 1)]
    )
    taps = conv_weight.reshape(KW, slabs, DH).transpose(1, 0, 2)

    mixed_shape = jax.ShapeDtypeStruct((H, rows, DH), jnp.bfloat16)
    query, key, value, state = pl.pallas_call(
        conv_kernel,
        grid=(H // 4,),
        in_specs=[group_slab(4, shift, rows, DH) for shift in (0, H, 2 * H)]
        + [group_slab(4, shift, KW - 1, DH) for shift in (0, H, 2 * H)]
        + [group_slab(4, shift, KW, DH) for shift in (0, H, 2 * H)],
        out_specs=[group_slab(4, 0, rows, DH)] * 3 + [group_slab(4, 0, DH, DH)],
        out_shape=[mixed_shape] * 3 + [jax.ShapeDtypeStruct((H, DH, DH), jnp.bfloat16)],
        scratch_shapes=[pltpu.VMEM((rows + PAD, DH), jnp.float32)],
        cost_estimate=pl.CostEstimate(
            flops=H * (3 * rows * DH * 12 + 2 * rows * DH * DH),
            transcendentals=H * 3 * rows * DH,
            bytes_accessed=H * 3 * rows * DH * 4,
        ),
    )(projected, projected, projected, earlier_rows, earlier_rows, earlier_rows, taps, taps, taps)

    block = min(BLOCK, rows)
    local_part = pl.pallas_call(
        local_kernel,
        grid=(H,),
        in_specs=[slab(0, rows, DH)] * 3,
        out_specs=slab(0, rows, DH),
        out_shape=jax.ShapeDtypeStruct((H, rows, DH), jnp.float32),
        cost_estimate=pl.CostEstimate(
            flops=H * (4 * rows * block * DH + 6 * rows * DH * DH),
            transcendentals=0,
            bytes_accessed=H * rows * DH * 10,
        ),
    )(query, key, value)

    prefix = earlier_states(state)

    tile = min(512, rows)
    out = pl.pallas_call(
        out_kernel,
        grid=(rows // tile,),
        in_specs=[
            pl.BlockSpec((H, tile, DH), lambda i: (0, i, 0)),
            pl.BlockSpec((H, tile, DH), lambda i: (0, i, 0)),
            pl.BlockSpec((H, DH, DH), lambda i: (0, 0, 0)),
            pl.BlockSpec((H, 1, DH), lambda i: (0, 0, 0)),
            pl.BlockSpec((width, width), lambda i: (0, 0)),
        ],
        out_specs=pl.BlockSpec((tile, width), lambda i: (i, 0)),
        out_shape=jax.ShapeDtypeStruct((rows, width), jnp.bfloat16),
        scratch_shapes=[pltpu.VMEM((tile, H * DH), jnp.bfloat16)],
        cost_estimate=pl.CostEstimate(
            flops=H * 4 * rows * DH * DH + 2 * rows * width * width,
            transcendentals=H * rows,
            bytes_accessed=H * rows * DH * 6 + width * width * 2 + rows * width * 2,
        ),
    )(query, local_part, prefix, head_gain.reshape(H, 1, DH), w_out)
    return out


def solution(mesh):
    seq = mesh.shape["seq"]
    inner = 4 if seq % 4 == 0 else 1
    grid = Mesh(
        mesh.devices.reshape(mesh.shape["trace"], seq // inner, inner), ("trace", "sy", "sz")
    )
    rows = P(("trace", "sy", "sz"), None)
    placed = (rows, P(), P(), P(), P(), P())
    return jax.shard_map(local, mesh=grid, in_specs=placed, out_specs=rows, check_vma=False)
```

```python
import jax
import jax.numpy as jnp
from jax import lax
from jax.experimental import pallas as pl
from jax.experimental.pallas import tpu as pltpu
from jax.sharding import Mesh
from jax.sharding import PartitionSpec as P

H = 8
DH = 128
KW = 4
BLOCK = 512
PAD = 8


def split_bf16(x):
    hi = lax.reduce_precision(x, exponent_bits=8, mantissa_bits=7)
    return hi.astype(jnp.bfloat16), (x - hi).astype(jnp.bfloat16)


def earlier_states(state):
    count = lax.axis_size("sz")
    rows_count = lax.axis_size("sy")
    quarters = state.astype(jnp.bfloat16).reshape((count, -1) + state.shape[1:])
    mine = lax.all_to_all(quarters, "sz", 0, 0).astype(jnp.float32)
    before = [jnp.zeros_like(mine[0])]
    for z in range(1, count):
        before.append(before[-1] + mine[z - 1])
    row_total = before[-1] + mine[count - 1]
    row = lax.axis_index("sy")
    later_row = (row < lax.iota(jnp.int32, rows_count)).astype(jnp.float32)
    same_row = (row == lax.iota(jnp.int32, rows_count)).astype(jnp.float32)
    messages = (
        later_row[:, None, None, None, None] * row_total[None, None]
        + same_row[:, None, None, None, None] * jnp.stack(before)[None]
    )
    received = lax.all_to_all(
        messages.astype(jnp.bfloat16).reshape((rows_count * count,) + row_total.shape),
        ("sy", "sz"),
        0,
        0,
    )
    received = received.reshape((rows_count, count) + row_total.shape).astype(jnp.float32)
    return jnp.sum(received, 0).reshape(state.shape)


def conv_kernel(pq, pk, pv, eq, ek, ev, tq, tk, tv, oq, ok, ov, state_ref, buf):
    rows = pq.shape[1]
    for g in range(pq.shape[0]):
        for proj, early, taps, out in ((pq, eq, tq, oq), (pk, ek, tk, ok), (pv, ev, tv, ov)):
            buf[PAD - (KW - 1) : PAD, :] = early[g].astype(jnp.float32)
            buf[PAD:, :] = proj[g].astype(jnp.float32)
            summed = jnp.zeros((rows, DH), jnp.float32)
            for offset in range(KW):
                summed = summed + taps[g, offset : offset + 1, :] * buf[pl.ds(PAD - offset, rows), :]
            out[g] = (summed * jax.nn.sigmoid(summed)).astype(out.dtype)
        state_ref[g] = lax.dot_general(
            ok[g], ov[g], (((0,), (0,)), ((), ())), preferred_element_type=jnp.float32
        ).astype(state_ref.dtype)


def group_slab(group, shift, rows, cols):
    return pl.BlockSpec((group, rows, cols), lambda h: (h + shift // group, 0, 0))


def local_kernel(q_ref, k_ref, v_ref, out_ref):
    rows = q_ref.shape[0]
    block = min(BLOCK, rows)
    causal = lax.broadcasted_iota(jnp.int32, (block, block), 0) >= lax.broadcasted_iota(
        jnp.int32, (block, block), 1
    )
    inner = jnp.zeros((DH, DH), jnp.float32)
    for b in range(rows // block):
        span = pl.ds(b * block, block)
        query, key, value = q_ref[span, :], k_ref[span, :], v_ref[span, :]
        scores = lax.dot_general(
            query, key, (((1,), (1,)), ((), ())), preferred_element_type=jnp.float32
        )
        scores = jnp.where(causal, scores, 0.0).astype(jnp.bfloat16)
        part = jnp.dot(scores, value, preferred_element_type=jnp.float32)
        if b > 0:
            hi, lo = split_bf16(inner)
            part = part + jnp.dot(query, hi, preferred_element_type=jnp.float32)
            part = part + jnp.dot(query, lo, preferred_element_type=jnp.float32)
        out_ref[span, :] = part
        inner = inner + lax.dot_general(
            key, value, (((0,), (0,)), ((), ())), preferred_element_type=jnp.float32
        )


def out_kernel(q_ref, local_ref, prefix_ref, gain_ref, w_ref, out_ref, headed):
    for head in range(q_ref.shape[0]):
        hi, lo = split_bf16(prefix_ref[head])
        query = q_ref[head]
        attended = local_ref[head] + jnp.dot(query, hi, preferred_element_type=jnp.float32)
        attended = attended + jnp.dot(query, lo, preferred_element_type=jnp.float32)
        scaled = attended * lax.rsqrt(jnp.mean(attended * attended, -1, keepdims=True) + 1e-05)
        headed[:, head * DH : (head + 1) * DH] = (scaled * gain_ref[head]).astype(headed.dtype)
    out_ref[...] = jnp.dot(
        headed[...], w_ref[...], preferred_element_type=jnp.float32
    ).astype(out_ref.dtype)


def slab(shift, rows, cols):
    return pl.BlockSpec((None, rows, cols), lambda h: (h + shift, 0, 0))


def local(tokens, norm_gain, w_qkv, conv_weight, head_gain, w_out):
    rows, width = tokens.shape
    tokens_f = tokens.astype(jnp.float32)
    scale = lax.rsqrt(jnp.mean(tokens_f * tokens_f, -1, keepdims=True) + 1e-06)
    normed = (tokens_f * scale * norm_gain).astype(jnp.bfloat16)

    slabs = w_qkv.shape[1] // DH
    projected = jnp.einsum(
        "td,dje->jte", normed, w_qkv.reshape(width, slabs, DH), preferred_element_type=jnp.float32
    ).astype(jnp.bfloat16)

    seq_axes = ("sy", "sz")
    count = lax.axis_size("sy") * lax.axis_size("sz")
    earlier_rows = lax.ppermute(
        projected[:, rows - (KW - 1) :, :], seq_axes, [(i, i + 1) for i in range(count - 1)]
    )
    taps = conv_weight.reshape(KW, slabs, DH).transpose(1, 0, 2)

    mixed_shape = jax.ShapeDtypeStruct((H, rows, DH), jnp.bfloat16)
    query, key, value, state = pl.pallas_call(
        conv_kernel,
        grid=(H // 2,),
        in_specs=[group_slab(2, shift, rows, DH) for shift in (0, H, 2 * H)]
        + [group_slab(2, shift, KW - 1, DH) for shift in (0, H, 2 * H)]
        + [group_slab(2, shift, KW, DH) for shift in (0, H, 2 * H)],
        out_specs=[group_slab(2, 0, rows, DH)] * 3 + [group_slab(2, 0, DH, DH)],
        out_shape=[mixed_shape] * 3 + [jax.ShapeDtypeStruct((H, DH, DH), jnp.bfloat16)],
        scratch_shapes=[pltpu.VMEM((rows + PAD, DH), jnp.float32)],
        cost_estimate=pl.CostEstimate(
            flops=H * (3 * rows * DH * 12 + 2 * rows * DH * DH),
            transcendentals=H * 3 * rows * DH,
            bytes_accessed=H * 3 * rows * DH * 4,
        ),
    )(projected, projected, projected, earlier_rows, earlier_rows, earlier_rows, taps, taps, taps)

    block = min(BLOCK, rows)
    local_part = pl.pallas_call(
        local_kernel,
        grid=(H,),
        in_specs=[slab(0, rows, DH)] * 3,
        out_specs=slab(0, rows, DH),
        out_shape=jax.ShapeDtypeStruct((H, rows, DH), jnp.float32),
        cost_estimate=pl.CostEstimate(
            flops=H * (4 * rows * block * DH + 6 * rows * DH * DH),
            transcendentals=0,
            bytes_accessed=H * rows * DH * 10,
        ),
    )(query, key, value)

    prefix = earlier_states(state)

    tile = min(1024, rows)
    out = pl.pallas_call(
        out_kernel,
        grid=(rows // tile,),
        in_specs=[
            pl.BlockSpec((H, tile, DH), lambda i: (0, i, 0)),
            pl.BlockSpec((H, tile, DH), lambda i: (0, i, 0)),
            pl.BlockSpec((H, DH, DH), lambda i: (0, 0, 0)),
            pl.BlockSpec((H, 1, DH), lambda i: (0, 0, 0)),
            pl.BlockSpec((width, width), lambda i: (0, 0)),
        ],
        out_specs=pl.BlockSpec((tile, width), lambda i: (i, 0)),
        out_shape=jax.ShapeDtypeStruct((rows, width), jnp.bfloat16),
        scratch_shapes=[pltpu.VMEM((tile, H * DH), jnp.bfloat16)],
        cost_estimate=pl.CostEstimate(
            flops=H * 4 * rows * DH * DH + 2 * rows * width * width,
            transcendentals=H * rows,
            bytes_accessed=H * rows * DH * 6 + width * width * 2 + rows * width * 2,
        ),
    )(query, local_part, prefix, head_gain.reshape(H, 1, DH), w_out)
    return out


def solution(mesh):
    seq = mesh.shape["seq"]
    inner = 4 if seq % 4 == 0 else 1
    grid = Mesh(
        mesh.devices.reshape(mesh.shape["trace"], seq // inner, inner), ("trace", "sy", "sz")
    )
    rows = P(("trace", "sy", "sz"), None)
    placed = (rows, P(), P(), P(), P(), P())
    return jax.shard_map(local, mesh=grid, in_specs=placed, out_specs=rows, check_vma=False)
```
